32 devices in a mesh: req: 4 (over y, x), seq: 8 (over z, core).
Axes of the slice: x: 2, y: 2, z: 4, core: 2. Of those that a mesh axis runs over, the one named last changes fastest.
Arguments:
- patches: bfloat16 [32, 4, 1280], P('req'), may hold values from -6 to 6
- key_cache: bfloat16 [32, 1024, 1280], P('req', 'seq'), may hold values from -119 to 119
- value_cache: bfloat16 [32, 1024, 1280], P('req', 'seq'), may hold values from -6 to 6
- cache_len: int32 [32], P('req'), may hold values from 16 to 1024, as said below
- attn_gain: float32 [1280], replicated, may hold values from 0.1 to 1.9
- w_qkv: bfloat16 [1280, 3840], replicated, may hold values from -0.15625 to 0.15625
- w_out: bfloat16 [1280, 1280], replicated, may hold values from -0.15625 to 0.15625
- ffn_gain: float32 [1280], replicated, may hold values from 0.1 to 1.9
- w_up: bfloat16 [1280, 1280], replicated, may hold values from -0.15625 to 0.15625
- w_down: bfloat16 [1280, 1280], replicated, may hold values from -0.15625 to 0.15625
Outputs:
- decoded: bfloat16 [32, 4, 1280], P('req')
The draws below stay inside these ranges and needn't reach their ends.
Inputs may be any that keep to these rules, and one draw needn't show every extreme that they name: `cache_len`: half of the requests hold between 16 and 64 cached patches, the other half between 768 and 1024.
All inputs are finite; a program needn't handle non-finite values.
Results may differ from the reference program's by a relative error of at most 0.012.
The reference program's roundings to bfloat16 on the way (of `normed`, `projected`, `attended`, `out_rows`, `normed_mixed`, `up_rows`, `hidden` and `down_rows`) count: a program that leaves them out, or rounds other values in their place, can miss the bound.
Values may be sent and summed in bfloat16 or wider, within the bound.
No kernel may reach another device: no remote copies, remote signals or barrier semaphores. Data moves between devices by JAX's collectives and lax.ppermute only.
A program may use at most 128 MiB of HBM per device.

```python
import jax
import jax.numpy as jnp
from jax import lax

D = 1280
HEADS = 16
HD = 80
FF = 1280
NEW = 4
CAP = 128
REQS = 32
SLOTS = 1024


def draw_key_cache(key, part):
    first_key = jax.random.fold_in(key, 0)
    cache_shape = (REQS, SLOTS, D)
    values = jax.random.normal(first_key, cache_shape, jnp.float32)
    return jnp.clip(values, -119.0, 119.0).astype(jnp.bfloat16)


def draw_cache_len(key, part):
    order_key, short_key, long_key = jax.random.split(key, 3)
    ranking = jax.random.permutation(order_key, REQS)
    short_len = jax.random.randint(short_key, (REQS,), SLOTS // 64, SLOTS // 16 + 1)
    long_len = jax.random.randint(long_key, (REQS,), SLOTS - 2 * CAP, SLOTS + 1)
    lengths = jnp.where(ranking < REQS // 2, long_len, short_len)
    lengths = jnp.where(ranking == 0, SLOTS, lengths)
    lengths = jnp.where(ranking == REQS - 1, SLOTS // 64, lengths)
    return lengths.astype(jnp.int32)


def shard_levels(rng, shape, pieces, least, largest):
    level = 1.0
    for dim, blocks in pieces:
        steps = jax.random.uniform(jax.random.fold_in(jax.random.fold_in(rng, 6), dim), (blocks,), jnp.float32, least / len(pieces), largest / len(pieces))
        level = level * jnp.repeat(jnp.exp(steps), shape[dim] // blocks).reshape((-1,) + (1,) * (len(shape) - 1 - dim))
    return level


def gaussian(stream_key, extent, width, bound, shards=(), kind=jnp.bfloat16):
    result = jax.random.normal(stream_key, extent, jnp.float32) * width
    if len(shards) > 0:
        result = shard_levels(stream_key, extent, shards, -0.22, 0.18) * result
    return jnp.clip(result, min=-bound, max=bound).astype(kind)


def setup_inputs(seed: int = 0) -> dict:
    key_list = jax.random.split(jax.random.key(seed), 11)
    patches = gaussian(key_list[0], (REQS, NEW, D), 1.0, 6.0, ((0, 4),))
    key_cache = draw_key_cache(jax.random.fold_in(key_list[10], 71), 0)
    value_cache = gaussian(key_list[2], (REQS, SLOTS, D), 1.0, 6.0, ((0, 4), (1, 8)))
    cache_len = draw_cache_len(jax.random.fold_in(key_list[10], 71), 0)
    attn_gain = jnp.clip(1.0 + 0.18 * jax.random.normal(key_list[4], (D,), jnp.float32), 0.1, 1.9)
    w_qkv = gaussian(key_list[5], (D, 3 * D), D ** -0.5, 0.15625)
    w_out = gaussian(key_list[6], (D, D), D ** -0.5, 0.15625)
    ffn_gain = jnp.clip(1.0 + 0.18 * jax.random.normal(key_list[7], (D,), jnp.float32), 0.1, 1.9)
    w_up = gaussian(key_list[8], (D, FF), D ** -0.5, 0.15625)
    w_down = gaussian(key_list[9], (FF, D), FF ** -0.5, 0.15625)
    return dict(patches=patches, key_cache=key_cache, value_cache=value_cache, cache_len=cache_len, attn_gain=attn_gain, w_qkv=w_qkv, w_out=w_out, ffn_gain=ffn_gain, w_up=w_up, w_down=w_down)


epsilon = 1e-06

def rms_norm(values, gain):
    return values * lax.rsqrt(lax.optimization_barrier(jnp.mean(values * values, axis=-1, keepdims=True)) + epsilon) * gain

def attend_request(operands):
    queries, keys_new, values_new, cache_keys, cache_values, length = operands
    position = jnp.arange(SLOTS, dtype=jnp.int32)
    live_mask = position < length
    scale_factor = HD ** (-0.5)
    query_float = queries.astype(jnp.float32)
    cache_scores = jnp.einsum('thd,shd->ths', query_float, cache_keys.astype(jnp.float32)) * scale_factor
    new_scores = jnp.einsum('thd,uhd->thu', query_float, keys_new.astype(jnp.float32)) * scale_factor
    causal = jnp.arange(NEW)[:, None] >= jnp.arange(NEW)[None, :]
    cache_masked = jnp.where(live_mask[None, None, :], cache_scores, -jnp.inf)
    new_masked = jnp.where(causal[:, None, :], new_scores, -jnp.inf)
    global_peak = jnp.maximum(lax.optimization_barrier(jnp.max(cache_masked, axis=2)), lax.optimization_barrier(jnp.max(new_masked, axis=2)))
    cache_weights = jnp.exp(cache_masked - global_peak[..., None])
    new_weights = jnp.exp(new_masked - global_peak[..., None])
    denominator = lax.optimization_barrier(jnp.sum(cache_weights, axis=2)) + lax.optimization_barrier(jnp.sum(new_weights, axis=2))
    numerator = jnp.einsum('ths,shd->thd', cache_weights.astype(jnp.bfloat16).astype(jnp.float32), cache_values.astype(jnp.float32))
    numerator = numerator + jnp.einsum('thu,uhd->thd', new_weights.astype(jnp.bfloat16).astype(jnp.float32), values_new.astype(jnp.float32))
    return (numerator / denominator[..., None]).astype(jnp.bfloat16)

def reference(patches, key_cache, value_cache, cache_len, attn_gain, w_qkv, w_out, ffn_gain, w_up, w_down):
    inputs = patches.astype(jnp.float32).reshape(REQS * NEW, D)
    normed = rms_norm(inputs, attn_gain).astype(jnp.bfloat16)
    projected = jnp.dot(normed, w_qkv, preferred_element_type=jnp.float32).astype(jnp.bfloat16)
    projected = projected.reshape(REQS, NEW, 3, HEADS, HD)
    attended = lax.map(attend_request, (projected[:, :, 0], projected[:, :, 1], projected[:, :, 2], key_cache.reshape(REQS, SLOTS, HEADS, HD), value_cache.reshape(REQS, SLOTS, HEADS, HD), cache_len))
    attended = attended.reshape(REQS * NEW, D)
    out_rows = jnp.dot(attended, w_out, preferred_element_type=jnp.float32).astype(jnp.bfloat16)
    mixed_rows = inputs + out_rows.astype(jnp.float32)
    normed_mixed = rms_norm(mixed_rows, ffn_gain).astype(jnp.bfloat16)
    up_rows = jnp.dot(normed_mixed, w_up, preferred_element_type=jnp.float32).astype(jnp.bfloat16)
    hidden = jax.nn.silu(up_rows.astype(jnp.float32)).astype(jnp.bfloat16)
    down_rows = jnp.dot(hidden, w_down, preferred_element_type=jnp.float32).astype(jnp.bfloat16)
    return (mixed_rows + down_rows.astype(jnp.float32)).astype(jnp.bfloat16).reshape(REQS, NEW, D)
```

```python
import jax
import jax.numpy as jnp
from jax import lax
from jax.sharding import PartitionSpec as P

HEADS = 16
HD = 80


epsilon = 1e-06
negative_fill = -1e30


def rms_norm(values, gain):
    return values * lax.rsqrt(jnp.mean(values * values, axis=-1, keepdims=True) + epsilon) * gain


def project(token_rows, weight):
    return jnp.dot(token_rows, weight, preferred_element_type=jnp.float32).astype(jnp.bfloat16)


def head_mask(heads, width):
    return (jnp.arange(width)[None, :] // HD) == jnp.arange(heads)[:, None]


def per_head_queries(queries, mask):
    groups, count, width = queries.shape
    heads = mask.shape[0]
    blocks = jnp.where(mask[None, None], queries[:, :, None, :], jnp.zeros((), queries.dtype))
    return blocks.reshape(groups, count * heads, width)


def head_diagonal(rows, mask):
    groups, count_heads, width = rows.shape
    heads = mask.shape[0]
    rows = rows.reshape(groups, count_heads // heads, heads, width)
    return jnp.sum(jnp.where(mask[None, None], rows, 0.0), axis=2)


def spread(per_head, width):
    return jnp.repeat(per_head, width // per_head.shape[-1], axis=-1)


def merge(first, second, heads):
    cols = first.shape[-1] - 2 * heads
    v1, m1, l1 = first[..., :cols], first[..., cols:cols + heads], first[..., cols + heads:]
    v2, m2, l2 = second[..., :cols], second[..., cols:cols + heads], second[..., cols + heads:]
    m = jnp.maximum(m1, m2)
    a1 = jnp.exp(m1 - m)
    a2 = jnp.exp(m2 - m)
    l = l1 * a1 + l2 * a2
    v = v1 * spread(a1, cols) + v2 * spread(a2, cols)
    return jnp.concatenate([v, m, l], axis=-1)


def exchange(part, distance, count):
    pairs = [(i, i ^ distance) for i in range(count)]
    return lax.ppermute(part, "seq", pairs)


def combine_over_seq(values, peak, weight_sum, count):
    groups, count_new, width = values.shape
    heads = peak.shape[-1]
    half_cols, half_heads = width // 2, heads // 2
    me = lax.axis_index("seq")
    core = me % 2

    def half(which):
        v = lax.dynamic_slice_in_dim(values, which * half_cols, half_cols, axis=2)
        m = lax.dynamic_slice_in_dim(peak, which * half_heads, half_heads, axis=2)
        l = lax.dynamic_slice_in_dim(weight_sum, which * half_heads, half_heads, axis=2)
        return jnp.concatenate([v, m, l], axis=-1)

    kept = half(core)
    sent = half(1 - core)
    got = exchange(sent, 1, count)
    low_first = core == 0
    state = merge(jnp.where(low_first, kept, got), jnp.where(low_first, got, kept), half_heads)
    distance = 2
    while distance < count:
        got = exchange(state, distance, count)
        low_first = (me & distance) == 0
        state = merge(
            jnp.where(low_first, state, got), jnp.where(low_first, got, state), half_heads
        )
        distance *= 2
    other = exchange(state, 1, count)
    low_half = jnp.where(core == 0, state, other)
    high_half = jnp.where(core == 0, other, state)
    v = jnp.concatenate([low_half[..., :half_cols], high_half[..., :half_cols]], axis=-1)
    m = jnp.concatenate(
        [low_half[..., half_cols:half_cols + half_heads], high_half[..., half_cols:half_cols + half_heads]],
        axis=-1,
    )
    l = jnp.concatenate(
        [low_half[..., half_cols + half_heads:], high_half[..., half_cols + half_heads:]], axis=-1
    )
    return v, m, l


def shards(
    patches, key_cache, value_cache, cache_len, attn_gain, w_qkv, w_out, ffn_gain, w_up, w_down
):
    groups, count_new, model_width = patches.shape
    slots_here = key_cache.shape[1]
    seq_count = lax.axis_size("seq")
    inputs = patches.reshape(groups * count_new, model_width).astype(jnp.float32)
    normed = rms_norm(inputs, attn_gain).astype(jnp.bfloat16)
    projected = project(normed, w_qkv).reshape(groups, count_new, 3 * model_width)
    queries = projected[:, :, :model_width]
    keys_new = projected[:, :, model_width:2 * model_width]
    values_new = projected[:, :, 2 * model_width:]
    mask = head_mask(HEADS, model_width)
    query_rows = per_head_queries(queries, mask)
    scale_factor = HD ** (-0.5)
    position = lax.axis_index("seq") * slots_here + jnp.arange(slots_here, dtype=jnp.int32)
    live_mask = (position[None, :] < cache_len[:, None])[:, None, :]
    cache_scores = (
        jnp.einsum("rqc,rsc->rqs", query_rows, key_cache, preferred_element_type=jnp.float32)
        * scale_factor
    )
    masked = jnp.where(live_mask, cache_scores, negative_fill)
    peak_score = jnp.max(masked, axis=2)
    weights = jnp.where(live_mask, jnp.exp(masked - peak_score[..., None]), 0.0)
    weight_sum = jnp.sum(weights, axis=2)
    value_rows = jnp.einsum(
        "rqs,rsc->rqc", weights.astype(jnp.bfloat16), value_cache, preferred_element_type=jnp.float32
    )
    value_sum = head_diagonal(value_rows, mask)
    value_sum, peak_score, weight_sum = combine_over_seq(
        value_sum,
        peak_score.reshape(groups, count_new, HEADS),
        weight_sum.reshape(groups, count_new, HEADS),
        seq_count,
    )
    new_scores = (
        jnp.einsum("rqc,ruc->rqu", query_rows, keys_new, preferred_element_type=jnp.float32)
        * scale_factor
    ).reshape(groups, count_new, HEADS, count_new)
    causal = (jnp.arange(count_new)[:, None] >= jnp.arange(count_new)[None, :])[None, :, None, :]
    new_masked = jnp.where(causal, new_scores, negative_fill)
    global_peak = jnp.maximum(peak_score, jnp.max(new_masked, axis=3))
    carry_scale = jnp.exp(peak_score - global_peak)
    new_weights = jnp.where(causal, jnp.exp(new_masked - global_peak[..., None]), 0.0)
    denominator = weight_sum * carry_scale + jnp.sum(new_weights, axis=3)
    new_rows = jnp.einsum(
        "rqu,ruc->rqc",
        new_weights.reshape(groups, count_new * HEADS, count_new).astype(jnp.bfloat16),
        values_new,
        preferred_element_type=jnp.float32,
    )
    new_values = head_diagonal(new_rows, mask)
    numerator = value_sum * spread(carry_scale, model_width) + new_values
    attended = (numerator / spread(denominator, model_width)).astype(jnp.bfloat16)
    out_rows = project(attended.reshape(groups * count_new, model_width), w_out)
    mixed_rows = inputs + out_rows.astype(jnp.float32)
    normed_mixed = rms_norm(mixed_rows, ffn_gain).astype(jnp.bfloat16)
    up_rows = project(normed_mixed, w_up)
    hidden = jax.nn.silu(up_rows.astype(jnp.float32)).astype(jnp.bfloat16)
    down_rows = project(hidden, w_down)
    decoded = (mixed_rows + down_rows.astype(jnp.float32)).astype(jnp.bfloat16)
    return decoded.reshape(groups, count_new, model_width)


def solution(mesh):
    placed = (
        P("req", None, None),
        P("req", "seq", None),
        P("req", "seq", None),
        P("req"),
        P(),
        P(),
        P(),
        P(),
        P(),
        P(),
    )
    return jax.shard_map(
        shards, mesh=mesh, in_specs=placed, out_specs=P("req", None, None), check_vma=False
    )
```

```python
import jax
import jax.numpy as jnp
from jax import lax
from jax.sharding import PartitionSpec as P

HEADS = 16
HD = 80


epsilon = 1e-06
negative_fill = -1e30


def rms_norm(values, gain):
    return values * lax.rsqrt(jnp.mean(values * values, axis=-1, keepdims=True) + epsilon) * gain


def project(token_rows, weight):
    return jnp.dot(token_rows, weight, preferred_element_type=jnp.float32).astype(jnp.bfloat16)


def head_mask(heads, width):
    return (jnp.arange(width)[None, :] // HD) == jnp.arange(heads)[:, None]


def per_head_queries(queries, mask):
    groups, count, width = queries.shape
    heads = mask.shape[0]
    blocks = jnp.where(mask[None, None], queries[:, :, None, :], jnp.zeros((), queries.dtype))
    return blocks.reshape(groups, count * heads, width)


def head_diagonal(rows, mask):
    groups, count_heads, width = rows.shape
    heads = mask.shape[0]
    rows = rows.reshape(groups, count_heads // heads, heads, width)
    return jnp.sum(jnp.where(mask[None, None], rows, 0.0), axis=2)


LANES = 128


def pack(values, peak, weight_sum):
    pad = jnp.zeros(values.shape[:-1] + (LANES - HD - 2,), jnp.float32)
    return jnp.concatenate([values, peak[..., None], weight_sum[..., None], pad], axis=-1)


def merge(first, second):
    m1 = first[..., HD:HD + 1]
    m2 = second[..., HD:HD + 1]
    m = jnp.maximum(m1, m2)
    a1 = jnp.exp(m1 - m)
    a2 = jnp.exp(m2 - m)
    merged = first * a1 + second * a2
    lane = lax.broadcasted_iota(jnp.int32, merged.shape, merged.ndim - 1)
    return jnp.where(lane == HD, m, merged)


def exchange(part, distance, count):
    pairs = [(i, i ^ distance) for i in range(count)]
    return lax.ppermute(part, "seq", pairs)


def combine_over_seq(packed, count):
    heads = packed.shape[1]
    half_heads = heads // 2
    me = lax.axis_index("seq")
    core = me % 2
    kept = lax.dynamic_slice_in_dim(packed, core * half_heads, half_heads, axis=1)
    sent = lax.dynamic_slice_in_dim(packed, (1 - core) * half_heads, half_heads, axis=1)
    got = exchange(sent, 1, count)
    low_first = core == 0
    state = merge(jnp.where(low_first, kept, got), jnp.where(low_first, got, kept))
    distance = 2
    while distance < count:
        got = exchange(state, distance, count)
        low_first = (me // distance) % 2 == 0
        state = merge(jnp.where(low_first, state, got), jnp.where(low_first, got, state))
        distance *= 2
    other = exchange(state, 1, count)
    low_half = jnp.where(core == 0, state, other)
    high_half = jnp.where(core == 0, other, state)
    return jnp.concatenate([low_half, high_half], axis=1)


def shards(
    patches, key_cache, value_cache, cache_len, attn_gain, w_qkv, w_out, ffn_gain, w_up, w_down
):
    groups, count_new, model_width = patches.shape
    slots_here = key_cache.shape[1]
    seq_count = lax.axis_size("seq")
    inputs = patches.reshape(groups * count_new, model_width).astype(jnp.float32)
    normed = rms_norm(inputs, attn_gain).astype(jnp.bfloat16)
    projected = project(normed, w_qkv).reshape(groups, count_new, 3 * model_width)
    queries = projected[:, :, :model_width]
    keys_new = projected[:, :, model_width:2 * model_width]
    values_new = projected[:, :, 2 * model_width:]
    mask = head_mask(HEADS, model_width)
    query_rows = per_head_queries(queries, mask)
    scale_factor = HD ** (-0.5)
    position = lax.axis_index("seq") * slots_here + jnp.arange(slots_here, dtype=jnp.int32)
    live_mask = (position[None, :] < cache_len[:, None])[:, None, :]
    cache_scores = (
        jnp.einsum("rqc,rsc->rqs", query_rows, key_cache, preferred_element_type=jnp.float32)
        * scale_factor
    )
    masked = jnp.where(live_mask, cache_scores, negative_fill)
    peak_score = jnp.max(masked, axis=2)
    weights = jnp.where(live_mask, jnp.exp(masked - peak_score[..., None]), 0.0)
    weight_sum = jnp.sum(weights, axis=2)
    value_rows = jnp.einsum(
        "rqs,rsc->rqc", weights.astype(jnp.bfloat16), value_cache, preferred_element_type=jnp.float32
    )
    value_sum = head_diagonal(value_rows, mask)
    rows = groups * count_new
    packed = pack(
        value_sum.reshape(rows, HEADS, HD),
        peak_score.reshape(rows, HEADS),
        weight_sum.reshape(rows, HEADS),
    )
    total = combine_over_seq(packed, seq_count).reshape(groups, count_new, HEADS, LANES)
    value_total = total[..., :HD]
    peak_total = total[..., HD]
    weight_total = total[..., HD + 1]
    query_heads = queries.reshape(groups, count_new, HEADS, HD)
    key_heads = keys_new.reshape(groups, count_new, HEADS, HD)
    value_heads = values_new.reshape(groups, count_new, HEADS, HD)
    new_scores = (
        jnp.einsum("rthd,ruhd->rthu", query_heads, key_heads, preferred_element_type=jnp.float32)
        * scale_factor
    )
    causal = (jnp.arange(count_new)[:, None] >= jnp.arange(count_new)[None, :])[None, :, None, :]
    new_masked = jnp.where(causal, new_scores, negative_fill)
    global_peak = jnp.maximum(peak_total, jnp.max(new_masked, axis=3))
    carry_scale = jnp.exp(peak_total - global_peak)
    new_weights = jnp.where(causal, jnp.exp(new_masked - global_peak[..., None]), 0.0)
    denominator = weight_total * carry_scale + jnp.sum(new_weights, axis=3)
    new_values = jnp.einsum(
        "rthu,ruhd->rthd",
        new_weights.astype(jnp.bfloat16),
        value_heads,
        preferred_element_type=jnp.float32,
    )
    numerator = value_total * carry_scale[..., None] + new_values
    attended = (numerator / denominator[..., None]).astype(jnp.bfloat16)
    out_rows = project(attended.reshape(groups * count_new, model_width), w_out)
    mixed_rows = inputs + out_rows.astype(jnp.float32)
    normed_mixed = rms_norm(mixed_rows, ffn_gain).astype(jnp.bfloat16)
    up_rows = project(normed_mixed, w_up)
    hidden = jax.nn.silu(up_rows.astype(jnp.float32)).astype(jnp.bfloat16)
    down_rows = project(hidden, w_down)
    decoded = (mixed_rows + down_rows.astype(jnp.float32)).astype(jnp.bfloat16)
    return decoded.reshape(groups, count_new, model_width)


def solution(mesh):
    placed = (
        P("req", None, None),
        P("req", "seq", None),
        P("req", "seq", None),
        P("req"),
        P(),
        P(),
        P(),
        P(),
        P(),
        P(),
    )
    return jax.shard_map(
        shards, mesh=mesh, in_specs=placed, out_specs=P("req", None, None), check_vma=False
    )
```

```python
import jax
import jax.numpy as jnp
from jax import lax
from jax.sharding import PartitionSpec as P

HEADS = 16
HD = 80


epsilon = 1e-06
negative_fill = -1e30


def rms_norm(values, gain):
    return values * lax.rsqrt(jnp.mean(values * values, axis=-1, keepdims=True) + epsilon) * gain


def project(token_rows, weight):
    return jnp.dot(token_rows, weight, preferred_element_type=jnp.float32).astype(jnp.bfloat16)


def head_mask(heads, width):
    return (jnp.arange(width)[None, :] // HD) == jnp.arange(heads)[:, None]


def per_head_queries(queries, mask):
    groups, count, width = queries.shape
    heads = mask.shape[0]
    blocks = jnp.where(mask[None, None], queries[:, :, None, :], jnp.zeros((), queries.dtype))
    return blocks.reshape(groups, count * heads, width)


def head_diagonal(rows, mask):
    groups, count_heads, width = rows.shape
    heads = mask.shape[0]
    rows = rows.reshape(groups, count_heads // heads, heads, width)
    return jnp.sum(jnp.where(mask[None, None], rows, 0.0), axis=2)


LANES = 128


def pack(values, peak, weight_sum):
    pad = jnp.zeros(values.shape[:-1] + (LANES - HD - 2,), jnp.float32)
    return jnp.concatenate([values, peak[..., None], weight_sum[..., None], pad], axis=-1)


def merge(first, second):
    m1 = first[..., HD:HD + 1]
    m2 = second[..., HD:HD + 1]
    m = jnp.maximum(m1, m2)
    a1 = jnp.exp(m1 - m)
    a2 = jnp.exp(m2 - m)
    merged = first * a1 + second * a2
    lane = lax.broadcasted_iota(jnp.int32, merged.shape, merged.ndim - 1)
    return jnp.where(lane == HD, m, merged)


def exchange(part, distance, count):
    pairs = [(i, i ^ distance) for i in range(count)]
    return lax.ppermute(part, "seq", pairs)


def combine_over_seq(packed, count):
    heads, rows, lanes = packed.shape
    half_heads = heads // 2
    me = lax.axis_index("seq")
    core = me % 2
    halves = packed.reshape(2, half_heads * rows, lanes)
    kept = lax.dynamic_index_in_dim(halves, core, axis=0, keepdims=False)
    sent = lax.dynamic_index_in_dim(halves, 1 - core, axis=0, keepdims=False)
    got = exchange(sent, 1, count)
    low_first = core == 0
    state = merge(jnp.where(low_first, kept, got), jnp.where(low_first, got, kept))
    distance = 2
    while distance < count:
        got = exchange(state, distance, count)
        low_first = (me // distance) % 2 == 0
        state = merge(jnp.where(low_first, state, got), jnp.where(low_first, got, state))
        distance *= 2
    other = exchange(state, 1, count)
    low_half = jnp.where(core == 0, state, other)
    high_half = jnp.where(core == 0, other, state)
    return jnp.concatenate([low_half, high_half], axis=0).reshape(heads, rows, lanes)


def shards(
    patches, key_cache, value_cache, cache_len, attn_gain, w_qkv, w_out, ffn_gain, w_up, w_down
):
    groups, count_new, model_width = patches.shape
    slots_here = key_cache.shape[1]
    seq_count = lax.axis_size("seq")
    inputs = patches.reshape(groups * count_new, model_width).astype(jnp.float32)
    normed = rms_norm(inputs, attn_gain).astype(jnp.bfloat16)
    projected = project(normed, w_qkv).reshape(groups, count_new, 3 * model_width)
    queries = projected[:, :, :model_width]
    keys_new = projected[:, :, model_width:2 * model_width]
    values_new = projected[:, :, 2 * model_width:]
    mask = head_mask(HEADS, model_width)
    query_rows = per_head_queries(queries, mask)
    scale_factor = HD ** (-0.5)
    position = lax.axis_index("seq") * slots_here + jnp.arange(slots_here, dtype=jnp.int32)
    live_mask = (position[None, :] < cache_len[:, None])[:, None, :]
    cache_scores = (
        jnp.einsum("rqc,rsc->rqs", query_rows, key_cache, preferred_element_type=jnp.float32)
        * scale_factor
    )
    masked = jnp.where(live_mask, cache_scores, negative_fill)
    peak_score = jnp.max(masked, axis=2)
    weights = jnp.where(live_mask, jnp.exp(masked - peak_score[..., None]), 0.0)
    weight_sum = jnp.sum(weights, axis=2)
    value_rows = jnp.einsum(
        "rqs,rsc->rqc", weights.astype(jnp.bfloat16), value_cache, preferred_element_type=jnp.float32
    )
    value_sum = head_diagonal(value_rows, mask)
    rows = groups * count_new
    packed = pack(
        value_sum.reshape(rows, HEADS, HD).transpose(1, 0, 2),
        peak_score.reshape(rows, HEADS).T,
        weight_sum.reshape(rows, HEADS).T,
    )
    total = combine_over_seq(packed, seq_count).transpose(1, 0, 2)
    total = total.reshape(groups, count_new, HEADS, LANES)
    value_total = total[..., :HD]
    peak_total = total[..., HD]
    weight_total = total[..., HD + 1]
    query_heads = queries.reshape(groups, count_new, HEADS, HD)
    key_heads = keys_new.reshape(groups, count_new, HEADS, HD)
    value_heads = values_new.reshape(groups, count_new, HEADS, HD)
    new_scores = (
        jnp.einsum("rthd,ruhd->rthu", query_heads, key_heads, preferred_element_type=jnp.float32)
        * scale_factor
    )
    causal = (jnp.arange(count_new)[:, None] >= jnp.arange(count_new)[None, :])[None, :, None, :]
    new_masked = jnp.where(causal, new_scores, negative_fill)
    global_peak = jnp.maximum(peak_total, jnp.max(new_masked, axis=3))
    carry_scale = jnp.exp(peak_total - global_peak)
    new_weights = jnp.where(causal, jnp.exp(new_masked - global_peak[..., None]), 0.0)
    denominator = weight_total * carry_scale + jnp.sum(new_weights, axis=3)
    new_values = jnp.einsum(
        "rthu,ruhd->rthd",
        new_weights.astype(jnp.bfloat16),
        value_heads,
        preferred_element_type=jnp.float32,
    )
    numerator = value_total * carry_scale[..., None] + new_values
    attended = (numerator / denominator[..., None]).astype(jnp.bfloat16)
    out_rows = project(attended.reshape(groups * count_new, model_width), w_out)
    mixed_rows = inputs + out_rows.astype(jnp.float32)
    normed_mixed = rms_norm(mixed_rows, ffn_gain).astype(jnp.bfloat16)
    up_rows = project(normed_mixed, w_up)
    hidden = jax.nn.silu(up_rows.astype(jnp.float32)).astype(jnp.bfloat16)
    down_rows = project(hidden, w_down)
    decoded = (mixed_rows + down_rows.astype(jnp.float32)).astype(jnp.bfloat16)
    return decoded.reshape(groups, count_new, model_width)


def solution(mesh):
    placed = (
        P("req", None, None),
        P("req", "seq", None),
        P("req", "seq", None),
        P("req"),
        P(),
        P(),
        P(),
        P(),
        P(),
        P(),
    )
    return jax.shard_map(
        shards, mesh=mesh, in_specs=placed, out_specs=P("req", None, None), check_vma=False
    )
```

```python
import jax
import jax.numpy as jnp
from jax import lax
from jax.sharding import PartitionSpec as P

HEADS = 16
HD = 80


epsilon = 1e-06
negative_fill = -1e30


def rms_norm(values, gain):
    return values * lax.rsqrt(jnp.mean(values * values, axis=-1, keepdims=True) + epsilon) * gain


def project(token_rows, weight):
    return jnp.dot(token_rows, weight, preferred_element_type=jnp.float32).astype(jnp.bfloat16)


def head_mask(heads, width):
    return (jnp.arange(width)[None, :] // HD) == jnp.arange(heads)[:, None]


def per_head_queries(queries, mask):
    groups, count, width = queries.shape
    heads = mask.shape[0]
    blocks = jnp.where(mask[None, None], queries[:, :, None, :], jnp.zeros((), queries.dtype))
    return blocks.reshape(groups, count * heads, width)


def head_diagonal(rows, mask):
    groups, count_heads, width = rows.shape
    heads = mask.shape[0]
    rows = rows.reshape(groups, count_heads // heads, heads, width)
    return jnp.sum(jnp.where(mask[None, None], rows, 0.0), axis=2)


LANES = 128


def pack(values, peak, weight_sum):
    pad = jnp.zeros(values.shape[:-1] + (LANES - HD - 2,), jnp.float32)
    return jnp.concatenate([values, peak[..., None], weight_sum[..., None], pad], axis=-1)


def merge(first, second):
    m1 = first[..., HD:HD + 1]
    m2 = second[..., HD:HD + 1]
    m = jnp.maximum(m1, m2)
    a1 = jnp.exp(m1 - m)
    a2 = jnp.exp(m2 - m)
    merged = first * a1 + second * a2
    lane = lax.broadcasted_iota(jnp.int32, merged.shape, merged.ndim - 1)
    return jnp.where(lane == HD, m, merged)


def exchange(part, distance, count):
    pairs = [(i, i ^ distance) for i in range(count)]
    return lax.ppermute(part, "seq", pairs)


def combine_over_seq(packed, count):
    heads, rows, lanes = packed.shape
    half_heads = heads // 2
    me = lax.axis_index("seq")
    core = me % 2
    halves = packed.reshape(2, half_heads * rows, lanes)
    kept = lax.dynamic_index_in_dim(halves, core, axis=0, keepdims=False)
    sent = lax.dynamic_index_in_dim(halves, 1 - core, axis=0, keepdims=False)
    got = exchange(sent, 1, count)
    low_first = core == 0
    state = merge(jnp.where(low_first, kept, got), jnp.where(low_first, got, kept))
    distance = 2
    while distance < count:
        got = exchange(state, distance, count)
        low_first = (me // distance) % 2 == 0
        state = merge(jnp.where(low_first, state, got), jnp.where(low_first, got, state))
        distance *= 2
    other = exchange(state, 1, count)
    low_half = jnp.where(core == 0, state, other)
    high_half = jnp.where(core == 0, other, state)
    return jnp.concatenate([low_half, high_half], axis=0).reshape(heads, rows, lanes)


def shards(
    patches, key_cache, value_cache, cache_len, attn_gain, w_qkv, w_out, ffn_gain, w_up, w_down
):
    groups, count_new, model_width = patches.shape
    slots_here = key_cache.shape[1]
    seq_count = lax.axis_size("seq")
    inputs = patches.reshape(groups * count_new, model_width).astype(jnp.float32)
    normed = rms_norm(inputs, attn_gain).astype(jnp.bfloat16)
    projected = project(normed, w_qkv).reshape(groups, count_new, 3 * model_width)
    queries = projected[:, :, :model_width]
    keys_new = projected[:, :, model_width:2 * model_width]
    values_new = projected[:, :, 2 * model_width:]
    mask = head_mask(HEADS, model_width)
    query_rows = per_head_queries(queries, mask)
    scale_factor = HD ** (-0.5)
    position = lax.axis_index("seq") * slots_here + jnp.arange(slots_here, dtype=jnp.int32)
    live_mask = (position[None, :] < cache_len[:, None])[:, None, :]
    cache_scores = (
        jnp.einsum("rqc,rsc->rqs", query_rows, key_cache, preferred_element_type=jnp.float32)
        * scale_factor
    )
    masked = jnp.where(live_mask, cache_scores, negative_fill)
    peak_score = jnp.max(masked, axis=2)
    weights = jnp.where(live_mask, jnp.exp(masked - peak_score[..., None]), 0.0)
    weight_sum = jnp.sum(weights, axis=2)
    value_rows = jnp.einsum(
        "rqs,rsc->rqc", weights.astype(jnp.bfloat16), value_cache, preferred_element_type=jnp.float32
    )
    value_sum = head_diagonal(value_rows, mask)
    rows = groups * count_new
    packed = pack(
        value_sum.reshape(rows, HEADS, HD).transpose(1, 0, 2),
        peak_score.reshape(rows, HEADS).T,
        weight_sum.reshape(rows, HEADS).T,
    )
    query_heads = queries.reshape(groups, count_new, HEADS, HD)
    key_heads = keys_new.reshape(groups, count_new, HEADS, HD)
    value_heads = values_new.reshape(groups, count_new, HEADS, HD)
    new_scores = (
        jnp.einsum("rthd,ruhd->rthu", query_heads, key_heads, preferred_element_type=jnp.float32)
        * scale_factor
    )
    causal = (jnp.arange(count_new)[:, None] >= jnp.arange(count_new)[None, :])[None, :, None, :]
    new_masked = jnp.where(causal, new_scores, negative_fill)
    new_peak = jnp.max(new_masked, axis=3)
    new_weights = jnp.where(causal, jnp.exp(new_masked - new_peak[..., None]), 0.0)
    new_sum = jnp.sum(new_weights, axis=3)
    new_values = jnp.einsum(
        "rthu,ruhd->rthd",
        new_weights.astype(jnp.bfloat16),
        value_heads,
        preferred_element_type=jnp.float32,
    )
    new_packed = pack(
        new_values.reshape(rows, HEADS, HD).transpose(1, 0, 2),
        new_peak.reshape(rows, HEADS).T,
        new_sum.reshape(rows, HEADS).T,
    )
    total = merge(combine_over_seq(packed, seq_count), new_packed)
    attended_heads = total[..., :HD] / total[..., HD + 1:HD + 2]
    attended = attended_heads.transpose(1, 0, 2).reshape(rows, model_width).astype(jnp.bfloat16)
    out_rows = project(attended, w_out)
    mixed_rows = inputs + out_rows.astype(jnp.float32)
    normed_mixed = rms_norm(mixed_rows, ffn_gain).astype(jnp.bfloat16)
    up_rows = project(normed_mixed, w_up)
    hidden = jax.nn.silu(up_rows.astype(jnp.float32)).astype(jnp.bfloat16)
    down_rows = project(hidden, w_down)
    decoded = (mixed_rows + down_rows.astype(jnp.float32)).astype(jnp.bfloat16)
    return decoded.reshape(groups, count_new, model_width)


def solution(mesh):
    placed = (
        P("req", None, None),
        P("req", "seq", None),
        P("req", "seq", None),
        P("req"),
        P(),
        P(),
        P(),
        P(),
        P(),
        P(),
    )
    return jax.shard_map(
        shards, mesh=mesh, in_specs=placed, out_specs=P("req", None, None), check_vma=False
    )
```

```python
import jax
import jax.numpy as jnp
from jax import lax
from jax.sharding import PartitionSpec as P
from jax.experimental import pallas as pl
from jax.experimental.pallas import tpu as pltpu

HEADS = 16
HD = 80


epsilon = 1e-06
negative_fill = -1e30


def rms_norm(values, gain):
    return values * lax.rsqrt(jnp.mean(values * values, axis=-1, keepdims=True) + epsilon) * gain


def project(token_rows, weight):
    return jnp.dot(token_rows, weight, preferred_element_type=jnp.float32).astype(jnp.bfloat16)


def head_mask(heads, width):
    return (jnp.arange(width)[None, :] // HD) == jnp.arange(heads)[:, None]


def per_head_queries(queries, mask):
    groups, count, width = queries.shape
    heads = mask.shape[0]
    blocks = jnp.where(mask[None, None], queries[:, :, None, :], jnp.zeros((), queries.dtype))
    return blocks.reshape(groups, count * heads, width)


def head_diagonal(rows, mask):
    groups, count_heads, width = rows.shape
    heads = mask.shape[0]
    rows = rows.reshape(groups, count_heads // heads, heads, width)
    return jnp.sum(jnp.where(mask[None, None], rows, 0.0), axis=2)


LANES = 128


def pack(values, peak, weight_sum):
    pad = jnp.zeros(values.shape[:-1] + (LANES - HD - 2,), jnp.float32)
    return jnp.concatenate([values, peak[..., None], weight_sum[..., None], pad], axis=-1)


def merge(first, second):
    m1 = first[..., HD:HD + 1]
    m2 = second[..., HD:HD + 1]
    m = jnp.maximum(m1, m2)
    a1 = jnp.exp(m1 - m)
    a2 = jnp.exp(m2 - m)
    merged = first * a1 + second * a2
    lane = lax.broadcasted_iota(jnp.int32, merged.shape, merged.ndim - 1)
    return jnp.where(lane == HD, m, merged)


def exchange(part, distance, count):
    pairs = [(i, i ^ distance) for i in range(count)]
    return lax.ppermute(part, "seq", pairs)


def combine_over_seq(packed, count):
    heads, rows, lanes = packed.shape
    half_heads = heads // 2
    me = lax.axis_index("seq")
    core = me % 2
    halves = packed.reshape(2, half_heads * rows, lanes)
    kept = lax.dynamic_index_in_dim(halves, core, axis=0, keepdims=False)
    sent = lax.dynamic_index_in_dim(halves, 1 - core, axis=0, keepdims=False)
    got = exchange(sent, 1, count)
    low_first = core == 0
    state = merge(jnp.where(low_first, kept, got), jnp.where(low_first, got, kept))
    distance = 2
    while distance < count:
        got = exchange(state, distance, count)
        low_first = (me // distance) % 2 == 0
        state = merge(jnp.where(low_first, state, got), jnp.where(low_first, got, state))
        distance *= 2
    other = exchange(state, 1, count)
    low_half = jnp.where(core == 0, state, other)
    high_half = jnp.where(core == 0, other, state)
    return jnp.concatenate([low_half, high_half], axis=0).reshape(heads, rows, lanes)


def cache_partial_kernel(offset_ref, length_ref, proj_ref, key_ref, value_ref, qmask_ref, fold_ref, out_ref):
    groups, slots, width = key_ref.shape
    heads = out_ref.shape[0]
    count = out_ref.shape[1] // groups
    scale_factor = HD ** (-0.5)
    qmask = qmask_ref[...]
    fold = fold_ref[...]
    position = offset_ref[0] + lax.broadcasted_iota(jnp.int32, (1, slots), 1)
    lane = lax.broadcasted_iota(jnp.int32, (heads * count, LANES), 1)
    for r in range(groups):
        queries = proj_ref[pl.ds(r * count, count), pl.ds(0, width)]
        query_rows = jnp.concatenate([queries] * heads, axis=0) * qmask
        scores = lax.dot_general(
            query_rows, key_ref[r], (((1,), (1,)), ((), ())), preferred_element_type=jnp.float32
        ) * scale_factor
        live = position < length_ref[r]
        masked = jnp.where(live, scores, negative_fill)
        peak = jnp.max(masked, axis=1, keepdims=True)
        weights = jnp.where(live, jnp.exp(masked - peak), 0.0)
        total = jnp.sum(weights, axis=1, keepdims=True)
        value_rows = jnp.dot(
            weights.astype(jnp.bfloat16), value_ref[r], preferred_element_type=jnp.float32
        )
        own = value_rows * qmask.astype(jnp.float32)
        folded = jnp.dot(own, fold, precision=lax.Precision.HIGHEST, preferred_element_type=jnp.float32)
        folded = jnp.where(lane == HD, peak, jnp.where(lane == HD + 1, total, folded))
        for h in range(heads):
            out_ref[h, pl.ds(r * count, count), :] = folded[h * count:(h + 1) * count, :]


def cache_partials(offset, cache_len, projected_rows, key_cache, value_cache):
    groups, slots, width = key_cache.shape
    rows = projected_rows.shape[0]
    count = rows // groups
    row_head = jnp.arange(HEADS * count)[:, None] // count
    col_head = jnp.arange(width)[None, :] // HD
    qmask = (row_head == col_head).astype(jnp.bfloat16)
    fold = (jnp.arange(width)[:, None] % HD == jnp.arange(LANES)[None, :]).astype(jnp.float32)
    smem = pl.BlockSpec(memory_space=pltpu.SMEM)
    vmem = pl.BlockSpec(memory_space=pltpu.VMEM)
    return pl.pallas_call(
        cache_partial_kernel,
        out_shape=jax.ShapeDtypeStruct((HEADS, rows, LANES), jnp.float32),
        in_specs=[smem, smem, vmem, vmem, vmem, vmem, vmem],
        out_specs=vmem,
    )(offset, cache_len, projected_rows, key_cache, value_cache, qmask, fold)


def shards(
    patches, key_cache, value_cache, cache_len, attn_gain, w_qkv, w_out, ffn_gain, w_up, w_down
):
    groups, count_new, model_width = patches.shape
    slots_here = key_cache.shape[1]
    seq_count = lax.axis_size("seq")
    inputs = patches.reshape(groups * count_new, model_width).astype(jnp.float32)
    normed = rms_norm(inputs, attn_gain).astype(jnp.bfloat16)
    projected = project(normed, w_qkv).reshape(groups, count_new, 3 * model_width)
    queries = projected[:, :, :model_width]
    keys_new = projected[:, :, model_width:2 * model_width]
    values_new = projected[:, :, 2 * model_width:]
    scale_factor = HD ** (-0.5)
    rows = groups * count_new
    offset = (lax.axis_index("seq") * slots_here).astype(jnp.int32).reshape(1)
    packed = cache_partials(
        offset, cache_len, projected.reshape(rows, 3 * model_width), key_cache, value_cache
    )
    query_heads = queries.reshape(groups, count_new, HEADS, HD)
    key_heads = keys_new.reshape(groups, count_new, HEADS, HD)
    value_heads = values_new.reshape(groups, count_new, HEADS, HD)
    new_scores = (
        jnp.einsum("rthd,ruhd->rthu", query_heads, key_heads, preferred_element_type=jnp.float32)
        * scale_factor
    )
    causal = (jnp.arange(count_new)[:, None] >= jnp.arange(count_new)[None, :])[None, :, None, :]
    new_masked = jnp.where(causal, new_scores, negative_fill)
    new_peak = jnp.max(new_masked, axis=3)
    new_weights = jnp.where(causal, jnp.exp(new_masked - new_peak[..., None]), 0.0)
    new_sum = jnp.sum(new_weights, axis=3)
    new_values = jnp.einsum(
        "rthu,ruhd->rthd",
        new_weights.astype(jnp.bfloat16),
        value_heads,
        preferred_element_type=jnp.float32,
    )
    new_packed = pack(
        new_values.reshape(rows, HEADS, HD).transpose(1, 0, 2),
        new_peak.reshape(rows, HEADS).T,
        new_sum.reshape(rows, HEADS).T,
    )
    total = merge(combine_over_seq(packed, seq_count), new_packed)
    attended_heads = total[..., :HD] / total[..., HD + 1:HD + 2]
    attended = attended_heads.transpose(1, 0, 2).reshape(rows, model_width).astype(jnp.bfloat16)
    out_rows = project(attended, w_out)
    mixed_rows = inputs + out_rows.astype(jnp.float32)
    normed_mixed = rms_norm(mixed_rows, ffn_gain).astype(jnp.bfloat16)
    up_rows = project(normed_mixed, w_up)
    hidden = jax.nn.silu(up_rows.astype(jnp.float32)).astype(jnp.bfloat16)
    down_rows = project(hidden, w_down)
    decoded = (mixed_rows + down_rows.astype(jnp.float32)).astype(jnp.bfloat16)
    return decoded.reshape(groups, count_new, model_width)


def solution(mesh):
    placed = (
        P("req", None, None),
        P("req", "seq", None),
        P("req", "seq", None),
        P("req"),
        P(),
        P(),
        P(),
        P(),
        P(),
        P(),
    )
    return jax.shard_map(
        shards, mesh=mesh, in_specs=placed, out_specs=P("req", None, None), check_vma=False
    )
```

```python
import numpy as np
import jax
import jax.numpy as jnp
from jax import lax
from jax.sharding import PartitionSpec as P
from jax.experimental import pallas as pl
from jax.experimental.pallas import tpu as pltpu

HEADS = 16
HD = 80


epsilon = 1e-06
negative_fill = -1e30


def rms_norm(values, gain):
    return values * lax.rsqrt(jnp.mean(values * values, axis=-1, keepdims=True) + epsilon) * gain


def project(token_rows, weight):
    return jnp.dot(token_rows, weight, preferred_element_type=jnp.float32).astype(jnp.bfloat16)


def head_mask(heads, width):
    return (jnp.arange(width)[None, :] // HD) == jnp.arange(heads)[:, None]


def per_head_queries(queries, mask):
    groups, count, width = queries.shape
    heads = mask.shape[0]
    blocks = jnp.where(mask[None, None], queries[:, :, None, :], jnp.zeros((), queries.dtype))
    return blocks.reshape(groups, count * heads, width)


def head_diagonal(rows, mask):
    groups, count_heads, width = rows.shape
    heads = mask.shape[0]
    rows = rows.reshape(groups, count_heads // heads, heads, width)
    return jnp.sum(jnp.where(mask[None, None], rows, 0.0), axis=2)


LANES = 128


def pack(values, peak, weight_sum):
    pad = jnp.zeros(values.shape[:-1] + (LANES - HD - 2,), jnp.float32)
    return jnp.concatenate([values, peak[..., None], weight_sum[..., None], pad], axis=-1)


def merge(first, second):
    m1 = first[..., HD:HD + 1]
    m2 = second[..., HD:HD + 1]
    m = jnp.maximum(m1, m2)
    a1 = jnp.exp(m1 - m)
    a2 = jnp.exp(m2 - m)
    merged = first * a1 + second * a2
    lane = lax.broadcasted_iota(jnp.int32, merged.shape, merged.ndim - 1)
    return jnp.where(lane == HD, m, merged)


def exchange(part, distance, count):
    pairs = [(i, i ^ distance) for i in range(count)]
    return lax.ppermute(part, "seq", pairs)


def combine_over_seq(packed, count):
    heads, rows, lanes = packed.shape
    half_heads = heads // 2
    me = lax.axis_index("seq")
    core = me % 2
    halves = packed.reshape(2, half_heads * rows, lanes)
    kept = lax.dynamic_index_in_dim(halves, core, axis=0, keepdims=False)
    sent = lax.dynamic_index_in_dim(halves, 1 - core, axis=0, keepdims=False)
    got = exchange(sent, 1, count)
    low_first = core == 0
    state = merge(jnp.where(low_first, kept, got), jnp.where(low_first, got, kept))
    distance = 2
    while distance < count:
        got = exchange(state, distance, count)
        low_first = (me // distance) % 2 == 0
        state = merge(jnp.where(low_first, state, got), jnp.where(low_first, got, state))
        distance *= 2
    other = exchange(state, 1, count)
    low_half = jnp.where(core == 0, state, other)
    high_half = jnp.where(core == 0, other, state)
    return jnp.concatenate([low_half, high_half], axis=0).reshape(heads, rows, lanes)


def cache_partial_kernel(
    offset_ref, length_ref, proj_ref, key_ref, value_ref, qmask_ref, fold_ref, out_ref, new_ref
):
    groups, slots, width = key_ref.shape
    heads = out_ref.shape[0]
    count = out_ref.shape[1] // groups
    scale_factor = HD ** (-0.5)
    qmask = qmask_ref[...]
    qmask_float = qmask.astype(jnp.float32)
    fold = fold_ref[...]
    position = offset_ref[0] + lax.broadcasted_iota(jnp.int32, (1, slots), 1)
    lane = lax.broadcasted_iota(jnp.int32, (heads * count, LANES), 1)
    patch = lax.broadcasted_iota(jnp.int32, (heads * count, 1), 0) & (count - 1)

    def emit(target, r, rows, peak, total):
        folded = jnp.dot(
            rows * qmask_float, fold, precision=lax.Precision.HIGHEST, preferred_element_type=jnp.float32
        )
        folded = jnp.where(lane == HD, peak, jnp.where(lane == HD + 1, total, folded))
        for h in range(heads):
            target[h, pl.ds(r * count, count), :] = folded[h * count:(h + 1) * count, :]

    for r in range(groups):
        queries = proj_ref[pl.ds(r * count, count), pl.ds(0, width)]
        query_rows = jnp.concatenate([queries] * heads, axis=0) * qmask
        scores = lax.dot_general(
            query_rows, key_ref[r], (((1,), (1,)), ((), ())), preferred_element_type=jnp.float32
        ) * scale_factor
        live = position < length_ref[r]
        masked = jnp.where(live, scores, negative_fill)
        peak = jnp.max(masked, axis=1, keepdims=True)
        weights = jnp.where(live, jnp.exp(masked - peak), 0.0)
        total = jnp.sum(weights, axis=1, keepdims=True)
        value_rows = jnp.dot(
            weights.astype(jnp.bfloat16), value_ref[r], preferred_element_type=jnp.float32
        )
        emit(out_ref, r, value_rows, peak, total)

        query_float = query_rows.astype(jnp.float32)
        keys_new = proj_ref[pl.ds(r * count, count), pl.ds(width, width)].astype(jnp.float32)
        values_new = proj_ref[pl.ds(r * count, count), pl.ds(2 * width, width)].astype(jnp.float32)
        new_scores = []
        for u in range(count):
            score = jnp.sum(query_float * keys_new[u:u + 1, :], axis=1, keepdims=True) * scale_factor
            new_scores.append(jnp.where(patch >= u, score, negative_fill))
        new_peak = new_scores[0]
        for score in new_scores[1:]:
            new_peak = jnp.maximum(new_peak, score)
        new_total = jnp.zeros_like(new_peak)
        new_rows = jnp.zeros((heads * count, width), jnp.float32)
        for u in range(count):
            weight = jnp.where(patch >= u, jnp.exp(new_scores[u] - new_peak), 0.0)
            new_total = new_total + weight
            weight = weight.astype(jnp.bfloat16).astype(jnp.float32)
            new_rows = new_rows + weight * values_new[u:u + 1, :]
        emit(new_ref, r, new_rows, new_peak, new_total)


def cache_partials(offset, cache_len, projected_rows, key_cache, value_cache):
    groups, slots, width = key_cache.shape
    rows = projected_rows.shape[0]
    count = rows // groups
    row_head = np.arange(HEADS * count)[:, None] // count
    col_head = np.arange(width)[None, :] // HD
    qmask = jnp.asarray((row_head == col_head).astype(np.float32), dtype=jnp.bfloat16)
    fold = jnp.asarray((np.arange(width)[:, None] % HD == np.arange(LANES)[None, :]).astype(np.float32))
    smem = pl.BlockSpec(memory_space=pltpu.SMEM)
    vmem = pl.BlockSpec(memory_space=pltpu.VMEM)
    packed = jax.ShapeDtypeStruct((HEADS, rows, LANES), jnp.float32)
    return pl.pallas_call(
        cache_partial_kernel,
        out_shape=(packed, packed),
        in_specs=[smem, smem, vmem, vmem, vmem, vmem, vmem],
        out_specs=(vmem, vmem),
    )(offset, cache_len, projected_rows, key_cache, value_cache, qmask, fold)


def shards(
    patches, key_cache, value_cache, cache_len, attn_gain, w_qkv, w_out, ffn_gain, w_up, w_down
):
    groups, count_new, model_width = patches.shape
    slots_here = key_cache.shape[1]
    seq_count = lax.axis_size("seq")
    inputs = patches.reshape(groups * count_new, model_width).astype(jnp.float32)
    normed = rms_norm(inputs, attn_gain).astype(jnp.bfloat16)
    projected = project(normed, w_qkv).reshape(groups, count_new, 3 * model_width)
    queries = projected[:, :, :model_width]
    keys_new = projected[:, :, model_width:2 * model_width]
    values_new = projected[:, :, 2 * model_width:]
    scale_factor = HD ** (-0.5)
    rows = groups * count_new
    offset = (lax.axis_index("seq") * slots_here).astype(jnp.int32).reshape(1)
    packed, new_packed = cache_partials(
        offset, cache_len, projected.reshape(rows, 3 * model_width), key_cache, value_cache
    )
    total = merge(combine_over_seq(packed, seq_count), new_packed)
    attended_heads = total[..., :HD] / total[..., HD + 1:HD + 2]
    attended = attended_heads.transpose(1, 0, 2).reshape(rows, model_width).astype(jnp.bfloat16)
    out_rows = project(attended, w_out)
    mixed_rows = inputs + out_rows.astype(jnp.float32)
    normed_mixed = rms_norm(mixed_rows, ffn_gain).astype(jnp.bfloat16)
    up_rows = project(normed_mixed, w_up)
    hidden = jax.nn.silu(up_rows.astype(jnp.float32)).astype(jnp.bfloat16)
    down_rows = project(hidden, w_down)
    decoded = (mixed_rows + down_rows.astype(jnp.float32)).astype(jnp.bfloat16)
    return decoded.reshape(groups, count_new, model_width)


def solution(mesh):
    placed = (
        P("req", None, None),
        P("req", "seq", None),
        P("req", "seq", None),
        P("req"),
        P(),
        P(),
        P(),
        P(),
        P(),
        P(),
    )
    return jax.shard_map(
        shards, mesh=mesh, in_specs=placed, out_specs=P("req", None, None), check_vma=False
    )
```

```python
import functools

import numpy as np
import jax
import jax.numpy as jnp
from jax import lax
from jax.sharding import PartitionSpec as P
from jax.experimental import pallas as pl
from jax.experimental.pallas import tpu as pltpu

HEADS = 16
HD = 80


epsilon = 1e-06
negative_fill = -1e30


def rms_norm(values, gain):
    return values * lax.rsqrt(jnp.mean(values * values, axis=-1, keepdims=True) + epsilon) * gain


def project(token_rows, weight):
    return jnp.dot(token_rows, weight, preferred_element_type=jnp.float32).astype(jnp.bfloat16)


LANES = 128


def merge(first, second):
    m1 = first[..., HD:HD + 1]
    m2 = second[..., HD:HD + 1]
    m = jnp.maximum(m1, m2)
    a1 = jnp.exp(m1 - m)
    a2 = jnp.exp(m2 - m)
    merged = first * a1 + second * a2
    lane = lax.broadcasted_iota(jnp.int32, merged.shape, merged.ndim - 1)
    return jnp.where(lane == HD, m, merged)


def exchange(part, distance, count):
    pairs = [(i, i ^ distance) for i in range(count)]
    return lax.ppermute(part, "seq", pairs)


def combine_over_seq(packed, count):
    heads, rows, lanes = packed.shape
    half_heads = heads // 2
    me = lax.axis_index("seq")
    core = me % 2
    halves = packed.reshape(2, half_heads * rows, lanes)
    kept = lax.dynamic_index_in_dim(halves, core, axis=0, keepdims=False)
    sent = lax.dynamic_index_in_dim(halves, 1 - core, axis=0, keepdims=False)
    got = exchange(sent, 1, count)
    low_first = core == 0
    state = merge(jnp.where(low_first, kept, got), jnp.where(low_first, got, kept))
    distance = 2
    while distance < count:
        got = exchange(state, distance, count)
        low_first = (me // distance) % 2 == 0
        state = merge(jnp.where(low_first, state, got), jnp.where(low_first, got, state))
        distance *= 2
    other = exchange(state, 1, count)
    low_half = jnp.where(core == 0, state, other)
    high_half = jnp.where(core == 0, other, state)
    return jnp.concatenate([low_half, high_half], axis=0).reshape(heads, rows, lanes)


def folded_store(target, r, rows, peak, total, qmask_float, fold, lane):
    heads = target.shape[0]
    count = rows.shape[0] // heads
    folded = jnp.dot(
        rows * qmask_float, fold, precision=lax.Precision.HIGHEST, preferred_element_type=jnp.float32
    )
    folded = jnp.where(lane == HD, peak, jnp.where(lane == HD + 1, total, folded))
    for h in range(heads):
        target[h, pl.ds(r * count, count), :] = folded[h * count:(h + 1) * count, :]


def cache_partial_kernel(offset_ref, length_ref, query_ref, key_ref, value_ref, qmask_ref, fold_ref, out_ref):
    groups, slots, _ = key_ref.shape
    heads = out_ref.shape[0]
    count = out_ref.shape[1] // groups
    scale_factor = HD ** (-0.5)
    qmask = qmask_ref[...]
    qmask_float = qmask.astype(jnp.float32)
    fold = fold_ref[...]
    position = offset_ref[0] + lax.broadcasted_iota(jnp.int32, (1, slots), 1)
    lane = lax.broadcasted_iota(jnp.int32, (heads * count, LANES), 1)
    for r in range(groups):
        queries = query_ref[pl.ds(r * count, count), :]
        query_rows = jnp.concatenate([queries] * heads, axis=0) * qmask
        scores = lax.dot_general(
            query_rows, key_ref[r], (((1,), (1,)), ((), ())), preferred_element_type=jnp.float32
        ) * scale_factor
        live = position < length_ref[r]
        masked = jnp.where(live, scores, negative_fill)
        peak = jnp.max(masked, axis=1, keepdims=True)
        weights = jnp.where(live, jnp.exp(masked - peak), 0.0)
        total = jnp.sum(weights, axis=1, keepdims=True)
        value_rows = jnp.dot(
            weights.astype(jnp.bfloat16), value_ref[r], preferred_element_type=jnp.float32
        )
        folded_store(out_ref, r, value_rows, peak, total, qmask_float, fold, lane)


def new_partial_kernel(count, query_ref, kv_ref, qmask_ref, fold_ref, out_ref):
    rows_all, width = query_ref.shape
    heads = out_ref.shape[0]
    groups = rows_all // count
    scale_factor = HD ** (-0.5)
    qmask = qmask_ref[...]
    qmask_float = qmask.astype(jnp.float32)
    fold = fold_ref[...]
    lane = lax.broadcasted_iota(jnp.int32, (heads * count, LANES), 1)
    patch = lax.broadcasted_iota(jnp.int32, (heads * count, 1), 0) & (count - 1)
    for r in range(groups):
        queries = query_ref[pl.ds(r * count, count), :]
        query_float = (jnp.concatenate([queries] * heads, axis=0) * qmask).astype(jnp.float32)
        keys_new = kv_ref[pl.ds(r * count, count), pl.ds(0, width)].astype(jnp.float32)
        values_new = kv_ref[pl.ds(r * count, count), pl.ds(width, width)].astype(jnp.float32)
        new_scores = []
        for u in range(count):
            score = jnp.sum(query_float * keys_new[u:u + 1, :], axis=1, keepdims=True) * scale_factor
            new_scores.append(jnp.where(patch >= u, score, negative_fill))
        new_peak = new_scores[0]
        for score in new_scores[1:]:
            new_peak = jnp.maximum(new_peak, score)
        new_total = jnp.zeros_like(new_peak)
        new_rows = jnp.zeros((heads * count, width), jnp.float32)
        for u in range(count):
            weight = jnp.where(patch >= u, jnp.exp(new_scores[u] - new_peak), 0.0)
            new_total = new_total + weight
            weight = weight.astype(jnp.bfloat16).astype(jnp.float32)
            new_rows = new_rows + weight * values_new[u:u + 1, :]
        folded_store(out_ref, r, new_rows, new_peak, new_total, qmask_float, fold, lane)


def head_constants(count, width):
    row_head = np.arange(HEADS * count)[:, None] // count
    col_head = np.arange(width)[None, :] // HD
    qmask = jnp.asarray((row_head == col_head).astype(np.float32), dtype=jnp.bfloat16)
    fold = jnp.asarray((np.arange(width)[:, None] % HD == np.arange(LANES)[None, :]).astype(np.float32))
    return qmask, fold


def cache_partials(offset, cache_len, query_rows, key_cache, value_cache):
    groups, _, width = key_cache.shape
    rows = query_rows.shape[0]
    qmask, fold = head_constants(rows // groups, width)
    smem = pl.BlockSpec(memory_space=pltpu.SMEM)
    vmem = pl.BlockSpec(memory_space=pltpu.VMEM)
    return pl.pallas_call(
        cache_partial_kernel,
        out_shape=jax.ShapeDtypeStruct((HEADS, rows, LANES), jnp.float32),
        in_specs=[smem, smem, vmem, vmem, vmem, vmem, vmem],
        out_specs=vmem,
    )(offset, cache_len, query_rows, key_cache, value_cache, qmask, fold)


def new_partials(query_rows, kv_rows, count):
    rows, width = query_rows.shape
    qmask, fold = head_constants(count, width)
    vmem = pl.BlockSpec(memory_space=pltpu.VMEM)
    return pl.pallas_call(
        functools.partial(new_partial_kernel, count),
        out_shape=jax.ShapeDtypeStruct((HEADS, rows, LANES), jnp.float32),
        in_specs=[vmem, vmem, vmem, vmem],
        out_specs=vmem,
    )(query_rows, kv_rows, qmask, fold)


def layer(
    patches, key_cache, value_cache, cache_len, attn_gain, w_qkv, w_out, ffn_gain, w_up, w_down
):
    groups, count_new, model_width = patches.shape
    slots_here = key_cache.shape[1]
    seq_count = lax.axis_size("seq")
    inputs = patches.reshape(groups * count_new, model_width).astype(jnp.float32)
    normed = rms_norm(inputs, attn_gain).astype(jnp.bfloat16)
    rows = groups * count_new
    query_rows = project(normed, w_qkv[:, :model_width])
    offset = (lax.axis_index("seq") * slots_here).astype(jnp.int32).reshape(1)
    packed = cache_partials(offset, cache_len, query_rows, key_cache, value_cache)
    kv_rows = project(normed, w_qkv[:, model_width:])
    new_packed = new_partials(query_rows, kv_rows, count_new)
    total = merge(combine_over_seq(packed, seq_count), new_packed)
    attended_heads = total[..., :HD] / total[..., HD + 1:HD + 2]
    attended = attended_heads.transpose(1, 0, 2).reshape(rows, model_width).astype(jnp.bfloat16)
    out_rows = project(attended, w_out)
    mixed_rows = inputs + out_rows.astype(jnp.float32)
    normed_mixed = rms_norm(mixed_rows, ffn_gain).astype(jnp.bfloat16)
    up_rows = project(normed_mixed, w_up)
    hidden = jax.nn.silu(up_rows.astype(jnp.float32)).astype(jnp.bfloat16)
    down_rows = project(hidden, w_down)
    decoded = (mixed_rows + down_rows.astype(jnp.float32)).astype(jnp.bfloat16)
    return decoded.reshape(groups, count_new, model_width)


def solution(mesh):
    placed = (
        P("req", None, None),
        P("req", "seq", None),
        P("req", "seq", None),
        P("req"),
        P(),
        P(),
        P(),
        P(),
        P(),
        P(),
    )
    return jax.shard_map(
        layer, mesh=mesh, in_specs=placed, out_specs=P("req", None, None), check_vma=False
    )
```

```python
import functools

import numpy as np
import jax
import jax.numpy as jnp
from jax import lax
from jax.sharding import PartitionSpec as P
from jax.experimental.layout import Layout, with_layout_constraint
from jax.experimental import pallas as pl
from jax.experimental.pallas import tpu as pltpu

HEADS = 16
HD = 80


epsilon = 1e-06
negative_fill = -1e30


def rms_norm(values, gain):
    return values * lax.rsqrt(jnp.mean(values * values, axis=-1, keepdims=True) + epsilon) * gain


def project(token_rows, weight):
    return jnp.dot(token_rows, weight, preferred_element_type=jnp.float32).astype(jnp.bfloat16)


LANES = 128


def merge(first, second):
    m1 = first[..., HD:HD + 1]
    m2 = second[..., HD:HD + 1]
    m = jnp.maximum(m1, m2)
    a1 = jnp.exp(m1 - m)
    a2 = jnp.exp(m2 - m)
    merged = first * a1 + second * a2
    lane = lax.broadcasted_iota(jnp.int32, merged.shape, merged.ndim - 1)
    return jnp.where(lane == HD, m, merged)


def exchange(part, distance, count):
    pairs = [(i, i ^ distance) for i in range(count)]
    row_major = Layout(major_to_minor=(0, 1))
    part = with_layout_constraint(part, row_major)
    return with_layout_constraint(lax.ppermute(part, "seq", pairs), row_major)


def combine_over_seq(kept, sent, count):
    half_heads, rows, lanes = kept.shape
    me = lax.axis_index("seq")
    core = me % 2
    kept = kept.reshape(half_heads * rows, lanes)
    sent = sent.reshape(half_heads * rows, lanes)
    got = exchange(sent, 1, count)
    low_first = core == 0
    state = merge(jnp.where(low_first, kept, got), jnp.where(low_first, got, kept))
    distance = 2
    while distance < count:
        got = exchange(state, distance, count)
        low_first = (me // distance) % 2 == 0
        state = merge(jnp.where(low_first, state, got), jnp.where(low_first, got, state))
        distance *= 2
    other = exchange(state, 1, count)
    low_half = jnp.where(core == 0, state, other)
    high_half = jnp.where(core == 0, other, state)
    return low_half.reshape(half_heads, rows, lanes), high_half.reshape(half_heads, rows, lanes)


def folded_rows(rows, peak, total, qmask_float, fold, lane):
    folded = jnp.dot(
        rows * qmask_float, fold, precision=lax.Precision.HIGHEST, preferred_element_type=jnp.float32
    )
    return jnp.where(lane == HD, peak, jnp.where(lane == HD + 1, total, folded))


def folded_store(target, r, rows, peak, total, qmask_float, fold, lane):
    heads = target.shape[0]
    count = rows.shape[0] // heads
    folded = folded_rows(rows, peak, total, qmask_float, fold, lane)
    for h in range(heads):
        target[h, pl.ds(r * count, count), :] = folded[h * count:(h + 1) * count, :]


def cache_partial_kernel(
    offset_ref, length_ref, query_ref, key_ref, value_ref, qmask_ref, fold_ref, kept_ref, sent_ref
):
    groups, slots, _ = key_ref.shape
    half_heads = kept_ref.shape[0]
    heads = 2 * half_heads
    count = kept_ref.shape[1] // groups
    core = offset_ref[1]
    scale_factor = HD ** (-0.5)
    qmask = qmask_ref[...]
    qmask_float = qmask.astype(jnp.float32)
    fold = fold_ref[...]
    position = offset_ref[0] + lax.broadcasted_iota(jnp.int32, (1, slots), 1)
    lane = lax.broadcasted_iota(jnp.int32, (heads * count, LANES), 1)
    for r in range(groups):
        queries = query_ref[pl.ds(r * count, count), :]
        query_rows = jnp.concatenate([queries] * heads, axis=0) * qmask
        scores = lax.dot_general(
            query_rows, key_ref[r], (((1,), (1,)), ((), ())), preferred_element_type=jnp.float32
        ) * scale_factor
        live = position < length_ref[r]
        masked = jnp.where(live, scores, negative_fill)
        peak = jnp.max(masked, axis=1, keepdims=True)
        weights = jnp.where(live, jnp.exp(masked - peak), 0.0)
        total = jnp.sum(weights, axis=1, keepdims=True)
        value_rows = jnp.dot(
            weights.astype(jnp.bfloat16), value_ref[r], preferred_element_type=jnp.float32
        )
        folded = folded_rows(value_rows, peak, total, qmask_float, fold, lane)
        for h in range(heads):
            block = folded[h * count:(h + 1) * count, :]
            rows_here = pl.ds(r * count, count)

            @pl.when(core == h // half_heads)
            def _():
                kept_ref[h % half_heads, rows_here, :] = block

            @pl.when(core != h // half_heads)
            def _():
                sent_ref[h % half_heads, rows_here, :] = block


def new_partial_kernel(count, query_ref, kv_ref, qmask_ref, fold_ref, out_ref):
    rows_all, width = query_ref.shape
    heads = out_ref.shape[0]
    groups = rows_all // count
    scale_factor = HD ** (-0.5)
    qmask = qmask_ref[...]
    qmask_float = qmask.astype(jnp.float32)
    fold = fold_ref[...]
    lane = lax.broadcasted_iota(jnp.int32, (heads * count, LANES), 1)
    patch = lax.broadcasted_iota(jnp.int32, (heads * count, 1), 0) & (count - 1)
    for r in range(groups):
        queries = query_ref[pl.ds(r * count, count), :]
        query_float = (jnp.concatenate([queries] * heads, axis=0) * qmask).astype(jnp.float32)
        keys_new = kv_ref[pl.ds(r * count, count), pl.ds(0, width)].astype(jnp.float32)
        values_new = kv_ref[pl.ds(r * count, count), pl.ds(width, width)].astype(jnp.float32)
        new_scores = []
        for u in range(count):
            score = jnp.sum(query_float * keys_new[u:u + 1, :], axis=1, keepdims=True) * scale_factor
            new_scores.append(jnp.where(patch >= u, score, negative_fill))
        new_peak = new_scores[0]
        for score in new_scores[1:]:
            new_peak = jnp.maximum(new_peak, score)
        new_total = jnp.zeros_like(new_peak)
        new_rows = jnp.zeros((heads * count, width), jnp.float32)
        for u in range(count):
            weight = jnp.where(patch >= u, jnp.exp(new_scores[u] - new_peak), 0.0)
            new_total = new_total + weight
            weight = weight.astype(jnp.bfloat16).astype(jnp.float32)
            new_rows = new_rows + weight * values_new[u:u + 1, :]
        folded_store(out_ref, r, new_rows, new_peak, new_total, qmask_float, fold, lane)


def head_constants(count, width):
    row_head = np.arange(HEADS * count)[:, None] // count
    col_head = np.arange(width)[None, :] // HD
    qmask = jnp.asarray((row_head == col_head).astype(np.float32), dtype=jnp.bfloat16)
    fold = jnp.asarray((np.arange(width)[:, None] % HD == np.arange(LANES)[None, :]).astype(np.float32))
    return qmask, fold


def cache_partials(offset, cache_len, query_rows, key_cache, value_cache):
    groups, _, width = key_cache.shape
    rows = query_rows.shape[0]
    qmask, fold = head_constants(rows // groups, width)
    smem = pl.BlockSpec(memory_space=pltpu.SMEM)
    vmem = pl.BlockSpec(memory_space=pltpu.VMEM)
    half = jax.ShapeDtypeStruct((HEADS // 2, rows, LANES), jnp.float32)
    return pl.pallas_call(
        cache_partial_kernel,
        out_shape=(half, half),
        in_specs=[smem, smem, vmem, vmem, vmem, vmem, vmem],
        out_specs=(vmem, vmem),
    )(offset, cache_len, query_rows, key_cache, value_cache, qmask, fold)


def new_partials(query_rows, kv_rows, count):
    rows, width = query_rows.shape
    qmask, fold = head_constants(count, width)
    vmem = pl.BlockSpec(memory_space=pltpu.VMEM)
    return pl.pallas_call(
        functools.partial(new_partial_kernel, count),
        out_shape=jax.ShapeDtypeStruct((HEADS, rows, LANES), jnp.float32),
        in_specs=[vmem, vmem, vmem, vmem],
        out_specs=vmem,
    )(query_rows, kv_rows, qmask, fold)


def tail_kernel(low_ref, high_ref, new_ref, patch_ref, w_out_ref, gain_ref, w_up_ref, w_down_ref, out_ref):
    half_heads, rows, _ = low_ref.shape
    width = w_out_ref.shape[0]
    out_sum = jnp.zeros((rows, width), jnp.float32)
    for h in range(2 * half_heads):
        source = low_ref if h < half_heads else high_ref
        first = source[h % half_heads]
        second = new_ref[h]
        m1 = first[:, HD:HD + 1]
        m2 = second[:, HD:HD + 1]
        m = jnp.maximum(m1, m2)
        merged = first * jnp.exp(m1 - m) + second * jnp.exp(m2 - m)
        attended = (merged / merged[:, HD + 1:HD + 2]).astype(jnp.bfloat16)
        out_sum = out_sum + jnp.dot(
            attended[:, :HD], w_out_ref[pl.ds(h * HD, HD), :], preferred_element_type=jnp.float32
        )
    out_rows = out_sum.astype(jnp.bfloat16).astype(jnp.float32)
    mixed_rows = patch_ref[...].astype(jnp.float32) + out_rows
    normed_mixed = rms_norm(mixed_rows, gain_ref[...]).astype(jnp.bfloat16)
    up_rows = jnp.dot(normed_mixed, w_up_ref[...], preferred_element_type=jnp.float32).astype(jnp.bfloat16)
    up_float = up_rows.astype(jnp.float32)
    hidden = (up_float / (1.0 + jnp.exp(-up_float))).astype(jnp.bfloat16)
    down_rows = jnp.dot(hidden, w_down_ref[...], preferred_element_type=jnp.float32).astype(jnp.bfloat16)
    out_ref[...] = (mixed_rows + down_rows.astype(jnp.float32)).astype(out_ref.dtype)


def tail(low_half, high_half, new_packed, patch_rows, w_out, ffn_gain, w_up, w_down):
    rows, width = patch_rows.shape
    vmem = pl.BlockSpec(memory_space=pltpu.VMEM)
    return pl.pallas_call(
        tail_kernel,
        out_shape=jax.ShapeDtypeStruct((rows, width), jnp.bfloat16),
        in_specs=[vmem] * 8,
        out_specs=vmem,
    )(low_half, high_half, new_packed, patch_rows, w_out, ffn_gain.reshape(1, width), w_up, w_down)


def layer(
    patches, key_cache, value_cache, cache_len, attn_gain, w_qkv, w_out, ffn_gain, w_up, w_down
):
    groups, count_new, model_width = patches.shape
    slots_here = key_cache.shape[1]
    seq_count = lax.axis_size("seq")
    inputs = patches.reshape(groups * count_new, model_width).astype(jnp.float32)
    normed = rms_norm(inputs, attn_gain).astype(jnp.bfloat16)
    rows = groups * count_new
    query_rows = project(normed, w_qkv[:, :model_width])
    me = lax.axis_index("seq")
    offset = jnp.stack([me * slots_here, me % 2]).astype(jnp.int32)
    kept, sent = cache_partials(offset, cache_len, query_rows, key_cache, value_cache)
    kv_rows = project(normed, w_qkv[:, model_width:])
    new_packed = new_partials(query_rows, kv_rows, count_new)
    low_half, high_half = combine_over_seq(kept, sent, seq_count)
    decoded = tail(
        low_half, high_half, new_packed, patches.reshape(rows, model_width), w_out, ffn_gain, w_up, w_down
    )
    return decoded.reshape(groups, count_new, model_width)


def solution(mesh):
    placed = (
        P("req", None, None),
        P("req", "seq", None),
        P("req", "seq", None),
        P("req"),
        P(),
        P(),
        P(),
        P(),
        P(),
        P(),
    )
    return jax.shard_map(layer, mesh=mesh, in_specs=placed, out_specs=P("req", None, None), check_vma=False)
```

```python
import numpy as np
import jax
import jax.numpy as jnp
from jax import lax
from jax.sharding import PartitionSpec as P
from jax.experimental.layout import Layout, with_layout_constraint
from jax.experimental import pallas as pl
from jax.experimental.pallas import tpu as pltpu

HEADS = 16
HD = 80


epsilon = 1e-06
negative_fill = -1e30


def rms_norm(values, gain):
    return values * lax.rsqrt(jnp.mean(values * values, axis=-1, keepdims=True) + epsilon) * gain


def project(token_rows, weight):
    return jnp.dot(token_rows, weight, preferred_element_type=jnp.float32).astype(jnp.bfloat16)


LANES = 128


def merge(first, second):
    m1 = first[..., HD:HD + 1]
    m2 = second[..., HD:HD + 1]
    m = jnp.maximum(m1, m2)
    a1 = jnp.exp(m1 - m)
    a2 = jnp.exp(m2 - m)
    merged = first * a1 + second * a2
    lane = lax.broadcasted_iota(jnp.int32, merged.shape, merged.ndim - 1)
    return jnp.where(lane == HD, m, merged)


def exchange(part, distance, count):
    pairs = [(i, i ^ distance) for i in range(count)]
    row_major = Layout(major_to_minor=(0, 1))
    part = with_layout_constraint(part, row_major)
    return with_layout_constraint(lax.ppermute(part, "seq", pairs), row_major)


def combine_over_seq(kept, sent, count):
    half_heads, rows, lanes = kept.shape
    me = lax.axis_index("seq")
    core = me % 2
    kept = kept.reshape(half_heads * rows, lanes)
    sent = sent.reshape(half_heads * rows, lanes)
    got = exchange(sent, 1, count)
    low_first = core == 0
    state = merge(jnp.where(low_first, kept, got), jnp.where(low_first, got, kept))
    distance = 2
    while distance < count:
        got = exchange(state, distance, count)
        low_first = (me // distance) % 2 == 0
        state = merge(jnp.where(low_first, state, got), jnp.where(low_first, got, state))
        distance *= 2
    other = exchange(state, 1, count)
    low_half = jnp.where(core == 0, state, other)
    high_half = jnp.where(core == 0, other, state)
    return low_half.reshape(half_heads, rows, lanes), high_half.reshape(half_heads, rows, lanes)


def folded_rows(rows, peak, total, qmask_float, fold, lane):
    folded = jnp.dot(
        rows * qmask_float, fold, precision=lax.Precision.HIGHEST, preferred_element_type=jnp.float32
    )
    return jnp.where(lane == HD, peak, jnp.where(lane == HD + 1, total, folded))


def folded_store(target, r, rows, peak, total, qmask_float, fold, lane):
    heads = target.shape[0]
    count = rows.shape[0] // heads
    folded = folded_rows(rows, peak, total, qmask_float, fold, lane)
    for h in range(heads):
        target[h, pl.ds(r * count, count), :] = folded[h * count:(h + 1) * count, :]


def cache_partial_kernel(
    offset_ref, length_ref, query_ref, key_ref, value_ref, qmask_ref, fold_ref, kept_ref, sent_ref
):
    groups, slots, _ = key_ref.shape
    half_heads = kept_ref.shape[0]
    heads = 2 * half_heads
    count = kept_ref.shape[1] // groups
    core = offset_ref[1]
    scale_factor = HD ** (-0.5)
    qmask = qmask_ref[...]
    qmask_float = qmask.astype(jnp.float32)
    fold = fold_ref[...]
    position = offset_ref[0] + lax.broadcasted_iota(jnp.int32, (1, slots), 1)
    lane = lax.broadcasted_iota(jnp.int32, (heads * count, LANES), 1)
    for r in range(groups):
        queries = query_ref[r]
        query_rows = jnp.concatenate([queries] * heads, axis=0) * qmask
        scores = lax.dot_general(
            query_rows, key_ref[r], (((1,), (1,)), ((), ())), preferred_element_type=jnp.float32
        ) * scale_factor
        live = position < length_ref[r]
        masked = jnp.where(live, scores, negative_fill)
        peak = jnp.max(masked, axis=1, keepdims=True)
        weights = jnp.where(live, jnp.exp(masked - peak), 0.0)
        total = jnp.sum(weights, axis=1, keepdims=True)
        value_rows = jnp.dot(
            weights.astype(jnp.bfloat16), value_ref[r], preferred_element_type=jnp.float32
        )
        folded = folded_rows(value_rows, peak, total, qmask_float, fold, lane)
        for h in range(heads):
            block = folded[h * count:(h + 1) * count, :]
            rows_here = pl.ds(r * count, count)

            @pl.when(core == h // half_heads)
            def _():
                kept_ref[h % half_heads, rows_here, :] = block

            @pl.when(core != h // half_heads)
            def _():
                sent_ref[h % half_heads, rows_here, :] = block


def new_partial_kernel(query_ref, kv_ref, qmask_ref, fold_ref, out_ref):
    groups, count, width = query_ref.shape
    heads = out_ref.shape[0]
    scale_factor = HD ** (-0.5)
    qmask = qmask_ref[...]
    qmask_float = qmask.astype(jnp.float32)
    fold = fold_ref[...]
    lane = lax.broadcasted_iota(jnp.int32, (heads * count, LANES), 1)
    patch = lax.broadcasted_iota(jnp.int32, (heads * count, 1), 0) & (count - 1)
    for r in range(groups):
        queries = query_ref[r]
        query_float = (jnp.concatenate([queries] * heads, axis=0) * qmask).astype(jnp.float32)
        pair = kv_ref[r]
        keys_new = pair[:, :width].astype(jnp.float32)
        values_new = pair[:, width:].astype(jnp.float32)
        new_scores = []
        for u in range(count):
            score = jnp.sum(query_float * keys_new[u:u + 1, :], axis=1, keepdims=True) * scale_factor
            new_scores.append(jnp.where(patch >= u, score, negative_fill))
        new_peak = new_scores[0]
        for score in new_scores[1:]:
            new_peak = jnp.maximum(new_peak, score)
        new_total = jnp.zeros_like(new_peak)
        new_rows = jnp.zeros((heads * count, width), jnp.float32)
        for u in range(count):
            weight = jnp.where(patch >= u, jnp.exp(new_scores[u] - new_peak), 0.0)
            new_total = new_total + weight
            weight = weight.astype(jnp.bfloat16).astype(jnp.float32)
            new_rows = new_rows + weight * values_new[u:u + 1, :]
        folded_store(out_ref, r, new_rows, new_peak, new_total, qmask_float, fold, lane)


def head_constants(count, width):
    row_head = np.arange(HEADS * count)[:, None] // count
    col_head = np.arange(width)[None, :] // HD
    qmask = jnp.asarray((row_head == col_head).astype(np.float32), dtype=jnp.bfloat16)
    fold = jnp.asarray((np.arange(width)[:, None] % HD == np.arange(LANES)[None, :]).astype(np.float32))
    return qmask, fold


def cache_partials(offset, cache_len, query_rows, key_cache, value_cache):
    groups, _, width = key_cache.shape
    count = query_rows.shape[1]
    rows = groups * count
    qmask, fold = head_constants(count, width)
    smem = pl.BlockSpec(memory_space=pltpu.SMEM)
    vmem = pl.BlockSpec(memory_space=pltpu.VMEM)
    half = jax.ShapeDtypeStruct((HEADS // 2, rows, LANES), jnp.float32)
    return pl.pallas_call(
        cache_partial_kernel,
        out_shape=(half, half),
        in_specs=[smem, smem, vmem, vmem, vmem, vmem, vmem],
        out_specs=(vmem, vmem),
    )(offset, cache_len, query_rows, key_cache, value_cache, qmask, fold)


def new_partials(query_rows, kv_rows):
    groups, count, width = query_rows.shape
    rows = groups * count
    qmask, fold = head_constants(count, width)
    vmem = pl.BlockSpec(memory_space=pltpu.VMEM)
    return pl.pallas_call(
        new_partial_kernel,
        out_shape=jax.ShapeDtypeStruct((HEADS, rows, LANES), jnp.float32),
        in_specs=[vmem, vmem, vmem, vmem],
        out_specs=vmem,
    )(query_rows, kv_rows, qmask, fold)


def tail_kernel(low_ref, high_ref, new_ref, patch_ref, w_out_ref, gain_ref, w_up_ref, w_down_ref, out_ref):
    half_heads, rows, _ = low_ref.shape
    width = w_out_ref.shape[0]
    out_sum = jnp.zeros((rows, width), jnp.float32)
    for h in range(2 * half_heads):
        source = low_ref if h < half_heads else high_ref
        first = source[h % half_heads]
        second = new_ref[h]
        m1 = first[:, HD:HD + 1]
        m2 = second[:, HD:HD + 1]
        m = jnp.maximum(m1, m2)
        merged = first * jnp.exp(m1 - m) + second * jnp.exp(m2 - m)
        attended = (merged / merged[:, HD + 1:HD + 2]).astype(jnp.bfloat16)
        out_sum = out_sum + jnp.dot(
            attended[:, :HD], w_out_ref[pl.ds(h * HD, HD), :], preferred_element_type=jnp.float32
        )
    out_rows = out_sum.astype(jnp.bfloat16).astype(jnp.float32)
    groups, count, _ = patch_ref.shape
    patch_rows = jnp.concatenate([patch_ref[r].astype(jnp.float32) for r in range(groups)], axis=0)
    mixed_rows = patch_rows + out_rows
    normed_mixed = rms_norm(mixed_rows, gain_ref[...]).astype(jnp.bfloat16)
    up_rows = jnp.dot(normed_mixed, w_up_ref[...], preferred_element_type=jnp.float32).astype(jnp.bfloat16)
    up_float = up_rows.astype(jnp.float32)
    hidden = (up_float / (1.0 + jnp.exp(-up_float))).astype(jnp.bfloat16)
    down_rows = jnp.dot(hidden, w_down_ref[...], preferred_element_type=jnp.float32).astype(jnp.bfloat16)
    decoded = mixed_rows + down_rows.astype(jnp.float32)
    for r in range(groups):
        out_ref[r] = decoded[r * count:(r + 1) * count, :].astype(out_ref.dtype)


def tail(low_half, high_half, new_packed, patches, w_out, ffn_gain, w_up, w_down):
    width = patches.shape[-1]
    vmem = pl.BlockSpec(memory_space=pltpu.VMEM)
    return pl.pallas_call(
        tail_kernel,
        out_shape=jax.ShapeDtypeStruct(patches.shape, jnp.bfloat16),
        in_specs=[vmem] * 8,
        out_specs=vmem,
    )(low_half, high_half, new_packed, patches, w_out, ffn_gain.reshape(1, width), w_up, w_down)


def layer(
    patches, key_cache, value_cache, cache_len, attn_gain, w_qkv, w_out, ffn_gain, w_up, w_down
):
    _, _, model_width = patches.shape
    slots_here = key_cache.shape[1]
    seq_count = lax.axis_size("seq")
    normed = rms_norm(patches.astype(jnp.float32), attn_gain).astype(jnp.bfloat16)
    query_rows = project(normed, w_qkv[:, :model_width])
    me = lax.axis_index("seq")
    offset = jnp.stack([me * slots_here, me % 2]).astype(jnp.int32)
    kept, sent = cache_partials(offset, cache_len, query_rows, key_cache, value_cache)
    kv_rows = project(normed, w_qkv[:, model_width:])
    new_packed = new_partials(query_rows, kv_rows)
    low_half, high_half = combine_over_seq(kept, sent, seq_count)
    return tail(low_half, high_half, new_packed, patches, w_out, ffn_gain, w_up, w_down)


def solution(mesh):
    placed = (
        P("req", None, None),
        P("req", "seq", None),
        P("req", "seq", None),
        P("req"),
        P(),
        P(),
        P(),
        P(),
        P(),
        P(),
    )
    return jax.shard_map(layer, mesh=mesh, in_specs=placed, out_specs=P("req", None, None), check_vma=False)
```

```python
import numpy as np
import jax
import jax.numpy as jnp
from jax import lax
from jax.sharding import PartitionSpec as P
from jax.experimental.layout import Layout, with_layout_constraint
from jax.experimental import pallas as pl
from jax.experimental.pallas import tpu as pltpu

HEADS = 16
HD = 80


epsilon = 1e-06
negative_fill = -1e30


def rms_norm(values, gain):
    return values * lax.rsqrt(jnp.mean(values * values, axis=-1, keepdims=True) + epsilon) * gain


def project(token_rows, weight):
    return jnp.dot(token_rows, weight, preferred_element_type=jnp.float32).astype(jnp.bfloat16)


LANES = 128


def merge(first, second):
    m1 = first[..., HD:HD + 1]
    m2 = second[..., HD:HD + 1]
    m = jnp.maximum(m1, m2)
    a1 = jnp.exp(m1 - m)
    a2 = jnp.exp(m2 - m)
    merged = first * a1 + second * a2
    lane = lax.broadcasted_iota(jnp.int32, merged.shape, merged.ndim - 1)
    return jnp.where(lane == HD, m, merged)


def exchange(part, distance, count):
    pairs = [(i, i ^ distance) for i in range(count)]
    row_major = Layout(major_to_minor=(0, 1))
    part = with_layout_constraint(part, row_major)
    return with_layout_constraint(lax.ppermute(part, "seq", pairs), row_major)


def combine_over_seq(kept, sent, count):
    half_heads, rows, lanes = kept.shape
    me = lax.axis_index("seq")
    core = me % 2
    kept = kept.reshape(half_heads * rows, lanes)
    sent = sent.reshape(half_heads * rows, lanes)
    got = exchange(sent, 1, count)
    low_first = core == 0
    state = merge(jnp.where(low_first, kept, got), jnp.where(low_first, got, kept))
    distance = 2
    while distance < count:
        got = exchange(state, distance, count)
        low_first = (me // distance) % 2 == 0
        state = merge(jnp.where(low_first, state, got), jnp.where(low_first, got, state))
        distance *= 2
    other = exchange(state, 1, count)
    low_half = jnp.where(core == 0, state, other)
    high_half = jnp.where(core == 0, other, state)
    return low_half.reshape(half_heads, rows, lanes), high_half.reshape(half_heads, rows, lanes)


def folded_rows(rows, peak, total, qmask_float, fold, lane):
    own = rows * qmask_float
    high = own.astype(jnp.bfloat16)
    rest = own - high.astype(jnp.float32)
    middle = rest.astype(jnp.bfloat16)
    low = (rest - middle.astype(jnp.float32)).astype(jnp.bfloat16)
    folded = (
        jnp.dot(high, fold, preferred_element_type=jnp.float32)
        + jnp.dot(middle, fold, preferred_element_type=jnp.float32)
    ) + jnp.dot(low, fold, preferred_element_type=jnp.float32)
    return jnp.where(lane == HD, peak, jnp.where(lane == HD + 1, total, folded))


def folded_store(target, r, rows, peak, total, qmask_float, fold, lane):
    heads = target.shape[0]
    count = rows.shape[0] // heads
    folded = folded_rows(rows, peak, total, qmask_float, fold, lane)
    for h in range(heads):
        target[h, pl.ds(r * count, count), :] = folded[h * count:(h + 1) * count, :]


def cache_partial_kernel(
    offset_ref, length_ref, query_ref, key_ref, value_ref, qmask_ref, fold_ref, kept_ref, sent_ref
):
    groups, slots, _ = key_ref.shape
    half_heads = kept_ref.shape[0]
    heads = 2 * half_heads
    count = kept_ref.shape[1] // groups
    core = offset_ref[1]
    scale_factor = HD ** (-0.5)
    qmask = qmask_ref[core]
    qmask_float = qmask.astype(jnp.float32)
    fold = fold_ref[...]
    position = offset_ref[0] + lax.broadcasted_iota(jnp.int32, (1, slots), 1)
    lane = lax.broadcasted_iota(jnp.int32, (heads * count, LANES), 1)
    for r in range(groups):
        queries = query_ref[r]
        query_rows = jnp.concatenate([queries] * heads, axis=0) * qmask
        scores = lax.dot_general(
            query_rows, key_ref[r], (((1,), (1,)), ((), ())), preferred_element_type=jnp.float32
        ) * scale_factor
        live = position < length_ref[r]
        masked = jnp.where(live, scores, negative_fill)
        peak = jnp.max(masked, axis=1, keepdims=True)
        weights = jnp.where(live, jnp.exp(masked - peak), 0.0)
        total = jnp.sum(weights, axis=1, keepdims=True)
        value_rows = jnp.dot(
            weights.astype(jnp.bfloat16), value_ref[r], preferred_element_type=jnp.float32
        )
        folded = folded_rows(value_rows, peak, total, qmask_float, fold, lane)
        for h in range(heads):
            target = kept_ref if h < half_heads else sent_ref
            target[h % half_heads, pl.ds(r * count, count), :] = folded[h * count:(h + 1) * count, :]


def new_partial_kernel(query_ref, kv_ref, qmask_ref, fold_ref, out_ref):
    groups, count, width = query_ref.shape
    heads = out_ref.shape[0]
    scale_factor = HD ** (-0.5)
    qmask = qmask_ref[...]
    qmask_float = qmask.astype(jnp.float32)
    fold = fold_ref[...]
    lane = lax.broadcasted_iota(jnp.int32, (heads * count, LANES), 1)
    patch = lax.broadcasted_iota(jnp.int32, (heads * count, 1), 0) & (count - 1)
    for r in range(groups):
        queries = query_ref[r]
        query_float = (jnp.concatenate([queries] * heads, axis=0) * qmask).astype(jnp.float32)
        pair = kv_ref[r]
        keys_new = pair[:, :width].astype(jnp.float32)
        values_new = pair[:, width:].astype(jnp.float32)
        new_scores = []
        for u in range(count):
            score = jnp.sum(query_float * keys_new[u:u + 1, :], axis=1, keepdims=True) * scale_factor
            new_scores.append(jnp.where(patch >= u, score, negative_fill))
        new_peak = new_scores[0]
        for score in new_scores[1:]:
            new_peak = jnp.maximum(new_peak, score)
        new_total = jnp.zeros_like(new_peak)
        new_rows = jnp.zeros((heads * count, width), jnp.float32)
        for u in range(count):
            weight = jnp.where(patch >= u, jnp.exp(new_scores[u] - new_peak), 0.0)
            new_total = new_total + weight
            weight = weight.astype(jnp.bfloat16).astype(jnp.float32)
            new_rows = new_rows + weight * values_new[u:u + 1, :]
        folded_store(out_ref, r, new_rows, new_peak, new_total, qmask_float, fold, lane)


def head_constants(count, width):
    row_head = np.arange(HEADS * count)[:, None] // count
    col_head = np.arange(width)[None, :] // HD
    qmask = jnp.asarray((row_head == col_head).astype(np.float32), dtype=jnp.bfloat16)
    fold = jnp.asarray(
        (np.arange(width)[:, None] % HD == np.arange(LANES)[None, :]).astype(np.float32), dtype=jnp.bfloat16
    )
    return qmask, fold


def ordered_masks(count, width):
    masks = []
    for core in range(2):
        row_head = (np.arange(HEADS * count)[:, None] // count + core * (HEADS // 2)) % HEADS
        col_head = np.arange(width)[None, :] // HD
        masks.append((row_head == col_head).astype(np.float32))
    return jnp.asarray(np.stack(masks), dtype=jnp.bfloat16)


def cache_partials(offset, cache_len, query_rows, key_cache, value_cache):
    groups, _, width = key_cache.shape
    count = query_rows.shape[1]
    rows = groups * count
    _, fold = head_constants(count, width)
    qmask = ordered_masks(count, width)
    smem = pl.BlockSpec(memory_space=pltpu.SMEM)
    vmem = pl.BlockSpec(memory_space=pltpu.VMEM)
    half = jax.ShapeDtypeStruct((HEADS // 2, rows, LANES), jnp.float32)
    return pl.pallas_call(
        cache_partial_kernel,
        out_shape=(half, half),
        in_specs=[smem, smem, vmem, vmem, vmem, vmem, vmem],
        out_specs=(vmem, vmem),
    )(offset, cache_len, query_rows, key_cache, value_cache, qmask, fold)


def new_partials(query_rows, kv_rows):
    groups, count, width = query_rows.shape
    rows = groups * count
    qmask, fold = head_constants(count, width)
    vmem = pl.BlockSpec(memory_space=pltpu.VMEM)
    return pl.pallas_call(
        new_partial_kernel,
        out_shape=jax.ShapeDtypeStruct((HEADS, rows, LANES), jnp.float32),
        in_specs=[vmem, vmem, vmem, vmem],
        out_specs=vmem,
    )(query_rows, kv_rows, qmask, fold)


def tail_kernel(low_ref, high_ref, new_ref, patch_ref, w_out_ref, gain_ref, w_up_ref, w_down_ref, out_ref):
    half_heads, rows, _ = low_ref.shape
    width = w_out_ref.shape[0]
    out_sum = jnp.zeros((rows, width), jnp.float32)
    for h in range(2 * half_heads):
        source = low_ref if h < half_heads else high_ref
        first = source[h % half_heads]
        second = new_ref[h]
        m1 = first[:, HD:HD + 1]
        m2 = second[:, HD:HD + 1]
        m = jnp.maximum(m1, m2)
        merged = first * jnp.exp(m1 - m) + second * jnp.exp(m2 - m)
        attended = (merged / merged[:, HD + 1:HD + 2]).astype(jnp.bfloat16)
        out_sum = out_sum + jnp.dot(
            attended[:, :HD], w_out_ref[pl.ds(h * HD, HD), :], preferred_element_type=jnp.float32
        )
    out_rows = out_sum.astype(jnp.bfloat16).astype(jnp.float32)
    groups, count, _ = patch_ref.shape
    patch_rows = jnp.concatenate([patch_ref[r].astype(jnp.float32) for r in range(groups)], axis=0)
    mixed_rows = patch_rows + out_rows
    normed_mixed = rms_norm(mixed_rows, gain_ref[...]).astype(jnp.bfloat16)
    up_rows = jnp.dot(normed_mixed, w_up_ref[...], preferred_element_type=jnp.float32).astype(jnp.bfloat16)
    up_float = up_rows.astype(jnp.float32)
    hidden = (up_float / (1.0 + jnp.exp(-up_float))).astype(jnp.bfloat16)
    down_rows = jnp.dot(hidden, w_down_ref[...], preferred_element_type=jnp.float32).astype(jnp.bfloat16)
    decoded = mixed_rows + down_rows.astype(jnp.float32)
    for r in range(groups):
        out_ref[r] = decoded[r * count:(r + 1) * count, :].astype(out_ref.dtype)


def tail(low_half, high_half, new_packed, patches, w_out, ffn_gain, w_up, w_down):
    width = patches.shape[-1]
    vmem = pl.BlockSpec(memory_space=pltpu.VMEM)
    return pl.pallas_call(
        tail_kernel,
        out_shape=jax.ShapeDtypeStruct(patches.shape, jnp.bfloat16),
        in_specs=[vmem] * 8,
        out_specs=vmem,
    )(low_half, high_half, new_packed, patches, w_out, ffn_gain.reshape(1, width), w_up, w_down)


def layer(
    patches, key_cache, value_cache, cache_len, attn_gain, w_qkv, w_out, ffn_gain, w_up, w_down
):
    _, _, model_width = patches.shape
    slots_here = key_cache.shape[1]
    seq_count = lax.axis_size("seq")
    normed = rms_norm(patches.astype(jnp.float32), attn_gain).astype(jnp.bfloat16)
    query_rows = project(normed, w_qkv[:, :model_width])
    me = lax.axis_index("seq")
    offset = jnp.stack([me * slots_here, me % 2]).astype(jnp.int32)
    kept, sent = cache_partials(offset, cache_len, query_rows, key_cache, value_cache)
    kv_rows = project(normed, w_qkv[:, model_width:])
    new_packed = new_partials(query_rows, kv_rows)
    low_half, high_half = combine_over_seq(kept, sent, seq_count)
    return tail(low_half, high_half, new_packed, patches, w_out, ffn_gain, w_up, w_down)


def solution(mesh):
    placed = (
        P("req", None, None),
        P("req", "seq", None),
        P("req", "seq", None),
        P("req"),
        P(),
        P(),
        P(),
        P(),
        P(),
        P(),
    )
    return jax.shard_map(layer, mesh=mesh, in_specs=placed, out_specs=P("req", None, None), check_vma=False)
```

```python
import numpy as np
import jax
import jax.numpy as jnp
from jax import lax
from jax.sharding import PartitionSpec as P
from jax.experimental.layout import Layout, with_layout_constraint
from jax.experimental import pallas as pl
from jax.experimental.pallas import tpu as pltpu

HEADS = 16
HD = 80


epsilon = 1e-06
negative_fill = -1e30


def rms_norm(values, gain):
    return values * lax.rsqrt(jnp.mean(values * values, axis=-1, keepdims=True) + epsilon) * gain


LANES = 128


def merge(first, second):
    m1 = first[..., HD:HD + 1]
    m2 = second[..., HD:HD + 1]
    m = jnp.maximum(m1, m2)
    a1 = jnp.exp(m1 - m)
    a2 = jnp.exp(m2 - m)
    merged = first * a1 + second * a2
    lane = lax.broadcasted_iota(jnp.int32, merged.shape, merged.ndim - 1)
    return jnp.where(lane == HD, m, merged)


def exchange(part, distance, count):
    pairs = [(i, i ^ distance) for i in range(count)]
    row_major = Layout(major_to_minor=(0, 1))
    part = with_layout_constraint(part, row_major)
    return with_layout_constraint(lax.ppermute(part, "seq", pairs), row_major)


def combine_over_seq(kept, sent, count):
    half_heads, rows, lanes = kept.shape
    me = lax.axis_index("seq")
    core = me % 2
    kept = kept.reshape(half_heads * rows, lanes)
    sent = sent.reshape(half_heads * rows, lanes)
    got = exchange(sent, 1, count)
    low_first = core == 0
    state = merge(jnp.where(low_first, kept, got), jnp.where(low_first, got, kept))
    distance = 2
    while distance < count:
        got = exchange(state, distance, count)
        low_first = (me // distance) % 2 == 0
        state = merge(jnp.where(low_first, state, got), jnp.where(low_first, got, state))
        distance *= 2
    other = exchange(state, 1, count)
    low_half = jnp.where(core == 0, state, other)
    high_half = jnp.where(core == 0, other, state)
    return low_half.reshape(half_heads, rows, lanes), high_half.reshape(half_heads, rows, lanes)


def folded_rows(rows, peak, total, qmask_float, fold, lane):
    own = rows * qmask_float
    high = own.astype(jnp.bfloat16)
    rest = own - high.astype(jnp.float32)
    middle = rest.astype(jnp.bfloat16)
    low = (rest - middle.astype(jnp.float32)).astype(jnp.bfloat16)
    folded = (
        jnp.dot(high, fold, preferred_element_type=jnp.float32)
        + jnp.dot(middle, fold, preferred_element_type=jnp.float32)
    ) + jnp.dot(low, fold, preferred_element_type=jnp.float32)
    return jnp.where(lane == HD, peak, jnp.where(lane == HD + 1, total, folded))


def folded_store(target, r, rows, peak, total, qmask_float, fold, lane):
    heads = target.shape[0]
    count = rows.shape[0] // heads
    folded = folded_rows(rows, peak, total, qmask_float, fold, lane)
    for h in range(heads):
        target[h, pl.ds(r * count, count), :] = folded[h * count:(h + 1) * count, :]


def normed_rows(patch_ref, gain_ref):
    groups = patch_ref.shape[0]
    rows = jnp.concatenate([patch_ref[r].astype(jnp.float32) for r in range(groups)], axis=0)
    return rms_norm(rows, gain_ref[...]).astype(jnp.bfloat16)


def cache_partial_kernel(
    length_ref, patch_ref, gain_ref, wq_ref, key_ref, value_ref, qmask_ref, fold_ref, kept_ref, sent_ref, query_ref
):
    groups, slots, _ = key_ref.shape
    half_heads = kept_ref.shape[0]
    heads = 2 * half_heads
    count = kept_ref.shape[1] // groups
    me = lax.axis_index("seq")
    core = me % 2
    query_float = jnp.dot(normed_rows(patch_ref, gain_ref), wq_ref[...], preferred_element_type=jnp.float32)
    for r in range(groups):
        query_ref[r] = query_float[r * count:(r + 1) * count, :].astype(query_ref.dtype)
    scale_factor = HD ** (-0.5)
    qmask = qmask_ref[core]
    qmask_float = qmask.astype(jnp.float32)
    fold = fold_ref[...]
    position = me * slots + lax.broadcasted_iota(jnp.int32, (1, slots), 1)
    lane = lax.broadcasted_iota(jnp.int32, (heads * count, LANES), 1)
    for r in range(groups):
        queries = query_ref[r]
        query_rows = jnp.concatenate([queries] * heads, axis=0) * qmask
        scores = lax.dot_general(
            query_rows, key_ref[r], (((1,), (1,)), ((), ())), preferred_element_type=jnp.float32
        ) * scale_factor
        live = position < length_ref[r]
        masked = jnp.where(live, scores, negative_fill)
        peak = jnp.max(masked, axis=1, keepdims=True)
        weights = jnp.where(live, jnp.exp(masked - peak), 0.0)
        total = jnp.sum(weights, axis=1, keepdims=True)
        value_rows = jnp.dot(
            weights.astype(jnp.bfloat16), value_ref[r], preferred_element_type=jnp.float32
        )
        folded = folded_rows(value_rows, peak, total, qmask_float, fold, lane)
        for h in range(heads):
            target = kept_ref if h < half_heads else sent_ref
            target[h % half_heads, pl.ds(r * count, count), :] = folded[h * count:(h + 1) * count, :]


def new_partial_kernel(patch_ref, gain_ref, wk_ref, wv_ref, query_ref, qmask_ref, fold_ref, out_ref):
    groups, count, width = query_ref.shape
    heads = out_ref.shape[0]
    normed = normed_rows(patch_ref, gain_ref)
    keys_all = jnp.dot(normed, wk_ref[...], preferred_element_type=jnp.float32).astype(jnp.bfloat16)
    values_all = jnp.dot(normed, wv_ref[...], preferred_element_type=jnp.float32).astype(jnp.bfloat16)
    scale_factor = HD ** (-0.5)
    qmask = qmask_ref[...]
    qmask_float = qmask.astype(jnp.float32)
    fold = fold_ref[...]
    lane = lax.broadcasted_iota(jnp.int32, (heads * count, LANES), 1)
    patch = lax.broadcasted_iota(jnp.int32, (heads * count, 1), 0) & (count - 1)
    for r in range(groups):
        queries = query_ref[r]
        query_float = (jnp.concatenate([queries] * heads, axis=0) * qmask).astype(jnp.float32)
        keys_new = keys_all.astype(jnp.float32)[r * count:(r + 1) * count, :]
        values_new = values_all.astype(jnp.float32)[r * count:(r + 1) * count, :]
        new_scores = []
        for u in range(count):
            score = jnp.sum(query_float * keys_new[u:u + 1, :], axis=1, keepdims=True) * scale_factor
            new_scores.append(jnp.where(patch >= u, score, negative_fill))
        new_peak = new_scores[0]
        for score in new_scores[1:]:
            new_peak = jnp.maximum(new_peak, score)
        new_total = jnp.zeros_like(new_peak)
        new_rows = jnp.zeros((heads * count, width), jnp.float32)
        for u in range(count):
            weight = jnp.where(patch >= u, jnp.exp(new_scores[u] - new_peak), 0.0)
            new_total = new_total + weight
            weight = weight.astype(jnp.bfloat16).astype(jnp.float32)
            new_rows = new_rows + weight * values_new[u:u + 1, :]
        folded_store(out_ref, r, new_rows, new_peak, new_total, qmask_float, fold, lane)


def head_constants(count, width):
    row_head = np.arange(HEADS * count)[:, None] // count
    col_head = np.arange(width)[None, :] // HD
    qmask = jnp.asarray((row_head == col_head).astype(np.float32), dtype=jnp.bfloat16)
    fold = jnp.asarray(
        (np.arange(width)[:, None] % HD == np.arange(LANES)[None, :]).astype(np.float32), dtype=jnp.bfloat16
    )
    return qmask, fold


def ordered_masks(count, width):
    masks = []
    for core in range(2):
        row_head = (np.arange(HEADS * count)[:, None] // count + core * (HEADS // 2)) % HEADS
        col_head = np.arange(width)[None, :] // HD
        masks.append((row_head == col_head).astype(np.float32))
    return jnp.asarray(np.stack(masks), dtype=jnp.bfloat16)


def cache_partials(cache_len, patches, attn_gain, w_qkv, key_cache, value_cache):
    groups, _, width = key_cache.shape
    count = patches.shape[1]
    rows = groups * count
    _, fold = head_constants(count, width)
    qmask = ordered_masks(count, width)
    smem = pl.BlockSpec(memory_space=pltpu.SMEM)
    vmem = pl.BlockSpec(memory_space=pltpu.VMEM)
    query_block = pl.BlockSpec((width, width), lambda i: (0, 0))
    half = jax.ShapeDtypeStruct((HEADS // 2, rows, LANES), jnp.float32)
    return pl.pallas_call(
        cache_partial_kernel,
        grid=(1,),
        out_shape=(half, half, jax.ShapeDtypeStruct(patches.shape, jnp.bfloat16)),
        in_specs=[smem, vmem, vmem, query_block, vmem, vmem, vmem, vmem],
        out_specs=(vmem, vmem, vmem),
    )(cache_len, patches, attn_gain.reshape(1, width), w_qkv, key_cache, value_cache, qmask, fold)


def new_partials(patches, attn_gain, w_qkv, query_rows):
    groups, count, width = query_rows.shape
    rows = groups * count
    qmask, fold = head_constants(count, width)
    vmem = pl.BlockSpec(memory_space=pltpu.VMEM)
    key_block = pl.BlockSpec((width, width), lambda i: (0, 1))
    value_block = pl.BlockSpec((width, width), lambda i: (0, 2))
    return pl.pallas_call(
        new_partial_kernel,
        grid=(1,),
        out_shape=jax.ShapeDtypeStruct((HEADS, rows, LANES), jnp.float32),
        in_specs=[vmem, vmem, key_block, value_block, vmem, vmem, vmem],
        out_specs=vmem,
    )(patches, attn_gain.reshape(1, width), w_qkv, w_qkv, query_rows, qmask, fold)


def tail_kernel(low_ref, high_ref, new_ref, patch_ref, w_out_ref, gain_ref, w_up_ref, w_down_ref, out_ref):
    half_heads, rows, _ = low_ref.shape
    width = w_out_ref.shape[0]
    out_sum = jnp.zeros((rows, width), jnp.float32)
    for h in range(2 * half_heads):
        source = low_ref if h < half_heads else high_ref
        first = source[h % half_heads]
        second = new_ref[h]
        m1 = first[:, HD:HD + 1]
        m2 = second[:, HD:HD + 1]
        m = jnp.maximum(m1, m2)
        merged = first * jnp.exp(m1 - m) + second * jnp.exp(m2 - m)
        attended = (merged / merged[:, HD + 1:HD + 2]).astype(jnp.bfloat16)
        out_sum = out_sum + jnp.dot(
            attended[:, :HD], w_out_ref[pl.ds(h * HD, HD), :], preferred_element_type=jnp.float32
        )
    out_rows = out_sum.astype(jnp.bfloat16).astype(jnp.float32)
    groups, count, _ = patch_ref.shape
    patch_rows = jnp.concatenate([patch_ref[r].astype(jnp.float32) for r in range(groups)], axis=0)
    mixed_rows = patch_rows + out_rows
    normed_mixed = rms_norm(mixed_rows, gain_ref[...]).astype(jnp.bfloat16)
    up_rows = jnp.dot(normed_mixed, w_up_ref[...], preferred_element_type=jnp.float32).astype(jnp.bfloat16)
    up_float = up_rows.astype(jnp.float32)
    hidden = (up_float / (1.0 + jnp.exp(-up_float))).astype(jnp.bfloat16)
    down_rows = jnp.dot(hidden, w_down_ref[...], preferred_element_type=jnp.float32).astype(jnp.bfloat16)
    decoded = mixed_rows + down_rows.astype(jnp.float32)
    for r in range(groups):
        out_ref[r] = decoded[r * count:(r + 1) * count, :].astype(out_ref.dtype)


def tail(low_half, high_half, new_packed, patches, w_out, ffn_gain, w_up, w_down):
    width = patches.shape[-1]
    vmem = pl.BlockSpec(memory_space=pltpu.VMEM)
    return pl.pallas_call(
        tail_kernel,
        out_shape=jax.ShapeDtypeStruct(patches.shape, jnp.bfloat16),
        in_specs=[vmem] * 8,
        out_specs=vmem,
    )(low_half, high_half, new_packed, patches, w_out, ffn_gain.reshape(1, width), w_up, w_down)


def layer(
    patches, key_cache, value_cache, cache_len, attn_gain, w_qkv, w_out, ffn_gain, w_up, w_down
):
    seq_count = lax.axis_size("seq")
    kept, sent, query_rows = cache_partials(cache_len, patches, attn_gain, w_qkv, key_cache, value_cache)
    new_packed = new_partials(patches, attn_gain, w_qkv, query_rows)
    low_half, high_half = combine_over_seq(kept, sent, seq_count)
    return tail(low_half, high_half, new_packed, patches, w_out, ffn_gain, w_up, w_down)


def solution(mesh):
    placed = (
        P("req", None, None),
        P("req", "seq", None),
        P("req", "seq", None),
        P("req"),
        P(),
        P(),
        P(),
        P(),
        P(),
        P(),
    )
    return jax.shard_map(layer, mesh=mesh, in_specs=placed, out_specs=P("req", None, None), check_vma=False)
```

```python
import numpy as np
import jax
import jax.numpy as jnp
from jax import lax
from jax.sharding import PartitionSpec as P
from jax.experimental.layout import Layout, with_layout_constraint
from jax.experimental import pallas as pl
from jax.experimental.pallas import tpu as pltpu

HEADS = 16
HD = 80


epsilon = 1e-06
negative_fill = -1e30


def rms_norm(values, gain):
    return values * lax.rsqrt(jnp.mean(values * values, axis=-1, keepdims=True) + epsilon) * gain


LANES = 128


def merge(first, second):
    m1 = first[..., HD:HD + 1]
    m2 = second[..., HD:HD + 1]
    m = jnp.maximum(m1, m2)
    a1 = jnp.exp(m1 - m)
    a2 = jnp.exp(m2 - m)
    merged = first * a1 + second * a2
    lane = lax.broadcasted_iota(jnp.int32, merged.shape, merged.ndim - 1)
    return jnp.where(lane == HD, m, merged)


def exchange(part, distance, count):
    pairs = [(i, i ^ distance) for i in range(count)]
    row_major = Layout(major_to_minor=(0, 1))
    part = with_layout_constraint(part, row_major)
    return with_layout_constraint(lax.ppermute(part, "seq", pairs), row_major)


def combine_over_seq(kept, sent, count):
    half_heads, rows, lanes = kept.shape
    me = lax.axis_index("seq")
    core = me % 2
    kept = kept.reshape(half_heads * rows, lanes)
    sent = sent.reshape(half_heads * rows, lanes)
    got = exchange(sent, 1, count)
    low_first = core == 0
    state = merge(jnp.where(low_first, kept, got), jnp.where(low_first, got, kept))
    distance = 2
    while distance < count:
        got = exchange(state, distance, count)
        low_first = (me // distance) % 2 == 0
        state = merge(jnp.where(low_first, state, got), jnp.where(low_first, got, state))
        distance *= 2
    other = exchange(state, 1, count)
    low_half = jnp.where(core == 0, state, other)
    high_half = jnp.where(core == 0, other, state)
    return low_half.reshape(half_heads, rows, lanes), high_half.reshape(half_heads, rows, lanes)


def folded_rows(rows, peak, total, qmask_float, fold, lane):
    own = rows * qmask_float
    high = own.astype(jnp.bfloat16)
    rest = own - high.astype(jnp.float32)
    middle = rest.astype(jnp.bfloat16)
    low = (rest - middle.astype(jnp.float32)).astype(jnp.bfloat16)
    folded = (
        jnp.dot(high, fold, preferred_element_type=jnp.float32)
        + jnp.dot(middle, fold, preferred_element_type=jnp.float32)
    ) + jnp.dot(low, fold, preferred_element_type=jnp.float32)
    return jnp.where(lane == HD, peak, jnp.where(lane == HD + 1, total, folded))


def folded_store(target, r, rows, peak, total, qmask_float, fold, lane):
    heads = target.shape[0]
    count = rows.shape[0] // heads
    folded = folded_rows(rows, peak, total, qmask_float, fold, lane)
    for h in range(heads):
        target[h, pl.ds(r * count, count), :] = folded[h * count:(h + 1) * count, :]


def normed_rows(patch_ref, gain_ref):
    groups = patch_ref.shape[0]
    rows = jnp.concatenate([patch_ref[r].astype(jnp.float32) for r in range(groups)], axis=0)
    return rms_norm(rows, gain_ref[...]).astype(jnp.bfloat16)


def cache_partial_kernel(
    length_ref, patch_ref, gain_ref, wq_ref, key_ref, value_ref, qmask_ref, fold_ref, kept_ref, sent_ref, query_ref
):
    groups, slots, _ = key_ref.shape
    half_heads = kept_ref.shape[0]
    heads = 2 * half_heads
    count = kept_ref.shape[1] // groups
    me = lax.axis_index("seq")
    core = me % 2
    query_float = jnp.dot(normed_rows(patch_ref, gain_ref), wq_ref[...], preferred_element_type=jnp.float32)
    for r in range(groups):
        query_ref[r] = query_float[r * count:(r + 1) * count, :].astype(query_ref.dtype)
    scale_factor = HD ** (-0.5)
    qmask = qmask_ref[core]
    qmask_float = qmask.astype(jnp.float32)
    fold = fold_ref[...]
    position = me * slots + lax.broadcasted_iota(jnp.int32, (1, slots), 1)
    lane = lax.broadcasted_iota(jnp.int32, (heads * count, LANES), 1)
    for r in range(groups):
        queries = query_ref[r]
        query_rows = jnp.concatenate([queries] * heads, axis=0) * qmask
        scores = lax.dot_general(
            query_rows, key_ref[r], (((1,), (1,)), ((), ())), preferred_element_type=jnp.float32
        ) * scale_factor
        live = position < length_ref[r]
        masked = jnp.where(live, scores, negative_fill)
        peak = jnp.max(masked, axis=1, keepdims=True)
        weights = jnp.where(live, jnp.exp(masked - peak), 0.0)
        total = jnp.sum(weights, axis=1, keepdims=True)
        value_rows = jnp.dot(
            weights.astype(jnp.bfloat16), value_ref[r], preferred_element_type=jnp.float32
        )
        folded = folded_rows(value_rows, peak, total, qmask_float, fold, lane)
        for h in range(heads):
            target = kept_ref if h < half_heads else sent_ref
            target[h % half_heads, pl.ds(r * count, count), :] = folded[h * count:(h + 1) * count, :]


def kv_projection_kernel(patch_ref, gain_ref, wk_ref, wv_ref, key_ref, value_ref):
    normed = normed_rows(patch_ref, gain_ref)
    key_ref[...] = jnp.dot(normed, wk_ref[...], preferred_element_type=jnp.float32).astype(key_ref.dtype)
    value_ref[...] = jnp.dot(normed, wv_ref[...], preferred_element_type=jnp.float32).astype(value_ref.dtype)


def new_partial_kernel(query_ref, key_new_ref, value_new_ref, qmask_ref, fold_ref, out_ref):
    groups, count, width = query_ref.shape
    heads = out_ref.shape[0]
    keys_all = key_new_ref[...]
    values_all = value_new_ref[...]
    scale_factor = HD ** (-0.5)
    qmask = qmask_ref[...]
    qmask_float = qmask.astype(jnp.float32)
    fold = fold_ref[...]
    lane = lax.broadcasted_iota(jnp.int32, (heads * count, LANES), 1)
    patch = lax.broadcasted_iota(jnp.int32, (heads * count, 1), 0) & (count - 1)
    for r in range(groups):
        queries = query_ref[r]
        query_float = (jnp.concatenate([queries] * heads, axis=0) * qmask).astype(jnp.float32)
        keys_new = keys_all.astype(jnp.float32)[r * count:(r + 1) * count, :]
        values_new = values_all.astype(jnp.float32)[r * count:(r + 1) * count, :]
        new_scores = []
        for u in range(count):
            score = jnp.sum(query_float * keys_new[u:u + 1, :], axis=1, keepdims=True) * scale_factor
            new_scores.append(jnp.where(patch >= u, score, negative_fill))
        new_peak = new_scores[0]
        for score in new_scores[1:]:
            new_peak = jnp.maximum(new_peak, score)
        new_total = jnp.zeros_like(new_peak)
        new_rows = jnp.zeros((heads * count, width), jnp.float32)
        for u in range(count):
            weight = jnp.where(patch >= u, jnp.exp(new_scores[u] - new_peak), 0.0)
            new_total = new_total + weight
            weight = weight.astype(jnp.bfloat16).astype(jnp.float32)
            new_rows = new_rows + weight * values_new[u:u + 1, :]
        folded_store(out_ref, r, new_rows, new_peak, new_total, qmask_float, fold, lane)


def head_constants(count, width):
    row_head = np.arange(HEADS * count)[:, None] // count
    col_head = np.arange(width)[None, :] // HD
    qmask = jnp.asarray((row_head == col_head).astype(np.float32), dtype=jnp.bfloat16)
    fold = jnp.asarray(
        (np.arange(width)[:, None] % HD == np.arange(LANES)[None, :]).astype(np.float32), dtype=jnp.bfloat16
    )
    return qmask, fold


def ordered_masks(count, width):
    masks = []
    for core in range(2):
        row_head = (np.arange(HEADS * count)[:, None] // count + core * (HEADS // 2)) % HEADS
        col_head = np.arange(width)[None, :] // HD
        masks.append((row_head == col_head).astype(np.float32))
    return jnp.asarray(np.stack(masks), dtype=jnp.bfloat16)


def cache_partials(cache_len, patches, attn_gain, w_qkv, key_cache, value_cache):
    groups, _, width = key_cache.shape
    count = patches.shape[1]
    rows = groups * count
    _, fold = head_constants(count, width)
    qmask = ordered_masks(count, width)
    smem = pl.BlockSpec(memory_space=pltpu.SMEM)
    vmem = pl.BlockSpec(memory_space=pltpu.VMEM)
    query_block = pl.BlockSpec((width, width), lambda i: (0, 0))
    half = jax.ShapeDtypeStruct((HEADS // 2, rows, LANES), jnp.float32)
    return pl.pallas_call(
        cache_partial_kernel,
        grid=(1,),
        out_shape=(half, half, jax.ShapeDtypeStruct(patches.shape, jnp.bfloat16)),
        in_specs=[smem, vmem, vmem, query_block, vmem, vmem, vmem, vmem],
        out_specs=(vmem, vmem, vmem),
    )(cache_len, patches, attn_gain, w_qkv, key_cache, value_cache, qmask, fold)


def kv_projection(patches, attn_gain, w_qkv):
    groups, count, width = patches.shape
    vmem = pl.BlockSpec(memory_space=pltpu.VMEM)
    key_block = pl.BlockSpec((width, width), lambda i: (0, 1))
    value_block = pl.BlockSpec((width, width), lambda i: (0, 2))
    rows = jax.ShapeDtypeStruct((groups * count, width), jnp.bfloat16)
    return pl.pallas_call(
        kv_projection_kernel,
        grid=(1,),
        out_shape=(rows, rows),
        in_specs=[vmem, vmem, key_block, value_block],
        out_specs=(vmem, vmem),
    )(patches, attn_gain, w_qkv, w_qkv)


def new_partials(query_rows, keys_new, values_new):
    groups, count, width = query_rows.shape
    rows = groups * count
    qmask, fold = head_constants(count, width)
    vmem = pl.BlockSpec(memory_space=pltpu.VMEM)
    return pl.pallas_call(
        new_partial_kernel,
        out_shape=jax.ShapeDtypeStruct((HEADS, rows, LANES), jnp.float32),
        in_specs=[vmem] * 5,
        out_specs=vmem,
    )(query_rows, keys_new, values_new, qmask, fold)


def tail_kernel(low_ref, high_ref, new_ref, patch_ref, w_out_ref, gain_ref, w_up_ref, w_down_ref, out_ref):
    half_heads, rows, _ = low_ref.shape
    width = w_out_ref.shape[0]
    out_sum = jnp.zeros((rows, width), jnp.float32)
    for h in range(2 * half_heads):
        source = low_ref if h < half_heads else high_ref
        first = source[h % half_heads]
        second = new_ref[h]
        m1 = first[:, HD:HD + 1]
        m2 = second[:, HD:HD + 1]
        m = jnp.maximum(m1, m2)
        merged = first * jnp.exp(m1 - m) + second * jnp.exp(m2 - m)
        attended = (merged / merged[:, HD + 1:HD + 2]).astype(jnp.bfloat16)
        out_sum = out_sum + jnp.dot(
            attended[:, :HD], w_out_ref[pl.ds(h * HD, HD), :], preferred_element_type=jnp.float32
        )
    out_rows = out_sum.astype(jnp.bfloat16).astype(jnp.float32)
    groups, count, _ = patch_ref.shape
    patch_rows = jnp.concatenate([patch_ref[r].astype(jnp.float32) for r in range(groups)], axis=0)
    mixed_rows = patch_rows + out_rows
    normed_mixed = rms_norm(mixed_rows, gain_ref[...]).astype(jnp.bfloat16)
    up_rows = jnp.dot(normed_mixed, w_up_ref[...], preferred_element_type=jnp.float32).astype(jnp.bfloat16)
    up_float = up_rows.astype(jnp.float32)
    hidden = (up_float / (1.0 + jnp.exp(-up_float))).astype(jnp.bfloat16)
    down_rows = jnp.dot(hidden, w_down_ref[...], preferred_element_type=jnp.float32).astype(jnp.bfloat16)
    decoded = mixed_rows + down_rows.astype(jnp.float32)
    for r in range(groups):
        out_ref[r] = decoded[r * count:(r + 1) * count, :].astype(out_ref.dtype)


def tail(low_half, high_half, new_packed, patches, w_out, ffn_gain, w_up, w_down):
    vmem = pl.BlockSpec(memory_space=pltpu.VMEM)
    return pl.pallas_call(
        tail_kernel,
        out_shape=jax.ShapeDtypeStruct(patches.shape, jnp.bfloat16),
        in_specs=[vmem] * 8,
        out_specs=vmem,
    )(low_half, high_half, new_packed, patches, w_out, ffn_gain, w_up, w_down)


def layer(
    patches, key_cache, value_cache, cache_len, attn_gain, w_qkv, w_out, ffn_gain, w_up, w_down
):
    seq_count = lax.axis_size("seq")
    kept, sent, query_rows = cache_partials(cache_len, patches, attn_gain, w_qkv, key_cache, value_cache)
    keys_new, values_new = kv_projection(patches, attn_gain, w_qkv)
    new_packed = new_partials(query_rows, keys_new, values_new)
    low_half, high_half = combine_over_seq(kept, sent, seq_count)
    return tail(low_half, high_half, new_packed, patches, w_out, ffn_gain, w_up, w_down)


def solution(mesh):
    placed = (
        P("req", None, None),
        P("req", "seq", None),
        P("req", "seq", None),
        P("req"),
        P(),
        P(),
        P(),
        P(),
        P(),
        P(),
    )
    return jax.shard_map(layer, mesh=mesh, in_specs=placed, out_specs=P("req", None, None), check_vma=False)
```

```python
import numpy as np
import jax
import jax.numpy as jnp
from jax import lax
from jax.sharding import PartitionSpec as P
from jax.experimental.layout import Layout, with_layout_constraint
from jax.experimental import pallas as pl
from jax.experimental.pallas import tpu as pltpu

HEADS = 16
HD = 80


epsilon = 1e-06
negative_fill = -1e30


def rms_norm(values, gain):
    return values * lax.rsqrt(jnp.mean(values * values, axis=-1, keepdims=True) + epsilon) * gain


LANES = 128


def merge(first, second):
    m1 = first[..., HD:HD + 1]
    m2 = second[..., HD:HD + 1]
    m = jnp.maximum(m1, m2)
    a1 = jnp.exp(m1 - m)
    a2 = jnp.exp(m2 - m)
    merged = first * a1 + second * a2
    lane = lax.broadcasted_iota(jnp.int32, merged.shape, merged.ndim - 1)
    return jnp.where(lane == HD, m, merged)


def exchange(part, distance, count):
    pairs = [(i, i ^ distance) for i in range(count)]
    row_major = Layout(major_to_minor=(0, 1))
    part = with_layout_constraint(part, row_major)
    return with_layout_constraint(lax.ppermute(part, "seq", pairs), row_major)


def combine_over_seq(kept, sent, count):
    half_heads, rows, lanes = kept.shape
    me = lax.axis_index("seq")
    core = me % 2
    kept = kept.reshape(half_heads * rows, lanes)
    sent = sent.reshape(half_heads * rows, lanes)
    got = exchange(sent, 1, count)
    low_first = core == 0
    state = merge(jnp.where(low_first, kept, got), jnp.where(low_first, got, kept))
    distance = 2
    while distance < count:
        got = exchange(state, distance, count)
        low_first = (me // distance) % 2 == 0
        state = merge(jnp.where(low_first, state, got), jnp.where(low_first, got, state))
        distance *= 2
    other = exchange(state, 1, count)
    return state.reshape(half_heads, rows, lanes), other.reshape(half_heads, rows, lanes)


def folded_rows(rows, peak, total, qmask_float, fold, lane):
    own = rows * qmask_float
    high = own.astype(jnp.bfloat16)
    rest = own - high.astype(jnp.float32)
    middle = rest.astype(jnp.bfloat16)
    low = (rest - middle.astype(jnp.float32)).astype(jnp.bfloat16)
    folded = (
        jnp.dot(high, fold, preferred_element_type=jnp.float32)
        + jnp.dot(middle, fold, preferred_element_type=jnp.float32)
    ) + jnp.dot(low, fold, preferred_element_type=jnp.float32)
    return jnp.where(lane == HD, peak, jnp.where(lane == HD + 1, total, folded))


def folded_store(target, r, rows, peak, total, qmask_float, fold, lane):
    heads = target.shape[0]
    count = rows.shape[0] // heads
    folded = folded_rows(rows, peak, total, qmask_float, fold, lane)
    for h in range(heads):
        target[h, pl.ds(r * count, count), :] = folded[h * count:(h + 1) * count, :]


def normed_rows(patch_ref, gain_ref):
    groups = patch_ref.shape[0]
    rows = jnp.concatenate([patch_ref[r].astype(jnp.float32) for r in range(groups)], axis=0)
    return rms_norm(rows, gain_ref[...]).astype(jnp.bfloat16)


def cache_partial_kernel(
    length_ref, patch_ref, gain_ref, wq_ref, key_ref, value_ref, qmask_ref, fold_ref, kept_ref, sent_ref, query_ref
):
    groups, slots, _ = key_ref.shape
    half_heads = kept_ref.shape[0]
    heads = 2 * half_heads
    count = kept_ref.shape[1] // groups
    me = lax.axis_index("seq")
    core = me % 2
    query_float = jnp.dot(normed_rows(patch_ref, gain_ref), wq_ref[...], preferred_element_type=jnp.float32)
    for r in range(groups):
        query_ref[r] = query_float[r * count:(r + 1) * count, :].astype(query_ref.dtype)
    scale_factor = HD ** (-0.5)
    qmask = qmask_ref[core]
    qmask_float = qmask.astype(jnp.float32)
    fold = fold_ref[...]
    position = me * slots + lax.broadcasted_iota(jnp.int32, (1, slots), 1)
    lane = lax.broadcasted_iota(jnp.int32, (heads * count, LANES), 1)
    for r in range(groups):
        queries = query_ref[r]
        query_rows = jnp.concatenate([queries] * heads, axis=0) * qmask
        scores = lax.dot_general(
            query_rows, key_ref[r], (((1,), (1,)), ((), ())), preferred_element_type=jnp.float32
        ) * scale_factor
        live = position < length_ref[r]
        masked = jnp.where(live, scores, negative_fill)
        peak = jnp.max(masked, axis=1, keepdims=True)
        weights = jnp.where(live, jnp.exp(masked - peak), 0.0)
        total = jnp.sum(weights, axis=1, keepdims=True)
        value_rows = jnp.dot(
            weights.astype(jnp.bfloat16), value_ref[r], preferred_element_type=jnp.float32
        )
        folded = folded_rows(value_rows, peak, total, qmask_float, fold, lane)
        for h in range(heads):
            target = kept_ref if h < half_heads else sent_ref
            target[h % half_heads, pl.ds(r * count, count), :] = folded[h * count:(h + 1) * count, :]


def kv_projection_kernel(patch_ref, gain_ref, wk_ref, wv_ref, key_ref, value_ref):
    normed = normed_rows(patch_ref, gain_ref)
    key_ref[...] = jnp.dot(normed, wk_ref[...], preferred_element_type=jnp.float32).astype(key_ref.dtype)
    value_ref[...] = jnp.dot(normed, wv_ref[...], preferred_element_type=jnp.float32).astype(value_ref.dtype)


def new_partial_kernel(query_ref, key_new_ref, value_new_ref, qmask_ref, fold_ref, out_ref):
    groups, count, width = query_ref.shape
    heads = out_ref.shape[0]
    keys_all = key_new_ref[...]
    values_all = value_new_ref[...]
    scale_factor = HD ** (-0.5)
    qmask = qmask_ref[...]
    qmask_float = qmask.astype(jnp.float32)
    fold = fold_ref[...]
    lane = lax.broadcasted_iota(jnp.int32, (heads * count, LANES), 1)
    patch = lax.broadcasted_iota(jnp.int32, (heads * count, 1), 0) & (count - 1)
    for r in range(groups):
        queries = query_ref[r]
        query_float = (jnp.concatenate([queries] * heads, axis=0) * qmask).astype(jnp.float32)
        keys_new = keys_all.astype(jnp.float32)[r * count:(r + 1) * count, :]
        values_new = values_all.astype(jnp.float32)[r * count:(r + 1) * count, :]
        new_scores = []
        for u in range(count):
            score = jnp.sum(query_float * keys_new[u:u + 1, :], axis=1, keepdims=True) * scale_factor
            new_scores.append(jnp.where(patch >= u, score, negative_fill))
        new_peak = new_scores[0]
        for score in new_scores[1:]:
            new_peak = jnp.maximum(new_peak, score)
        new_total = jnp.zeros_like(new_peak)
        new_rows = jnp.zeros((heads * count, width), jnp.float32)
        for u in range(count):
            weight = jnp.where(patch >= u, jnp.exp(new_scores[u] - new_peak), 0.0)
            new_total = new_total + weight
            weight = weight.astype(jnp.bfloat16).astype(jnp.float32)
            new_rows = new_rows + weight * values_new[u:u + 1, :]
        folded_store(out_ref, r, new_rows, new_peak, new_total, qmask_float, fold, lane)


def head_constants(count, width):
    row_head = np.arange(HEADS * count)[:, None] // count
    col_head = np.arange(width)[None, :] // HD
    qmask = jnp.asarray((row_head == col_head).astype(np.float32), dtype=jnp.bfloat16)
    fold = jnp.asarray(
        (np.arange(width)[:, None] % HD == np.arange(LANES)[None, :]).astype(np.float32), dtype=jnp.bfloat16
    )
    return qmask, fold


def ordered_masks(count, width):
    masks = []
    for core in range(2):
        row_head = (np.arange(HEADS * count)[:, None] // count + core * (HEADS // 2)) % HEADS
        col_head = np.arange(width)[None, :] // HD
        masks.append((row_head == col_head).astype(np.float32))
    return jnp.asarray(np.stack(masks), dtype=jnp.bfloat16)


def cache_partials(cache_len, patches, attn_gain, w_qkv, key_cache, value_cache):
    groups, _, width = key_cache.shape
    count = patches.shape[1]
    rows = groups * count
    _, fold = head_constants(count, width)
    qmask = ordered_masks(count, width)
    smem = pl.BlockSpec(memory_space=pltpu.SMEM)
    vmem = pl.BlockSpec(memory_space=pltpu.VMEM)
    query_block = pl.BlockSpec((width, width), lambda i: (0, 0))
    half = jax.ShapeDtypeStruct((HEADS // 2, rows, LANES), jnp.float32)
    return pl.pallas_call(
        cache_partial_kernel,
        grid=(1,),
        out_shape=(half, half, jax.ShapeDtypeStruct(patches.shape, jnp.bfloat16)),
        in_specs=[smem, vmem, vmem, query_block, vmem, vmem, vmem, vmem],
        out_specs=(vmem, vmem, vmem),
    )(cache_len, patches, attn_gain, w_qkv, key_cache, value_cache, qmask, fold)


def kv_projection(patches, attn_gain, w_qkv):
    groups, count, width = patches.shape
    vmem = pl.BlockSpec(memory_space=pltpu.VMEM)
    key_block = pl.BlockSpec((width, width), lambda i: (0, 1))
    value_block = pl.BlockSpec((width, width), lambda i: (0, 2))
    rows = jax.ShapeDtypeStruct((groups * count, width), jnp.bfloat16)
    return pl.pallas_call(
        kv_projection_kernel,
        grid=(1,),
        out_shape=(rows, rows),
        in_specs=[vmem, vmem, key_block, value_block],
        out_specs=(vmem, vmem),
    )(patches, attn_gain, w_qkv, w_qkv)


def new_partials(query_rows, keys_new, values_new):
    groups, count, width = query_rows.shape
    rows = groups * count
    qmask, fold = head_constants(count, width)
    vmem = pl.BlockSpec(memory_space=pltpu.VMEM)
    return pl.pallas_call(
        new_partial_kernel,
        out_shape=jax.ShapeDtypeStruct((HEADS, rows, LANES), jnp.float32),
        in_specs=[vmem] * 5,
        out_specs=vmem,
    )(query_rows, keys_new, values_new, qmask, fold)


def tail_kernel(
    state_ref, other_ref, new_ref, patch_ref, w_out_ref, gain_ref, w_up_hbm, w_down_hbm, out_ref,
    w_up_ref, w_down_ref, copy_sems,
):
    copy_up = pltpu.make_async_copy(w_up_hbm, w_up_ref, copy_sems.at[0])
    copy_down = pltpu.make_async_copy(w_down_hbm, w_down_ref, copy_sems.at[1])
    copy_up.start()
    copy_down.start()
    half_heads, rows, _ = state_ref.shape
    width = w_out_ref.shape[0]
    low_first = lax.axis_index("seq") % 2 == 0
    out_sum = jnp.zeros((rows, width), jnp.float32)
    for h in range(2 * half_heads):
        mine, theirs = state_ref[h % half_heads], other_ref[h % half_heads]
        first = jnp.where(low_first == (h < half_heads), mine, theirs)
        second = new_ref[h]
        m1 = first[:, HD:HD + 1]
        m2 = second[:, HD:HD + 1]
        m = jnp.maximum(m1, m2)
        merged = first * jnp.exp(m1 - m) + second * jnp.exp(m2 - m)
        attended = (merged / merged[:, HD + 1:HD + 2]).astype(jnp.bfloat16)
        out_sum = out_sum + jnp.dot(
            attended[:, :HD], w_out_ref[pl.ds(h * HD, HD), :], preferred_element_type=jnp.float32
        )
    out_rows = out_sum.astype(jnp.bfloat16).astype(jnp.float32)
    groups, count, _ = patch_ref.shape
    patch_rows = jnp.concatenate([patch_ref[r].astype(jnp.float32) for r in range(groups)], axis=0)
    mixed_rows = patch_rows + out_rows
    normed_mixed = rms_norm(mixed_rows, gain_ref[...]).astype(jnp.bfloat16)
    copy_up.wait()
    up_rows = jnp.dot(normed_mixed, w_up_ref[...], preferred_element_type=jnp.float32).astype(jnp.bfloat16)
    up_float = up_rows.astype(jnp.float32)
    hidden = (up_float / (1.0 + jnp.exp(-up_float))).astype(jnp.bfloat16)
    copy_down.wait()
    down_rows = jnp.dot(hidden, w_down_ref[...], preferred_element_type=jnp.float32).astype(jnp.bfloat16)
    decoded = mixed_rows + down_rows.astype(jnp.float32)
    for r in range(groups):
        out_ref[r] = decoded[r * count:(r + 1) * count, :].astype(out_ref.dtype)


def tail(state, other, new_packed, patches, w_out, ffn_gain, w_up, w_down):
    vmem = pl.BlockSpec(memory_space=pltpu.VMEM)
    hbm = pl.BlockSpec(memory_space=pl.ANY)
    return pl.pallas_call(
        tail_kernel,
        out_shape=jax.ShapeDtypeStruct(patches.shape, jnp.bfloat16),
        in_specs=[vmem] * 6 + [hbm, hbm],
        out_specs=vmem,
        scratch_shapes=[
            pltpu.VMEM(w_up.shape, w_up.dtype),
            pltpu.VMEM(w_down.shape, w_down.dtype),
            pltpu.SemaphoreType.DMA((2,)),
        ],
    )(state, other, new_packed, patches, w_out, ffn_gain, w_up, w_down)


def layer(
    patches, key_cache, value_cache, cache_len, attn_gain, w_qkv, w_out, ffn_gain, w_up, w_down
):
    seq_count = lax.axis_size("seq")
    kept, sent, query_rows = cache_partials(cache_len, patches, attn_gain, w_qkv, key_cache, value_cache)
    keys_new, values_new = kv_projection(patches, attn_gain, w_qkv)
    new_packed = new_partials(query_rows, keys_new, values_new)
    state, other = combine_over_seq(kept, sent, seq_count)
    return tail(state, other, new_packed, patches, w_out, ffn_gain, w_up, w_down)


def solution(mesh):
    placed = (
        P("req", None, None),
        P("req", "seq", None),
        P("req", "seq", None),
        P("req"),
        P(),
        P(),
        P(),
        P(),
        P(),
        P(),
    )
    return jax.shard_map(layer, mesh=mesh, in_specs=placed, out_specs=P("req", None, None), check_vma=False)
```

```python
import numpy as np
import jax
import jax.numpy as jnp
from jax import lax
from jax.sharding import PartitionSpec as P
from jax.experimental.layout import Layout, with_layout_constraint
from jax.experimental import pallas as pl
from jax.experimental.pallas import tpu as pltpu

HEADS = 16
HD = 80


epsilon = 1e-06
negative_fill = -1e30


def rms_norm(values, gain):
    return values * lax.rsqrt(jnp.mean(values * values, axis=-1, keepdims=True) + epsilon) * gain


LANES = 128


def merge(first, second):
    m1 = first[..., HD:HD + 1]
    m2 = second[..., HD:HD + 1]
    m = jnp.maximum(m1, m2)
    a1 = jnp.exp(m1 - m)
    a2 = jnp.exp(m2 - m)
    merged = first * a1 + second * a2
    lane = lax.broadcasted_iota(jnp.int32, merged.shape, merged.ndim - 1)
    return jnp.where(lane == HD, m, merged)


def exchange(part, distance, count):
    pairs = [(i, i ^ distance) for i in range(count)]
    row_major = Layout(major_to_minor=(0, 1))
    part = with_layout_constraint(part, row_major)
    return with_layout_constraint(lax.ppermute(part, "seq", pairs), row_major)


def combine_over_seq(kept, sent, count):
    half_heads, rows, lanes = kept.shape
    me = lax.axis_index("seq")
    core = me % 2
    kept = kept.reshape(half_heads * rows, lanes)
    sent = sent.reshape(half_heads * rows, lanes)
    got = exchange(sent, 1, count)
    low_first = core == 0
    state = merge(jnp.where(low_first, kept, got), jnp.where(low_first, got, kept))
    distance = 2
    while distance < count:
        got = exchange(state, distance, count)
        low_first = (me // distance) % 2 == 0
        state = merge(jnp.where(low_first, state, got), jnp.where(low_first, got, state))
        distance *= 2
    other = exchange(state, 1, count)
    return state.reshape(half_heads, rows, lanes), other.reshape(half_heads, rows, lanes)


def folded_rows(rows, peak, total, qmask_float, fold, lane):
    own = rows * qmask_float
    high = own.astype(jnp.bfloat16)
    rest = own - high.astype(jnp.float32)
    middle = rest.astype(jnp.bfloat16)
    low = (rest - middle.astype(jnp.float32)).astype(jnp.bfloat16)
    folded = (
        jnp.dot(high, fold, preferred_element_type=jnp.float32)
        + jnp.dot(middle, fold, preferred_element_type=jnp.float32)
    ) + jnp.dot(low, fold, preferred_element_type=jnp.float32)
    return jnp.where(lane == HD, peak, jnp.where(lane == HD + 1, total, folded))


def folded_store(target, r, rows, peak, total, qmask_float, fold, lane):
    heads = target.shape[0]
    count = rows.shape[0] // heads
    folded = folded_rows(rows, peak, total, qmask_float, fold, lane)
    for h in range(heads):
        target[h, pl.ds(r * count, count), :] = folded[h * count:(h + 1) * count, :]


def normed_rows(patch_ref, gain_ref):
    groups = patch_ref.shape[0]
    rows = jnp.concatenate([patch_ref[r].astype(jnp.float32) for r in range(groups)], axis=0)
    return rms_norm(rows, gain_ref[...]).astype(jnp.bfloat16)


def cache_partial_kernel(
    length_ref, patch_ref, gain_ref, wqkv_hbm, key_hbm, value_hbm, qmask_ref, fold_ref, kept_ref, sent_ref,
    query_ref, wq_ref, key_ref, value_ref, copy_sems,
):
    groups, slots, width = key_ref.shape
    half_heads = kept_ref.shape[0]
    heads = 2 * half_heads
    count = kept_ref.shape[1] // groups
    me = lax.axis_index("seq")
    core = me % 2
    copy_wq = pltpu.make_async_copy(wqkv_hbm.at[:, pl.ds(0, width)], wq_ref, copy_sems.at[0])
    copy_wq.start()
    copy_keys, copy_values = [], []
    for r in range(groups):
        copy_keys.append(pltpu.make_async_copy(key_hbm.at[r], key_ref.at[r], copy_sems.at[1 + r]))
        copy_values.append(
            pltpu.make_async_copy(value_hbm.at[r], value_ref.at[r], copy_sems.at[1 + groups + r])
        )
        copy_keys[r].start()
        copy_values[r].start()
    normed = normed_rows(patch_ref, gain_ref)
    copy_wq.wait()
    query_float = jnp.dot(normed, wq_ref[...], preferred_element_type=jnp.float32)
    for r in range(groups):
        query_ref[r] = query_float[r * count:(r + 1) * count, :].astype(query_ref.dtype)
    scale_factor = HD ** (-0.5)
    qmask = qmask_ref[core]
    qmask_float = qmask.astype(jnp.float32)
    fold = fold_ref[...]
    position = me * slots + lax.broadcasted_iota(jnp.int32, (1, slots), 1)
    lane = lax.broadcasted_iota(jnp.int32, (heads * count, LANES), 1)
    for r in range(groups):
        queries = query_ref[r]
        query_rows = jnp.concatenate([queries] * heads, axis=0) * qmask
        copy_keys[r].wait()
        scores = lax.dot_general(
            query_rows, key_ref[r], (((1,), (1,)), ((), ())), preferred_element_type=jnp.float32
        ) * scale_factor
        live = position < length_ref[r]
        masked = jnp.where(live, scores, negative_fill)
        peak = jnp.max(masked, axis=1, keepdims=True)
        weights = jnp.where(live, jnp.exp(masked - peak), 0.0)
        total = jnp.sum(weights, axis=1, keepdims=True)
        copy_values[r].wait()
        value_rows = jnp.dot(
            weights.astype(jnp.bfloat16), value_ref[r], preferred_element_type=jnp.float32
        )
        folded = folded_rows(value_rows, peak, total, qmask_float, fold, lane)
        for h in range(heads):
            target = kept_ref if h < half_heads else sent_ref
            target[h % half_heads, pl.ds(r * count, count), :] = folded[h * count:(h + 1) * count, :]


def kv_projection_kernel(patch_ref, gain_ref, wk_ref, wv_ref, key_ref, value_ref):
    normed = normed_rows(patch_ref, gain_ref)
    key_ref[...] = jnp.dot(normed, wk_ref[...], preferred_element_type=jnp.float32).astype(key_ref.dtype)
    value_ref[...] = jnp.dot(normed, wv_ref[...], preferred_element_type=jnp.float32).astype(value_ref.dtype)


def new_partial_kernel(query_ref, key_new_ref, value_new_ref, qmask_ref, fold_ref, out_ref):
    groups, count, width = query_ref.shape
    heads = out_ref.shape[0]
    keys_all = key_new_ref[...]
    values_all = value_new_ref[...]
    scale_factor = HD ** (-0.5)
    qmask = qmask_ref[...]
    qmask_float = qmask.astype(jnp.float32)
    fold = fold_ref[...]
    lane = lax.broadcasted_iota(jnp.int32, (heads * count, LANES), 1)
    patch = lax.broadcasted_iota(jnp.int32, (heads * count, 1), 0) & (count - 1)
    for r in range(groups):
        queries = query_ref[r]
        query_float = (jnp.concatenate([queries] * heads, axis=0) * qmask).astype(jnp.float32)
        keys_new = keys_all.astype(jnp.float32)[r * count:(r + 1) * count, :]
        values_new = values_all.astype(jnp.float32)[r * count:(r + 1) * count, :]
        new_scores = []
        for u in range(count):
            score = jnp.sum(query_float * keys_new[u:u + 1, :], axis=1, keepdims=True) * scale_factor
            new_scores.append(jnp.where(patch >= u, score, negative_fill))
        new_peak = new_scores[0]
        for score in new_scores[1:]:
            new_peak = jnp.maximum(new_peak, score)
        new_total = jnp.zeros_like(new_peak)
        new_rows = jnp.zeros((heads * count, width), jnp.float32)
        for u in range(count):
            weight = jnp.where(patch >= u, jnp.exp(new_scores[u] - new_peak), 0.0)
            new_total = new_total + weight
            weight = weight.astype(jnp.bfloat16).astype(jnp.float32)
            new_rows = new_rows + weight * values_new[u:u + 1, :]
        folded_store(out_ref, r, new_rows, new_peak, new_total, qmask_float, fold, lane)


def head_constants(count, width):
    row_head = np.arange(HEADS * count)[:, None] // count
    col_head = np.arange(width)[None, :] // HD
    qmask = jnp.asarray((row_head == col_head).astype(np.float32), dtype=jnp.bfloat16)
    fold = jnp.asarray(
        (np.arange(width)[:, None] % HD == np.arange(LANES)[None, :]).astype(np.float32), dtype=jnp.bfloat16
    )
    return qmask, fold


def ordered_masks(count, width):
    masks = []
    for core in range(2):
        row_head = (np.arange(HEADS * count)[:, None] // count + core * (HEADS // 2)) % HEADS
        col_head = np.arange(width)[None, :] // HD
        masks.append((row_head == col_head).astype(np.float32))
    return jnp.asarray(np.stack(masks), dtype=jnp.bfloat16)


def cache_partials(cache_len, patches, attn_gain, w_qkv, key_cache, value_cache):
    groups, _, width = key_cache.shape
    count = patches.shape[1]
    rows = groups * count
    _, fold = head_constants(count, width)
    qmask = ordered_masks(count, width)
    smem = pl.BlockSpec(memory_space=pltpu.SMEM)
    vmem = pl.BlockSpec(memory_space=pltpu.VMEM)
    hbm = pl.BlockSpec(memory_space=pl.ANY)
    half = jax.ShapeDtypeStruct((HEADS // 2, rows, LANES), jnp.float32)
    return pl.pallas_call(
        cache_partial_kernel,
        out_shape=(half, half, jax.ShapeDtypeStruct(patches.shape, jnp.bfloat16)),
        in_specs=[smem, vmem, vmem, hbm, hbm, hbm, vmem, vmem],
        out_specs=(vmem, vmem, vmem),
        scratch_shapes=[
            pltpu.VMEM((width, width), w_qkv.dtype),
            pltpu.VMEM(key_cache.shape, key_cache.dtype),
            pltpu.VMEM(value_cache.shape, value_cache.dtype),
            pltpu.SemaphoreType.DMA((1 + 2 * groups,)),
        ],
    )(cache_len, patches, attn_gain, w_qkv, key_cache, value_cache, qmask, fold)


def kv_projection(patches, attn_gain, w_qkv):
    groups, count, width = patches.shape
    vmem = pl.BlockSpec(memory_space=pltpu.VMEM)
    key_block = pl.BlockSpec((width, width), lambda i: (0, 1))
    value_block = pl.BlockSpec((width, width), lambda i: (0, 2))
    rows = jax.ShapeDtypeStruct((groups * count, width), jnp.bfloat16)
    return pl.pallas_call(
        kv_projection_kernel,
        grid=(1,),
        out_shape=(rows, rows),
        in_specs=[vmem, vmem, key_block, value_block],
        out_specs=(vmem, vmem),
    )(patches, attn_gain, w_qkv, w_qkv)


def new_partials(query_rows, keys_new, values_new):
    groups, count, width = query_rows.shape
    rows = groups * count
    qmask, fold = head_constants(count, width)
    vmem = pl.BlockSpec(memory_space=pltpu.VMEM)
    return pl.pallas_call(
        new_partial_kernel,
        out_shape=jax.ShapeDtypeStruct((HEADS, rows, LANES), jnp.float32),
        in_specs=[vmem] * 5,
        out_specs=vmem,
    )(query_rows, keys_new, values_new, qmask, fold)


def tail_kernel(
    state_ref, other_ref, new_ref, patch_ref, w_out_ref, gain_ref, w_up_hbm, w_down_hbm, out_ref,
    w_up_ref, w_down_ref, copy_sems,
):
    copy_up = pltpu.make_async_copy(w_up_hbm, w_up_ref, copy_sems.at[0])
    copy_down = pltpu.make_async_copy(w_down_hbm, w_down_ref, copy_sems.at[1])
    copy_up.start()
    copy_down.start()
    half_heads, rows, _ = state_ref.shape
    width = w_out_ref.shape[0]
    low_first = lax.axis_index("seq") % 2 == 0
    out_sum = jnp.zeros((rows, width), jnp.float32)
    for h in range(2 * half_heads):
        mine, theirs = state_ref[h % half_heads], other_ref[h % half_heads]
        first = jnp.where(low_first == (h < half_heads), mine, theirs)
        second = new_ref[h]
        m1 = first[:, HD:HD + 1]
        m2 = second[:, HD:HD + 1]
        m = jnp.maximum(m1, m2)
        merged = first * jnp.exp(m1 - m) + second * jnp.exp(m2 - m)
        attended = (merged / merged[:, HD + 1:HD + 2]).astype(jnp.bfloat16)
        out_sum = out_sum + jnp.dot(
            attended[:, :HD], w_out_ref[pl.ds(h * HD, HD), :], preferred_element_type=jnp.float32
        )
    out_rows = out_sum.astype(jnp.bfloat16).astype(jnp.float32)
    groups, count, _ = patch_ref.shape
    patch_rows = jnp.concatenate([patch_ref[r].astype(jnp.float32) for r in range(groups)], axis=0)
    mixed_rows = patch_rows + out_rows
    normed_mixed = rms_norm(mixed_rows, gain_ref[...]).astype(jnp.bfloat16)
    copy_up.wait()
    up_rows = jnp.dot(normed_mixed, w_up_ref[...], preferred_element_type=jnp.float32).astype(jnp.bfloat16)
    up_float = up_rows.astype(jnp.float32)
    hidden = (up_float / (1.0 + jnp.exp(-up_float))).astype(jnp.bfloat16)
    copy_down.wait()
    down_rows = jnp.dot(hidden, w_down_ref[...], preferred_element_type=jnp.float32).astype(jnp.bfloat16)
    decoded = mixed_rows + down_rows.astype(jnp.float32)
    for r in range(groups):
        out_ref[r] = decoded[r * count:(r + 1) * count, :].astype(out_ref.dtype)


def tail(state, other, new_packed, patches, w_out, ffn_gain, w_up, w_down):
    vmem = pl.BlockSpec(memory_space=pltpu.VMEM)
    hbm = pl.BlockSpec(memory_space=pl.ANY)
    return pl.pallas_call(
        tail_kernel,
        out_shape=jax.ShapeDtypeStruct(patches.shape, jnp.bfloat16),
        in_specs=[vmem] * 6 + [hbm, hbm],
        out_specs=vmem,
        scratch_shapes=[
            pltpu.VMEM(w_up.shape, w_up.dtype),
            pltpu.VMEM(w_down.shape, w_down.dtype),
            pltpu.SemaphoreType.DMA((2,)),
        ],
    )(state, other, new_packed, patches, w_out, ffn_gain, w_up, w_down)


def layer(
    patches, key_cache, value_cache, cache_len, attn_gain, w_qkv, w_out, ffn_gain, w_up, w_down
):
    seq_count = lax.axis_size("seq")
    kept, sent, query_rows = cache_partials(cache_len, patches, attn_gain, w_qkv, key_cache, value_cache)
    keys_new, values_new = kv_projection(patches, attn_gain, w_qkv)
    new_packed = new_partials(query_rows, keys_new, values_new)
    state, other = combine_over_seq(kept, sent, seq_count)
    return tail(state, other, new_packed, patches, w_out, ffn_gain, w_up, w_down)


def solution(mesh):
    placed = (
        P("req", None, None),
        P("req", "seq", None),
        P("req", "seq", None),
        P("req"),
        P(),
        P(),
        P(),
        P(),
        P(),
        P(),
    )
    return jax.shard_map(layer, mesh=mesh, in_specs=placed, out_specs=P("req", None, None), check_vma=False)
```

```python
import numpy as np
import jax
import jax.numpy as jnp
from jax import lax
from jax.sharding import PartitionSpec as P
from jax.experimental.layout import Layout, with_layout_constraint
from jax.experimental import pallas as pl
from jax.experimental.pallas import tpu as pltpu

HEADS = 16
HD = 80


epsilon = 1e-06
negative_fill = -1e30


def rms_norm(values, gain):
    return values * lax.rsqrt(jnp.mean(values * values, axis=-1, keepdims=True) + epsilon) * gain


LANES = 128


def merge(first, second):
    m1 = first[..., HD:HD + 1]
    m2 = second[..., HD:HD + 1]
    m = jnp.maximum(m1, m2)
    a1 = jnp.exp(m1 - m)
    a2 = jnp.exp(m2 - m)
    merged = first * a1 + second * a2
    lane = lax.broadcasted_iota(jnp.int32, merged.shape, merged.ndim - 1)
    return jnp.where(lane == HD, m, merged)


def exchange(part, distance, count):
    pairs = [(i, i ^ distance) for i in range(count)]
    row_major = Layout(major_to_minor=(0, 1))
    part = with_layout_constraint(part, row_major)
    return with_layout_constraint(lax.ppermute(part, "seq", pairs), row_major)


def combine_over_seq(kept, sent, count):
    half_heads, rows, lanes = kept.shape
    me = lax.axis_index("seq")
    core = me % 2
    kept = kept.reshape(half_heads * rows, lanes)
    sent = sent.reshape(half_heads * rows, lanes)
    got = exchange(sent, 1, count)
    low_first = core == 0
    state = merge(jnp.where(low_first, kept, got), jnp.where(low_first, got, kept))
    distance = 2
    while distance < count:
        got = exchange(state, distance, count)
        low_first = (me // distance) % 2 == 0
        state = merge(jnp.where(low_first, state, got), jnp.where(low_first, got, state))
        distance *= 2
    other = exchange(state, 1, count)
    return state.reshape(half_heads, rows, lanes), other.reshape(half_heads, rows, lanes)


def folded_rows(rows, peak, total, qmask_float, fold, lane):
    own = rows * qmask_float
    high = own.astype(jnp.bfloat16)
    rest = own - high.astype(jnp.float32)
    middle = rest.astype(jnp.bfloat16)
    low = (rest - middle.astype(jnp.float32)).astype(jnp.bfloat16)
    folded = (
        jnp.dot(high, fold, preferred_element_type=jnp.float32)
        + jnp.dot(middle, fold, preferred_element_type=jnp.float32)
    ) + jnp.dot(low, fold, preferred_element_type=jnp.float32)
    return jnp.where(lane == HD, peak, jnp.where(lane == HD + 1, total, folded))


def folded_store(target, r, rows, peak, total, qmask_float, fold, lane):
    heads = target.shape[0]
    count = rows.shape[0] // heads
    folded = folded_rows(rows, peak, total, qmask_float, fold, lane)
    for h in range(heads):
        target[h, pl.ds(r * count, count), :] = folded[h * count:(h + 1) * count, :]


def normed_rows(patch_ref, gain_ref):
    groups = patch_ref.shape[0]
    rows = jnp.concatenate([patch_ref[r].astype(jnp.float32) for r in range(groups)], axis=0)
    return rms_norm(rows, gain_ref[...]).astype(jnp.bfloat16)


def cache_partial_kernel(
    length_ref, patch_ref, gain_ref, wq_ref, key_ref, value_ref, qmask_ref, fold_ref, kept_ref, sent_ref, query_ref
):
    groups, slots, _ = key_ref.shape
    half_heads = kept_ref.shape[0]
    heads = 2 * half_heads
    count = kept_ref.shape[1] // groups
    me = lax.axis_index("seq")
    core = me % 2
    query_float = jnp.dot(normed_rows(patch_ref, gain_ref), wq_ref[...], preferred_element_type=jnp.float32)
    for r in range(groups):
        query_ref[r] = query_float[r * count:(r + 1) * count, :].astype(query_ref.dtype)
    scale_factor = HD ** (-0.5)
    qmask = qmask_ref[core]
    qmask_float = qmask.astype(jnp.float32)
    fold = fold_ref[...]
    position = me * slots + lax.broadcasted_iota(jnp.int32, (1, slots), 1)
    lane = lax.broadcasted_iota(jnp.int32, (heads * count, LANES), 1)
    for r in range(groups):
        queries = query_ref[r]
        query_rows = jnp.concatenate([queries] * heads, axis=0) * qmask
        scores = lax.dot_general(
            query_rows, key_ref[r], (((1,), (1,)), ((), ())), preferred_element_type=jnp.float32
        ) * scale_factor
        live = position < length_ref[r]
        masked = jnp.where(live, scores, negative_fill)
        peak = jnp.max(masked, axis=1, keepdims=True)
        weights = jnp.where(live, jnp.exp(masked - peak), 0.0)
        total = jnp.sum(weights, axis=1, keepdims=True)
        value_rows = jnp.dot(
            weights.astype(jnp.bfloat16), value_ref[r], preferred_element_type=jnp.float32
        )
        folded = folded_rows(value_rows, peak, total, qmask_float, fold, lane)
        for h in range(heads):
            target = kept_ref if h < half_heads else sent_ref
            target[h % half_heads, pl.ds(r * count, count), :] = folded[h * count:(h + 1) * count, :]


def kv_projection_kernel(patch_ref, gain_ref, wk_ref, wv_ref, key_ref, value_ref):
    normed = normed_rows(patch_ref, gain_ref)
    key_ref[...] = jnp.dot(normed, wk_ref[...], preferred_element_type=jnp.float32).astype(key_ref.dtype)
    value_ref[...] = jnp.dot(normed, wv_ref[...], preferred_element_type=jnp.float32).astype(value_ref.dtype)


def new_partial_kernel(query_ref, key_new_ref, value_new_ref, qmask_ref, fold_ref, out_ref):
    groups, count, width = query_ref.shape
    heads = out_ref.shape[0]
    keys_all = key_new_ref[...]
    values_all = value_new_ref[...]
    scale_factor = HD ** (-0.5)
    qmask = qmask_ref[...]
    qmask_float = qmask.astype(jnp.float32)
    fold = fold_ref[...]
    lane = lax.broadcasted_iota(jnp.int32, (heads * count, LANES), 1)
    patch = lax.broadcasted_iota(jnp.int32, (heads * count, 1), 0) & (count - 1)
    for r in range(groups):
        queries = query_ref[r]
        query_float = (jnp.concatenate([queries] * heads, axis=0) * qmask).astype(jnp.float32)
        keys_new = keys_all.astype(jnp.float32)[r * count:(r + 1) * count, :]
        values_new = values_all.astype(jnp.float32)[r * count:(r + 1) * count, :]
        new_scores = []
        for u in range(count):
            score = jnp.sum(query_float * keys_new[u:u + 1, :], axis=1, keepdims=True) * scale_factor
            new_scores.append(jnp.where(patch >= u, score, negative_fill))
        new_peak = new_scores[0]
        for score in new_scores[1:]:
            new_peak = jnp.maximum(new_peak, score)
        new_total = jnp.zeros_like(new_peak)
        new_rows = jnp.zeros((heads * count, width), jnp.float32)
        for u in range(count):
            weight = jnp.where(patch >= u, jnp.exp(new_scores[u] - new_peak), 0.0)
            new_total = new_total + weight
            weight = weight.astype(jnp.bfloat16).astype(jnp.float32)
            new_rows = new_rows + weight * values_new[u:u + 1, :]
        folded_store(out_ref, r, new_rows, new_peak, new_total, qmask_float, fold, lane)


def head_constants(count, width):
    row_head = np.arange(HEADS * count)[:, None] // count
    col_head = np.arange(width)[None, :] // HD
    qmask = jnp.asarray((row_head == col_head).astype(np.float32), dtype=jnp.bfloat16)
    fold = jnp.asarray(
        (np.arange(width)[:, None] % HD == np.arange(LANES)[None, :]).astype(np.float32), dtype=jnp.bfloat16
    )
    return qmask, fold


def ordered_masks(count, width):
    masks = []
    for core in range(2):
        row_head = (np.arange(HEADS * count)[:, None] // count + core * (HEADS // 2)) % HEADS
        col_head = np.arange(width)[None, :] // HD
        masks.append((row_head == col_head).astype(np.float32))
    return jnp.asarray(np.stack(masks), dtype=jnp.bfloat16)


def cache_partials(cache_len, patches, attn_gain, w_qkv, key_cache, value_cache):
    groups, _, width = key_cache.shape
    count = patches.shape[1]
    rows = groups * count
    _, fold = head_constants(count, width)
    qmask = ordered_masks(count, width)
    smem = pl.BlockSpec(memory_space=pltpu.SMEM)
    vmem = pl.BlockSpec(memory_space=pltpu.VMEM)
    query_block = pl.BlockSpec((width, width), lambda i: (0, 0))
    half = jax.ShapeDtypeStruct((HEADS // 2, rows, LANES), jnp.float32)
    return pl.pallas_call(
        cache_partial_kernel,
        grid=(1,),
        out_shape=(half, half, jax.ShapeDtypeStruct(patches.shape, jnp.bfloat16)),
        in_specs=[smem, vmem, vmem, query_block, vmem, vmem, vmem, vmem],
        out_specs=(vmem, vmem, vmem),
    )(cache_len, patches, attn_gain, w_qkv, key_cache, value_cache, qmask, fold)


def kv_projection(patches, attn_gain, w_qkv):
    groups, count, width = patches.shape
    vmem = pl.BlockSpec(memory_space=pltpu.VMEM)
    key_block = pl.BlockSpec((width, width), lambda i: (0, 1))
    value_block = pl.BlockSpec((width, width), lambda i: (0, 2))
    rows = jax.ShapeDtypeStruct((groups * count, width), jnp.bfloat16)
    return pl.pallas_call(
        kv_projection_kernel,
        grid=(1,),
        out_shape=(rows, rows),
        in_specs=[vmem, vmem, key_block, value_block],
        out_specs=(vmem, vmem),
    )(patches, attn_gain, w_qkv, w_qkv)


def new_partials(query_rows, keys_new, values_new):
    groups, count, width = query_rows.shape
    rows = groups * count
    qmask, fold = head_constants(count, width)
    vmem = pl.BlockSpec(memory_space=pltpu.VMEM)
    return pl.pallas_call(
        new_partial_kernel,
        out_shape=jax.ShapeDtypeStruct((HEADS, rows, LANES), jnp.float32),
        in_specs=[vmem] * 5,
        out_specs=vmem,
    )(query_rows, keys_new, values_new, qmask, fold)


def tail_kernel(
    state_ref, other_ref, new_ref, patch_ref, w_out_hbm, gain_ref, w_up_hbm, w_down_hbm, out_ref,
    w_out_ref, w_up_ref, w_down_ref, copy_sems,
):
    half_heads, rows, _ = state_ref.shape
    width = w_out_ref.shape[0]
    half_rows = half_heads * HD
    copy_out = [
        pltpu.make_async_copy(
            w_out_hbm.at[pl.ds(i * half_rows, half_rows)], w_out_ref.at[pl.ds(i * half_rows, half_rows)],
            copy_sems.at[2 + i],
        )
        for i in range(2)
    ]
    copy_up = pltpu.make_async_copy(w_up_hbm, w_up_ref, copy_sems.at[0])
    copy_down = pltpu.make_async_copy(w_down_hbm, w_down_ref, copy_sems.at[1])
    for copy in copy_out:
        copy.start()
    copy_up.start()
    copy_down.start()
    low_first = lax.axis_index("seq") % 2 == 0
    out_sum = jnp.zeros((rows, width), jnp.float32)
    for h in range(2 * half_heads):
        if h % half_heads == 0:
            copy_out[h // half_heads].wait()
        mine, theirs = state_ref[h % half_heads], other_ref[h % half_heads]
        first = jnp.where(low_first == (h < half_heads), mine, theirs)
        second = new_ref[h]
        m1 = first[:, HD:HD + 1]
        m2 = second[:, HD:HD + 1]
        m = jnp.maximum(m1, m2)
        merged = first * jnp.exp(m1 - m) + second * jnp.exp(m2 - m)
        attended = (merged / merged[:, HD + 1:HD + 2]).astype(jnp.bfloat16)
        out_sum = out_sum + jnp.dot(
            attended[:, :HD], w_out_ref[pl.ds(h * HD, HD), :], preferred_element_type=jnp.float32
        )
    out_rows = out_sum.astype(jnp.bfloat16).astype(jnp.float32)
    groups, count, _ = patch_ref.shape
    patch_rows = jnp.concatenate([patch_ref[r].astype(jnp.float32) for r in range(groups)], axis=0)
    mixed_rows = patch_rows + out_rows
    normed_mixed = rms_norm(mixed_rows, gain_ref[...]).astype(jnp.bfloat16)
    copy_up.wait()
    up_rows = jnp.dot(normed_mixed, w_up_ref[...], preferred_element_type=jnp.float32).astype(jnp.bfloat16)
    up_float = up_rows.astype(jnp.float32)
    hidden = (up_float / (1.0 + jnp.exp(-up_float))).astype(jnp.bfloat16)
    copy_down.wait()
    down_rows = jnp.dot(hidden, w_down_ref[...], preferred_element_type=jnp.float32).astype(jnp.bfloat16)
    decoded = mixed_rows + down_rows.astype(jnp.float32)
    for r in range(groups):
        out_ref[r] = decoded[r * count:(r + 1) * count, :].astype(out_ref.dtype)


def tail(state, other, new_packed, patches, w_out, ffn_gain, w_up, w_down):
    vmem = pl.BlockSpec(memory_space=pltpu.VMEM)
    hbm = pl.BlockSpec(memory_space=pl.ANY)
    return pl.pallas_call(
        tail_kernel,
        out_shape=jax.ShapeDtypeStruct(patches.shape, jnp.bfloat16),
        in_specs=[vmem] * 4 + [hbm, vmem, hbm, hbm],
        out_specs=vmem,
        scratch_shapes=[
            pltpu.VMEM(w_out.shape, w_out.dtype),
            pltpu.VMEM(w_up.shape, w_up.dtype),
            pltpu.VMEM(w_down.shape, w_down.dtype),
            pltpu.SemaphoreType.DMA((4,)),
        ],
    )(state, other, new_packed, patches, w_out, ffn_gain, w_up, w_down)


def layer(
    patches, key_cache, value_cache, cache_len, attn_gain, w_qkv, w_out, ffn_gain, w_up, w_down
):
    seq_count = lax.axis_size("seq")
    kept, sent, query_rows = cache_partials(cache_len, patches, attn_gain, w_qkv, key_cache, value_cache)
    keys_new, values_new = kv_projection(patches, attn_gain, w_qkv)
    new_packed = new_partials(query_rows, keys_new, values_new)
    state, other = combine_over_seq(kept, sent, seq_count)
    return tail(state, other, new_packed, patches, w_out, ffn_gain, w_up, w_down)


def solution(mesh):
    placed = (
        P("req", None, None),
        P("req", "seq", None),
        P("req", "seq", None),
        P("req"),
        P(),
        P(),
        P(),
        P(),
        P(),
        P(),
    )
    return jax.shard_map(layer, mesh=mesh, in_specs=placed, out_specs=P("req", None, None), check_vma=False)
```

```python
import numpy as np
import jax
import jax.numpy as jnp
from jax import lax
from jax.sharding import PartitionSpec as P
from jax.experimental.layout import Layout, with_layout_constraint
from jax.experimental import pallas as pl
from jax.experimental.pallas import tpu as pltpu

HEADS = 16
HD = 80


epsilon = 1e-06
negative_fill = -1e30


def rms_norm(values, gain):
    return values * lax.rsqrt(jnp.mean(values * values, axis=-1, keepdims=True) + epsilon) * gain


LANES = 128


def merge(first, second):
    m1 = first[..., HD:HD + 1]
    m2 = second[..., HD:HD + 1]
    m = jnp.maximum(m1, m2)
    a1 = jnp.exp(m1 - m)
    a2 = jnp.exp(m2 - m)
    merged = first * a1 + second * a2
    lane = lax.broadcasted_iota(jnp.int32, merged.shape, merged.ndim - 1)
    return jnp.where(lane == HD, m, merged)


def exchange(part, distance, count):
    pairs = [(i, i ^ distance) for i in range(count)]
    row_major = Layout(major_to_minor=(0, 1))
    part = with_layout_constraint(part, row_major)
    return with_layout_constraint(lax.ppermute(part, "seq", pairs), row_major)


def combine_over_seq(kept, sent, count):
    half_heads, rows, lanes = kept.shape
    me = lax.axis_index("seq")
    core = me % 2
    kept = kept.reshape(half_heads * rows, lanes)
    sent = sent.reshape(half_heads * rows, lanes)
    got = exchange(sent, 1, count)
    low_first = core == 0
    state = merge(jnp.where(low_first, kept, got), jnp.where(low_first, got, kept))
    distance = 2
    while distance < count:
        got = exchange(state, distance, count)
        low_first = (me // distance) % 2 == 0
        state = merge(jnp.where(low_first, state, got), jnp.where(low_first, got, state))
        distance *= 2
    other = exchange(state, 1, count)
    return state.reshape(half_heads, rows, lanes), other.reshape(half_heads, rows, lanes)


def folded_rows(rows, peak, total, qmask_float, fold, lane):
    own = rows * qmask_float
    high = own.astype(jnp.bfloat16)
    rest = own - high.astype(jnp.float32)
    middle = rest.astype(jnp.bfloat16)
    low = (rest - middle.astype(jnp.float32)).astype(jnp.bfloat16)
    folded = (
        jnp.dot(high, fold, preferred_element_type=jnp.float32)
        + jnp.dot(middle, fold, preferred_element_type=jnp.float32)
    ) + jnp.dot(low, fold, preferred_element_type=jnp.float32)
    return jnp.where(lane == HD, peak, jnp.where(lane == HD + 1, total, folded))


def folded_store(target, r, rows, peak, total, qmask_float, fold, lane):
    heads = target.shape[0]
    count = rows.shape[0] // heads
    folded = folded_rows(rows, peak, total, qmask_float, fold, lane)
    for h in range(heads):
        target[h, pl.ds(r * count, count), :] = folded[h * count:(h + 1) * count, :]


def normed_rows(patch_ref, gain_ref):
    groups = patch_ref.shape[0]
    rows = jnp.concatenate([patch_ref[r].astype(jnp.float32) for r in range(groups)], axis=0)
    return rms_norm(rows, gain_ref[...]).astype(jnp.bfloat16)


def cache_partial_kernel(
    length_ref, patch_ref, gain_ref, wq_ref, key_hbm, value_hbm, qmask_ref, fold_ref, kept_ref, sent_ref, query_ref,
    key_ref, value_ref, copy_sems,
):
    groups, slots, _ = key_ref.shape
    half_heads = kept_ref.shape[0]
    heads = 2 * half_heads
    count = kept_ref.shape[1] // groups
    me = lax.axis_index("seq")
    core = me % 2
    copy_keys = pltpu.make_async_copy(key_hbm, key_ref, copy_sems.at[0])
    copy_values = pltpu.make_async_copy(value_hbm, value_ref, copy_sems.at[1])
    copy_keys.start()
    copy_values.start()
    query_float = jnp.dot(normed_rows(patch_ref, gain_ref), wq_ref[...], preferred_element_type=jnp.float32)
    for r in range(groups):
        query_ref[r] = query_float[r * count:(r + 1) * count, :].astype(query_ref.dtype)
    scale_factor = HD ** (-0.5)
    qmask = qmask_ref[core]
    qmask_float = qmask.astype(jnp.float32)
    fold = fold_ref[...]
    position = me * slots + lax.broadcasted_iota(jnp.int32, (1, slots), 1)
    lane = lax.broadcasted_iota(jnp.int32, (heads * count, LANES), 1)
    copy_keys.wait()
    copy_values.wait()
    for r in range(groups):
        queries = query_ref[r]
        query_rows = jnp.concatenate([queries] * heads, axis=0) * qmask
        scores = lax.dot_general(
            query_rows, key_ref[r], (((1,), (1,)), ((), ())), preferred_element_type=jnp.float32
        ) * scale_factor
        live = position < length_ref[r]
        masked = jnp.where(live, scores, negative_fill)
        peak = jnp.max(masked, axis=1, keepdims=True)
        weights = jnp.where(live, jnp.exp(masked - peak), 0.0)
        total = jnp.sum(weights, axis=1, keepdims=True)
        value_rows = jnp.dot(
            weights.astype(jnp.bfloat16), value_ref[r], preferred_element_type=jnp.float32
        )
        folded = folded_rows(value_rows, peak, total, qmask_float, fold, lane)
        for h in range(heads):
            target = kept_ref if h < half_heads else sent_ref
            target[h % half_heads, pl.ds(r * count, count), :] = folded[h * count:(h + 1) * count, :]


def kv_projection_kernel(patch_ref, gain_ref, wk_ref, wv_ref, key_ref, value_ref):
    normed = normed_rows(patch_ref, gain_ref)
    key_ref[...] = jnp.dot(normed, wk_ref[...], preferred_element_type=jnp.float32).astype(key_ref.dtype)
    value_ref[...] = jnp.dot(normed, wv_ref[...], preferred_element_type=jnp.float32).astype(value_ref.dtype)


def new_partial_kernel(query_ref, key_new_ref, value_new_ref, qmask_ref, fold_ref, out_ref):
    groups, count, width = query_ref.shape
    heads = out_ref.shape[0]
    keys_all = key_new_ref[...]
    values_all = value_new_ref[...]
    scale_factor = HD ** (-0.5)
    qmask = qmask_ref[...]
    qmask_float = qmask.astype(jnp.float32)
    fold = fold_ref[...]
    lane = lax.broadcasted_iota(jnp.int32, (heads * count, LANES), 1)
    patch = lax.broadcasted_iota(jnp.int32, (heads * count, 1), 0) & (count - 1)
    for r in range(groups):
        queries = query_ref[r]
        query_float = (jnp.concatenate([queries] * heads, axis=0) * qmask).astype(jnp.float32)
        keys_new = keys_all.astype(jnp.float32)[r * count:(r + 1) * count, :]
        values_new = values_all.astype(jnp.float32)[r * count:(r + 1) * count, :]
        new_scores = []
        for u in range(count):
            score = jnp.sum(query_float * keys_new[u:u + 1, :], axis=1, keepdims=True) * scale_factor
            new_scores.append(jnp.where(patch >= u, score, negative_fill))
        new_peak = new_scores[0]
        for score in new_scores[1:]:
            new_peak = jnp.maximum(new_peak, score)
        new_total = jnp.zeros_like(new_peak)
        new_rows = jnp.zeros((heads * count, width), jnp.float32)
        for u in range(count):
            weight = jnp.where(patch >= u, jnp.exp(new_scores[u] - new_peak), 0.0)
            new_total = new_total + weight
            weight = weight.astype(jnp.bfloat16).astype(jnp.float32)
            new_rows = new_rows + weight * values_new[u:u + 1, :]
        folded_store(out_ref, r, new_rows, new_peak, new_total, qmask_float, fold, lane)


def head_constants(count, width):
    row_head = np.arange(HEADS * count)[:, None] // count
    col_head = np.arange(width)[None, :] // HD
    qmask = jnp.asarray((row_head == col_head).astype(np.float32), dtype=jnp.bfloat16)
    fold = jnp.asarray(
        (np.arange(width)[:, None] % HD == np.arange(LANES)[None, :]).astype(np.float32), dtype=jnp.bfloat16
    )
    return qmask, fold


def ordered_masks(count, width):
    masks = []
    for core in range(2):
        row_head = (np.arange(HEADS * count)[:, None] // count + core * (HEADS // 2)) % HEADS
        col_head = np.arange(width)[None, :] // HD
        masks.append((row_head == col_head).astype(np.float32))
    return jnp.asarray(np.stack(masks), dtype=jnp.bfloat16)


def cache_partials(cache_len, patches, attn_gain, w_qkv, key_cache, value_cache):
    groups, _, width = key_cache.shape
    count = patches.shape[1]
    rows = groups * count
    _, fold = head_constants(count, width)
    qmask = ordered_masks(count, width)
    smem = pl.BlockSpec(memory_space=pltpu.SMEM)
    vmem = pl.BlockSpec(memory_space=pltpu.VMEM)
    hbm = pl.BlockSpec(memory_space=pl.ANY)
    query_block = pl.BlockSpec((width, width), lambda i: (0, 0))
    half = jax.ShapeDtypeStruct((HEADS // 2, rows, LANES), jnp.float32)
    return pl.pallas_call(
        cache_partial_kernel,
        grid=(1,),
        out_shape=(half, half, jax.ShapeDtypeStruct(patches.shape, jnp.bfloat16)),
        in_specs=[smem, vmem, vmem, query_block, hbm, hbm, vmem, vmem],
        out_specs=(vmem, vmem, vmem),
        scratch_shapes=[
            pltpu.VMEM(key_cache.shape, key_cache.dtype),
            pltpu.VMEM(value_cache.shape, value_cache.dtype),
            pltpu.SemaphoreType.DMA((2,)),
        ],
    )(cache_len, patches, attn_gain, w_qkv, key_cache, value_cache, qmask, fold)


def kv_projection(patches, attn_gain, w_qkv):
    groups, count, width = patches.shape
    vmem = pl.BlockSpec(memory_space=pltpu.VMEM)
    key_block = pl.BlockSpec((width, width), lambda i: (0, 1))
    value_block = pl.BlockSpec((width, width), lambda i: (0, 2))
    rows = jax.ShapeDtypeStruct((groups * count, width), jnp.bfloat16)
    return pl.pallas_call(
        kv_projection_kernel,
        grid=(1,),
        out_shape=(rows, rows),
        in_specs=[vmem, vmem, key_block, value_block],
        out_specs=(vmem, vmem),
    )(patches, attn_gain, w_qkv, w_qkv)


def new_partials(query_rows, keys_new, values_new):
    groups, count, width = query_rows.shape
    rows = groups * count
    qmask, fold = head_constants(count, width)
    vmem = pl.BlockSpec(memory_space=pltpu.VMEM)
    return pl.pallas_call(
        new_partial_kernel,
        out_shape=jax.ShapeDtypeStruct((HEADS, rows, LANES), jnp.float32),
        in_specs=[vmem] * 5,
        out_specs=vmem,
    )(query_rows, keys_new, values_new, qmask, fold)


def tail_kernel(
    state_ref, other_ref, new_ref, patch_ref, w_out_ref, gain_ref, w_up_hbm, w_down_hbm, out_ref,
    w_up_ref, w_down_ref, copy_sems,
):
    copy_up = pltpu.make_async_copy(w_up_hbm, w_up_ref, copy_sems.at[0])
    copy_down = pltpu.make_async_copy(w_down_hbm, w_down_ref, copy_sems.at[1])
    copy_up.start()
    copy_down.start()
    half_heads, rows, _ = state_ref.shape
    width = w_out_ref.shape[0]
    low_first = lax.axis_index("seq") % 2 == 0
    out_sum = jnp.zeros((rows, width), jnp.float32)
    for h in range(2 * half_heads):
        mine, theirs = state_ref[h % half_heads], other_ref[h % half_heads]
        first = jnp.where(low_first == (h < half_heads), mine, theirs)
        second = new_ref[h]
        m1 = first[:, HD:HD + 1]
        m2 = second[:, HD:HD + 1]
        m = jnp.maximum(m1, m2)
        merged = first * jnp.exp(m1 - m) + second * jnp.exp(m2 - m)
        attended = (merged / merged[:, HD + 1:HD + 2]).astype(jnp.bfloat16)
        out_sum = out_sum + jnp.dot(
            attended[:, :HD], w_out_ref[pl.ds(h * HD, HD), :], preferred_element_type=jnp.float32
        )
    out_rows = out_sum.astype(jnp.bfloat16).astype(jnp.float32)
    groups, count, _ = patch_ref.shape
    patch_rows = jnp.concatenate([patch_ref[r].astype(jnp.float32) for r in range(groups)], axis=0)
    mixed_rows = patch_rows + out_rows
    normed_mixed = rms_norm(mixed_rows, gain_ref[...]).astype(jnp.bfloat16)
    copy_up.wait()
    up_rows = jnp.dot(normed_mixed, w_up_ref[...], preferred_element_type=jnp.float32).astype(jnp.bfloat16)
    up_float = up_rows.astype(jnp.float32)
    hidden = (up_float / (1.0 + jnp.exp(-up_float))).astype(jnp.bfloat16)
    copy_down.wait()
    down_rows = jnp.dot(hidden, w_down_ref[...], preferred_element_type=jnp.float32).astype(jnp.bfloat16)
    decoded = mixed_rows + down_rows.astype(jnp.float32)
    for r in range(groups):
        out_ref[r] = decoded[r * count:(r + 1) * count, :].astype(out_ref.dtype)


def tail(state, other, new_packed, patches, w_out, ffn_gain, w_up, w_down):
    vmem = pl.BlockSpec(memory_space=pltpu.VMEM)
    hbm = pl.BlockSpec(memory_space=pl.ANY)
    return pl.pallas_call(
        tail_kernel,
        out_shape=jax.ShapeDtypeStruct(patches.shape, jnp.bfloat16),
        in_specs=[vmem] * 6 + [hbm, hbm],
        out_specs=vmem,
        scratch_shapes=[
            pltpu.VMEM(w_up.shape, w_up.dtype),
            pltpu.VMEM(w_down.shape, w_down.dtype),
            pltpu.SemaphoreType.DMA((2,)),
        ],
    )(state, other, new_packed, patches, w_out, ffn_gain, w_up, w_down)


def layer(
    patches, key_cache, value_cache, cache_len, attn_gain, w_qkv, w_out, ffn_gain, w_up, w_down
):
    seq_count = lax.axis_size("seq")
    kept, sent, query_rows = cache_partials(cache_len, patches, attn_gain, w_qkv, key_cache, value_cache)
    keys_new, values_new = kv_projection(patches, attn_gain, w_qkv)
    new_packed = new_partials(query_rows, keys_new, values_new)
    state, other = combine_over_seq(kept, sent, seq_count)
    return tail(state, other, new_packed, patches, w_out, ffn_gain, w_up, w_down)


def solution(mesh):
    placed = (
        P("req", None, None),
        P("req", "seq", None),
        P("req", "seq", None),
        P("req"),
        P(),
        P(),
        P(),
        P(),
        P(),
        P(),
    )
    return jax.shard_map(layer, mesh=mesh, in_specs=placed, out_specs=P("req", None, None), check_vma=False)
```

```python
import numpy as np
import jax
import jax.numpy as jnp
from jax import lax
from jax.sharding import PartitionSpec as P
from jax.experimental.layout import Layout, with_layout_constraint
from jax.experimental import pallas as pl
from jax.experimental.pallas import tpu as pltpu

HEADS = 16
HD = 80


epsilon = 1e-06
negative_fill = -1e30


def rms_norm(values, gain):
    return values * lax.rsqrt(jnp.mean(values * values, axis=-1, keepdims=True) + epsilon) * gain


LANES = 128


def merge(first, second):
    m1 = first[..., HD:HD + 1]
    m2 = second[..., HD:HD + 1]
    m = jnp.maximum(m1, m2)
    a1 = jnp.exp(m1 - m)
    a2 = jnp.exp(m2 - m)
    merged = first * a1 + second * a2
    lane = lax.broadcasted_iota(jnp.int32, merged.shape, merged.ndim - 1)
    return jnp.where(lane == HD, m, merged)


def exchange(part, distance, count):
    pairs = [(i, i ^ distance) for i in range(count)]
    row_major = Layout(major_to_minor=(0, 1))
    part = with_layout_constraint(part, row_major)
    return with_layout_constraint(lax.ppermute(part, "seq", pairs), row_major)


def combine_over_seq(kept, sent, count):
    half_heads, rows, lanes = kept.shape
    me = lax.axis_index("seq")
    core = me % 2
    kept = kept.reshape(half_heads * rows, lanes)
    sent = sent.reshape(half_heads * rows, lanes)
    got = exchange(sent, 1, count)
    low_first = core == 0
    state = merge(jnp.where(low_first, kept, got), jnp.where(low_first, got, kept))
    distance = 2
    while distance < count:
        got = exchange(state, distance, count)
        low_first = (me // distance) % 2 == 0
        state = merge(jnp.where(low_first, state, got), jnp.where(low_first, got, state))
        distance *= 2
    other = exchange(state, 1, count)
    return state.reshape(half_heads, rows, lanes), other.reshape(half_heads, rows, lanes)


def folded_rows(rows, peak, total, qmask_float, fold, lane):
    own = rows * qmask_float
    high = own.astype(jnp.bfloat16)
    rest = own - high.astype(jnp.float32)
    middle = rest.astype(jnp.bfloat16)
    low = (rest - middle.astype(jnp.float32)).astype(jnp.bfloat16)
    folded = (
        jnp.dot(high, fold, preferred_element_type=jnp.float32)
        + jnp.dot(middle, fold, preferred_element_type=jnp.float32)
    ) + jnp.dot(low, fold, preferred_element_type=jnp.float32)
    return jnp.where(lane == HD, peak, jnp.where(lane == HD + 1, total, folded))


def folded_store(target, r, rows, peak, total, qmask_float, fold, lane):
    heads = target.shape[0]
    count = rows.shape[0] // heads
    folded = folded_rows(rows, peak, total, qmask_float, fold, lane)
    for h in range(heads):
        target[h, pl.ds(r * count, count), :] = folded[h * count:(h + 1) * count, :]


def normed_rows(patch_ref, gain_ref):
    groups = patch_ref.shape[0]
    rows = jnp.concatenate([patch_ref[r].astype(jnp.float32) for r in range(groups)], axis=0)
    return rms_norm(rows, gain_ref[...]).astype(jnp.bfloat16)


def cache_partial_kernel(
    length_ref, patch_ref, gain_ref, wq_ref, key_ref, value_ref, qmask_ref, fold_ref, kept_ref, sent_ref, query_ref
):
    groups, slots, _ = key_ref.shape
    half_heads = kept_ref.shape[0]
    heads = 2 * half_heads
    count = kept_ref.shape[1] // groups
    me = lax.axis_index("seq")
    core = me % 2
    query_float = jnp.dot(normed_rows(patch_ref, gain_ref), wq_ref[...], preferred_element_type=jnp.float32)
    for r in range(groups):
        query_ref[r] = query_float[r * count:(r + 1) * count, :].astype(query_ref.dtype)
    scale_factor = HD ** (-0.5)
    qmask = qmask_ref[core]
    qmask_float = qmask.astype(jnp.float32)
    fold = fold_ref[...]
    position = me * slots + lax.broadcasted_iota(jnp.int32, (1, slots), 1)
    lane = lax.broadcasted_iota(jnp.int32, (heads * count, LANES), 1)
    for r in range(groups):
        queries = query_ref[r]
        query_rows = jnp.concatenate([queries] * heads, axis=0) * qmask
        scores = lax.dot_general(
            query_rows, key_ref[r], (((1,), (1,)), ((), ())), preferred_element_type=jnp.float32
        ) * scale_factor
        live = position < length_ref[r]
        masked = jnp.where(live, scores, negative_fill)
        peak = jnp.max(masked, axis=1, keepdims=True)
        weights = jnp.where(live, jnp.exp(masked - peak), 0.0)
        total = jnp.sum(weights, axis=1, keepdims=True)
        value_rows = jnp.dot(
            weights.astype(jnp.bfloat16), value_ref[r], preferred_element_type=jnp.float32
        )
        folded = folded_rows(value_rows, peak, total, qmask_float, fold, lane)
        for h in range(heads):
            target = kept_ref if h < half_heads else sent_ref
            target[h % half_heads, pl.ds(r * count, count), :] = folded[h * count:(h + 1) * count, :]


def kv_projection_kernel(patch_ref, gain_ref, w_ref, out_ref):
    normed = normed_rows(patch_ref, gain_ref)
    out_ref[...] = jnp.dot(normed, w_ref[...], preferred_element_type=jnp.float32).astype(out_ref.dtype)


def new_partial_kernel(query_ref, kv_ref, qmask_ref, fold_ref, out_ref):
    groups, count, width = query_ref.shape
    heads = out_ref.shape[0]
    keys_all = kv_ref[:, pl.ds(0, width)]
    values_all = kv_ref[:, pl.ds(width, width)]
    scale_factor = HD ** (-0.5)
    qmask = qmask_ref[...]
    qmask_float = qmask.astype(jnp.float32)
    fold = fold_ref[...]
    lane = lax.broadcasted_iota(jnp.int32, (heads * count, LANES), 1)
    patch = lax.broadcasted_iota(jnp.int32, (heads * count, 1), 0) & (count - 1)
    for r in range(groups):
        queries = query_ref[r]
        query_float = (jnp.concatenate([queries] * heads, axis=0) * qmask).astype(jnp.float32)
        keys_new = keys_all.astype(jnp.float32)[r * count:(r + 1) * count, :]
        values_new = values_all.astype(jnp.float32)[r * count:(r + 1) * count, :]
        new_scores = []
        for u in range(count):
            score = jnp.sum(query_float * keys_new[u:u + 1, :], axis=1, keepdims=True) * scale_factor
            new_scores.append(jnp.where(patch >= u, score, negative_fill))
        new_peak = new_scores[0]
        for score in new_scores[1:]:
            new_peak = jnp.maximum(new_peak, score)
        new_total = jnp.zeros_like(new_peak)
        new_rows = jnp.zeros((heads * count, width), jnp.float32)
        for u in range(count):
            weight = jnp.where(patch >= u, jnp.exp(new_scores[u] - new_peak), 0.0)
            new_total = new_total + weight
            weight = weight.astype(jnp.bfloat16).astype(jnp.float32)
            new_rows = new_rows + weight * values_new[u:u + 1, :]
        folded_store(out_ref, r, new_rows, new_peak, new_total, qmask_float, fold, lane)


def head_constants(count, width):
    row_head = np.arange(HEADS * count)[:, None] // count
    col_head = np.arange(width)[None, :] // HD
    qmask = jnp.asarray((row_head == col_head).astype(np.float32), dtype=jnp.bfloat16)
    fold = jnp.asarray(
        (np.arange(width)[:, None] % HD == np.arange(LANES)[None, :]).astype(np.float32), dtype=jnp.bfloat16
    )
    return qmask, fold


def ordered_masks(count, width):
    masks = []
    for core in range(2):
        row_head = (np.arange(HEADS * count)[:, None] // count + core * (HEADS // 2)) % HEADS
        col_head = np.arange(width)[None, :] // HD
        masks.append((row_head == col_head).astype(np.float32))
    return jnp.asarray(np.stack(masks), dtype=jnp.bfloat16)


def cache_partials(cache_len, patches, attn_gain, w_qkv, key_cache, value_cache):
    groups, _, width = key_cache.shape
    count = patches.shape[1]
    rows = groups * count
    _, fold = head_constants(count, width)
    qmask = ordered_masks(count, width)
    smem = pl.BlockSpec(memory_space=pltpu.SMEM)
    vmem = pl.BlockSpec(memory_space=pltpu.VMEM)
    query_block = pl.BlockSpec((width, width), lambda i: (0, 0))
    half = jax.ShapeDtypeStruct((HEADS // 2, rows, LANES), jnp.float32)
    return pl.pallas_call(
        cache_partial_kernel,
        grid=(1,),
        out_shape=(half, half, jax.ShapeDtypeStruct(patches.shape, jnp.bfloat16)),
        in_specs=[smem, vmem, vmem, query_block, vmem, vmem, vmem, vmem],
        out_specs=(vmem, vmem, vmem),
    )(cache_len, patches, attn_gain, w_qkv, key_cache, value_cache, qmask, fold)


def kv_projection(patches, attn_gain, w_qkv):
    groups, count, width = patches.shape
    vmem = pl.BlockSpec(memory_space=pltpu.VMEM)
    weight_block = pl.BlockSpec((width, width), lambda i: (0, 1 + i))
    out_block = pl.BlockSpec((groups * count, width), lambda i: (0, i))
    both = pl.pallas_call(
        kv_projection_kernel,
        grid=(2,),
        out_shape=jax.ShapeDtypeStruct((groups * count, 2 * width), jnp.bfloat16),
        in_specs=[vmem, vmem, weight_block],
        out_specs=out_block,
    )(patches, attn_gain, w_qkv)
    return both


def new_partials(query_rows, kv_rows):
    groups, count, width = query_rows.shape
    rows = groups * count
    qmask, fold = head_constants(count, width)
    vmem = pl.BlockSpec(memory_space=pltpu.VMEM)
    return pl.pallas_call(
        new_partial_kernel,
        out_shape=jax.ShapeDtypeStruct((HEADS, rows, LANES), jnp.float32),
        in_specs=[vmem] * 4,
        out_specs=vmem,
    )(query_rows, kv_rows, qmask, fold)


def tail_kernel(
    state_ref, other_ref, new_ref, patch_ref, w_out_ref, gain_ref, w_up_hbm, w_down_hbm, out_ref,
    w_up_ref, w_down_ref, copy_sems,
):
    copy_up = pltpu.make_async_copy(w_up_hbm, w_up_ref, copy_sems.at[0])
    copy_down = pltpu.make_async_copy(w_down_hbm, w_down_ref, copy_sems.at[1])
    copy_up.start()
    copy_down.start()
    half_heads, rows, _ = state_ref.shape
    width = w_out_ref.shape[0]
    low_first = lax.axis_index("seq") % 2 == 0
    out_sum = jnp.zeros((rows, width), jnp.float32)
    for h in range(2 * half_heads):
        mine, theirs = state_ref[h % half_heads], other_ref[h % half_heads]
        first = jnp.where(low_first == (h < half_heads), mine, theirs)
        second = new_ref[h]
        m1 = first[:, HD:HD + 1]
        m2 = second[:, HD:HD + 1]
        m = jnp.maximum(m1, m2)
        merged = first * jnp.exp(m1 - m) + second * jnp.exp(m2 - m)
        attended = (merged / merged[:, HD + 1:HD + 2]).astype(jnp.bfloat16)
        out_sum = out_sum + jnp.dot(
            attended[:, :HD], w_out_ref[pl.ds(h * HD, HD), :], preferred_element_type=jnp.float32
        )
    out_rows = out_sum.astype(jnp.bfloat16).astype(jnp.float32)
    groups, count, _ = patch_ref.shape
    patch_rows = jnp.concatenate([patch_ref[r].astype(jnp.float32) for r in range(groups)], axis=0)
    mixed_rows = patch_rows + out_rows
    normed_mixed = rms_norm(mixed_rows, gain_ref[...]).astype(jnp.bfloat16)
    copy_up.wait()
    up_rows = jnp.dot(normed_mixed, w_up_ref[...], preferred_element_type=jnp.float32).astype(jnp.bfloat16)
    up_float = up_rows.astype(jnp.float32)
    hidden = (up_float / (1.0 + jnp.exp(-up_float))).astype(jnp.bfloat16)
    copy_down.wait()
    down_rows = jnp.dot(hidden, w_down_ref[...], preferred_element_type=jnp.float32).astype(jnp.bfloat16)
    decoded = mixed_rows + down_rows.astype(jnp.float32)
    for r in range(groups):
        out_ref[r] = decoded[r * count:(r + 1) * count, :].astype(out_ref.dtype)


def tail(state, other, new_packed, patches, w_out, ffn_gain, w_up, w_down):
    vmem = pl.BlockSpec(memory_space=pltpu.VMEM)
    hbm = pl.BlockSpec(memory_space=pl.ANY)
    return pl.pallas_call(
        tail_kernel,
        out_shape=jax.ShapeDtypeStruct(patches.shape, jnp.bfloat16),
        in_specs=[vmem] * 6 + [hbm, hbm],
        out_specs=vmem,
        scratch_shapes=[
            pltpu.VMEM(w_up.shape, w_up.dtype),
            pltpu.VMEM(w_down.shape, w_down.dtype),
            pltpu.SemaphoreType.DMA((2,)),
        ],
    )(state, other, new_packed, patches, w_out, ffn_gain, w_up, w_down)


def layer(
    patches, key_cache, value_cache, cache_len, attn_gain, w_qkv, w_out, ffn_gain, w_up, w_down
):
    seq_count = lax.axis_size("seq")
    kept, sent, query_rows = cache_partials(cache_len, patches, attn_gain, w_qkv, key_cache, value_cache)
    kv_rows = kv_projection(patches, attn_gain, w_qkv)
    new_packed = new_partials(query_rows, kv_rows)
    state, other = combine_over_seq(kept, sent, seq_count)
    return tail(state, other, new_packed, patches, w_out, ffn_gain, w_up, w_down)


def solution(mesh):
    placed = (
        P("req", None, None),
        P("req", "seq", None),
        P("req", "seq", None),
        P("req"),
        P(),
        P(),
        P(),
        P(),
        P(),
        P(),
    )
    return jax.shard_map(layer, mesh=mesh, in_specs=placed, out_specs=P("req", None, None), check_vma=False)
```

```python
import numpy as np
import jax
import jax.numpy as jnp
from jax import lax
from jax.sharding import PartitionSpec as P
from jax.experimental.layout import Layout, with_layout_constraint
from jax.experimental import pallas as pl
from jax.experimental.pallas import tpu as pltpu

HEADS = 16
HD = 80


epsilon = 1e-06
negative_fill = -1e30


def rms_norm(values, gain):
    return values * lax.rsqrt(jnp.mean(values * values, axis=-1, keepdims=True) + epsilon) * gain


LANES = 128


def merge(first, second):
    m1 = first[..., HD:HD + 1]
    m2 = second[..., HD:HD + 1]
    m = jnp.maximum(m1, m2)
    a1 = jnp.exp(m1 - m)
    a2 = jnp.exp(m2 - m)
    merged = first * a1 + second * a2
    lane = lax.broadcasted_iota(jnp.int32, merged.shape, merged.ndim - 1)
    return jnp.where(lane == HD, m, merged)


def exchange(part, distance, count):
    pairs = [(i, i ^ distance) for i in range(count)]
    row_major = Layout(major_to_minor=(0, 1))
    part = with_layout_constraint(part, row_major)
    return with_layout_constraint(lax.ppermute(part, "seq", pairs), row_major)


def combine_over_seq(kept, sent, count):
    half_heads, rows, lanes = kept.shape
    me = lax.axis_index("seq")
    core = me % 2
    kept = kept.reshape(half_heads * rows, lanes)
    sent = sent.reshape(half_heads * rows, lanes)
    got = exchange(sent, 1, count)
    low_first = core == 0
    state = merge(jnp.where(low_first, kept, got), jnp.where(low_first, got, kept))
    distance = 2
    while distance < count:
        got = exchange(state, distance, count)
        low_first = (me // distance) % 2 == 0
        state = merge(jnp.where(low_first, state, got), jnp.where(low_first, got, state))
        distance *= 2
    other = exchange(state, 1, count)
    return state.reshape(half_heads, rows, lanes), other.reshape(half_heads, rows, lanes)


def folded_rows(rows, peak, total, qmask_float, fold, lane):
    own = rows * qmask_float
    high = own.astype(jnp.bfloat16)
    rest = own - high.astype(jnp.float32)
    middle = rest.astype(jnp.bfloat16)
    low = (rest - middle.astype(jnp.float32)).astype(jnp.bfloat16)
    folded = (
        jnp.dot(high, fold, preferred_element_type=jnp.float32)
        + jnp.dot(middle, fold, preferred_element_type=jnp.float32)
    ) + jnp.dot(low, fold, preferred_element_type=jnp.float32)
    return jnp.where(lane == HD, peak, jnp.where(lane == HD + 1, total, folded))


def folded_store(target, r, rows, peak, total, qmask_float, fold, lane):
    heads = target.shape[0]
    count = rows.shape[0] // heads
    folded = folded_rows(rows, peak, total, qmask_float, fold, lane)
    for h in range(heads):
        target[h, pl.ds(r * count, count), :] = folded[h * count:(h + 1) * count, :]


def normed_rows(patch_ref, gain_ref):
    groups = patch_ref.shape[0]
    rows = jnp.concatenate([patch_ref[r].astype(jnp.float32) for r in range(groups)], axis=0)
    return rms_norm(rows, gain_ref[...]).astype(jnp.bfloat16)


def cache_partial_kernel(
    length_ref, patch_ref, gain_ref, wq_ref, key_ref, value_ref, qmask_ref, fold_ref, kept_ref, sent_ref, query_ref
):
    groups, slots, _ = key_ref.shape
    half_heads = kept_ref.shape[0]
    heads = 2 * half_heads
    count = kept_ref.shape[1] // groups
    step = pl.program_id(0)
    me = lax.axis_index("seq")
    core = me % 2

    @pl.when(step == 0)
    def _():
        query_float = jnp.dot(normed_rows(patch_ref, gain_ref), wq_ref[...], preferred_element_type=jnp.float32)
        for r in range(query_ref.shape[0]):
            query_ref[r] = query_float[r * count:(r + 1) * count, :].astype(query_ref.dtype)

    scale_factor = HD ** (-0.5)
    qmask = qmask_ref[core]
    qmask_float = qmask.astype(jnp.float32)
    fold = fold_ref[...]
    position = me * slots + lax.broadcasted_iota(jnp.int32, (1, slots), 1)
    lane = lax.broadcasted_iota(jnp.int32, (heads * count, LANES), 1)
    for r in range(groups):
        queries = query_ref[step * groups + r]
        query_rows = jnp.concatenate([queries] * heads, axis=0) * qmask
        scores = lax.dot_general(
            query_rows, key_ref[r], (((1,), (1,)), ((), ())), preferred_element_type=jnp.float32
        ) * scale_factor
        live = position < length_ref[step * groups + r]
        masked = jnp.where(live, scores, negative_fill)
        peak = jnp.max(masked, axis=1, keepdims=True)
        weights = jnp.where(live, jnp.exp(masked - peak), 0.0)
        total = jnp.sum(weights, axis=1, keepdims=True)
        value_rows = jnp.dot(
            weights.astype(jnp.bfloat16), value_ref[r], preferred_element_type=jnp.float32
        )
        folded = folded_rows(value_rows, peak, total, qmask_float, fold, lane)
        for h in range(heads):
            target = kept_ref if h < half_heads else sent_ref
            target[h % half_heads, pl.ds(r * count, count), :] = folded[h * count:(h + 1) * count, :]


def kv_projection_kernel(patch_ref, gain_ref, w_ref, out_ref):
    normed = normed_rows(patch_ref, gain_ref)
    out_ref[...] = jnp.dot(normed, w_ref[...], preferred_element_type=jnp.float32).astype(out_ref.dtype)


def new_partial_kernel(query_ref, kv_ref, qmask_ref, fold_ref, out_ref):
    groups, count, width = query_ref.shape
    heads = out_ref.shape[0]
    keys_all = kv_ref[:, pl.ds(0, width)]
    values_all = kv_ref[:, pl.ds(width, width)]
    scale_factor = HD ** (-0.5)
    qmask = qmask_ref[...]
    qmask_float = qmask.astype(jnp.float32)
    fold = fold_ref[...]
    lane = lax.broadcasted_iota(jnp.int32, (heads * count, LANES), 1)
    patch = lax.broadcasted_iota(jnp.int32, (heads * count, 1), 0) & (count - 1)
    for r in range(groups):
        queries = query_ref[r]
        query_float = (jnp.concatenate([queries] * heads, axis=0) * qmask).astype(jnp.float32)
        keys_new = keys_all.astype(jnp.float32)[r * count:(r + 1) * count, :]
        values_new = values_all.astype(jnp.float32)[r * count:(r + 1) * count, :]
        new_scores = []
        for u in range(count):
            score = jnp.sum(query_float * keys_new[u:u + 1, :], axis=1, keepdims=True) * scale_factor
            new_scores.append(jnp.where(patch >= u, score, negative_fill))
        new_peak = new_scores[0]
        for score in new_scores[1:]:
            new_peak = jnp.maximum(new_peak, score)
        new_total = jnp.zeros_like(new_peak)
        new_rows = jnp.zeros((heads * count, width), jnp.float32)
        for u in range(count):
            weight = jnp.where(patch >= u, jnp.exp(new_scores[u] - new_peak), 0.0)
            new_total = new_total + weight
            weight = weight.astype(jnp.bfloat16).astype(jnp.float32)
            new_rows = new_rows + weight * values_new[u:u + 1, :]
        folded_store(out_ref, r, new_rows, new_peak, new_total, qmask_float, fold, lane)


def head_constants(count, width):
    row_head = np.arange(HEADS * count)[:, None] // count
    col_head = np.arange(width)[None, :] // HD
    qmask = jnp.asarray((row_head == col_head).astype(np.float32), dtype=jnp.bfloat16)
    fold = jnp.asarray(
        (np.arange(width)[:, None] % HD == np.arange(LANES)[None, :]).astype(np.float32), dtype=jnp.bfloat16
    )
    return qmask, fold


def ordered_masks(count, width):
    masks = []
    for core in range(2):
        row_head = (np.arange(HEADS * count)[:, None] // count + core * (HEADS // 2)) % HEADS
        col_head = np.arange(width)[None, :] // HD
        masks.append((row_head == col_head).astype(np.float32))
    return jnp.asarray(np.stack(masks), dtype=jnp.bfloat16)


def cache_partials(cache_len, patches, attn_gain, w_qkv, key_cache, value_cache):
    groups, slots, width = key_cache.shape
    count = patches.shape[1]
    rows = groups * count
    _, fold = head_constants(count, width)
    qmask = ordered_masks(count, width)
    smem = pl.BlockSpec(memory_space=pltpu.SMEM)
    vmem = pl.BlockSpec(memory_space=pltpu.VMEM)
    query_block = pl.BlockSpec((width, width), lambda i: (0, 0))
    steps = 4
    cache_block = pl.BlockSpec((groups // steps, slots, width), lambda i: (i, 0, 0))
    half_block = pl.BlockSpec((HEADS // 2, rows // steps, LANES), lambda i: (0, i, 0))
    half = jax.ShapeDtypeStruct((HEADS // 2, rows, LANES), jnp.float32)
    return pl.pallas_call(
        cache_partial_kernel,
        grid=(steps,),
        out_shape=(half, half, jax.ShapeDtypeStruct(patches.shape, jnp.bfloat16)),
        in_specs=[smem, vmem, vmem, query_block, cache_block, cache_block, vmem, vmem],
        out_specs=(half_block, half_block, vmem),
    )(cache_len, patches, attn_gain, w_qkv, key_cache, value_cache, qmask, fold)


def kv_projection(patches, attn_gain, w_qkv):
    groups, count, width = patches.shape
    vmem = pl.BlockSpec(memory_space=pltpu.VMEM)
    weight_block = pl.BlockSpec((width, width), lambda i: (0, 1 + i))
    out_block = pl.BlockSpec((groups * count, width), lambda i: (0, i))
    both = pl.pallas_call(
        kv_projection_kernel,
        grid=(2,),
        out_shape=jax.ShapeDtypeStruct((groups * count, 2 * width), jnp.bfloat16),
        in_specs=[vmem, vmem, weight_block],
        out_specs=out_block,
    )(patches, attn_gain, w_qkv)
    return both


def new_partials(query_rows, kv_rows):
    groups, count, width = query_rows.shape
    rows = groups * count
    qmask, fold = head_constants(count, width)
    vmem = pl.BlockSpec(memory_space=pltpu.VMEM)
    return pl.pallas_call(
        new_partial_kernel,
        out_shape=jax.ShapeDtypeStruct((HEADS, rows, LANES), jnp.float32),
        in_specs=[vmem] * 4,
        out_specs=vmem,
    )(query_rows, kv_rows, qmask, fold)


def tail_kernel(
    state_ref, other_ref, new_ref, patch_ref, w_out_ref, gain_ref, w_up_hbm, w_down_hbm, out_ref,
    w_up_ref, w_down_ref, copy_sems,
):
    copy_up = pltpu.make_async_copy(w_up_hbm, w_up_ref, copy_sems.at[0])
    copy_down = pltpu.make_async_copy(w_down_hbm, w_down_ref, copy_sems.at[1])
    copy_up.start()
    copy_down.start()
    half_heads, rows, _ = state_ref.shape
    width = w_out_ref.shape[0]
    low_first = lax.axis_index("seq") % 2 == 0
    out_sum = jnp.zeros((rows, width), jnp.float32)
    for h in range(2 * half_heads):
        mine, theirs = state_ref[h % half_heads], other_ref[h % half_heads]
        first = jnp.where(low_first == (h < half_heads), mine, theirs)
        second = new_ref[h]
        m1 = first[:, HD:HD + 1]
        m2 = second[:, HD:HD + 1]
        m = jnp.maximum(m1, m2)
        merged = first * jnp.exp(m1 - m) + second * jnp.exp(m2 - m)
        attended = (merged / merged[:, HD + 1:HD + 2]).astype(jnp.bfloat16)
        out_sum = out_sum + jnp.dot(
            attended[:, :HD], w_out_ref[pl.ds(h * HD, HD), :], preferred_element_type=jnp.float32
        )
    out_rows = out_sum.astype(jnp.bfloat16).astype(jnp.float32)
    groups, count, _ = patch_ref.shape
    patch_rows = jnp.concatenate([patch_ref[r].astype(jnp.float32) for r in range(groups)], axis=0)
    mixed_rows = patch_rows + out_rows
    normed_mixed = rms_norm(mixed_rows, gain_ref[...]).astype(jnp.bfloat16)
    copy_up.wait()
    up_rows = jnp.dot(normed_mixed, w_up_ref[...], preferred_element_type=jnp.float32).astype(jnp.bfloat16)
    up_float = up_rows.astype(jnp.float32)
    hidden = (up_float / (1.0 + jnp.exp(-up_float))).astype(jnp.bfloat16)
    copy_down.wait()
    down_rows = jnp.dot(hidden, w_down_ref[...], preferred_element_type=jnp.float32).astype(jnp.bfloat16)
    decoded = mixed_rows + down_rows.astype(jnp.float32)
    for r in range(groups):
        out_ref[r] = decoded[r * count:(r + 1) * count, :].astype(out_ref.dtype)


def tail(state, other, new_packed, patches, w_out, ffn_gain, w_up, w_down):
    vmem = pl.BlockSpec(memory_space=pltpu.VMEM)
    hbm = pl.BlockSpec(memory_space=pl.ANY)
    return pl.pallas_call(
        tail_kernel,
        out_shape=jax.ShapeDtypeStruct(patches.shape, jnp.bfloat16),
        in_specs=[vmem] * 6 + [hbm, hbm],
        out_specs=vmem,
        scratch_shapes=[
            pltpu.VMEM(w_up.shape, w_up.dtype),
            pltpu.VMEM(w_down.shape, w_down.dtype),
            pltpu.SemaphoreType.DMA((2,)),
        ],
    )(state, other, new_packed, patches, w_out, ffn_gain, w_up, w_down)


def layer(
    patches, key_cache, value_cache, cache_len, attn_gain, w_qkv, w_out, ffn_gain, w_up, w_down
):
    seq_count = lax.axis_size("seq")
    kept, sent, query_rows = cache_partials(cache_len, patches, attn_gain, w_qkv, key_cache, value_cache)
    kv_rows = kv_projection(patches, attn_gain, w_qkv)
    new_packed = new_partials(query_rows, kv_rows)
    state, other = combine_over_seq(kept, sent, seq_count)
    return tail(state, other, new_packed, patches, w_out, ffn_gain, w_up, w_down)


def solution(mesh):
    placed = (
        P("req", None, None),
        P("req", "seq", None),
        P("req", "seq", None),
        P("req"),
        P(),
        P(),
        P(),
        P(),
        P(),
        P(),
    )
    return jax.shard_map(layer, mesh=mesh, in_specs=placed, out_specs=P("req", None, None), check_vma=False)
```

```python
import numpy as np
import jax
import jax.numpy as jnp
from jax import lax
from jax.sharding import PartitionSpec as P
from jax.experimental.layout import Layout, with_layout_constraint
from jax.experimental import pallas as pl
from jax.experimental.pallas import tpu as pltpu

HEADS = 16
HD = 80


epsilon = 1e-06
negative_fill = -1e30


def rms_norm(values, gain):
    return values * lax.rsqrt(jnp.mean(values * values, axis=-1, keepdims=True) + epsilon) * gain


LANES = 128


def merge(first, second):
    m1 = first[..., HD:HD + 1]
    m2 = second[..., HD:HD + 1]
    m = jnp.maximum(m1, m2)
    a1 = jnp.exp(m1 - m)
    a2 = jnp.exp(m2 - m)
    merged = first * a1 + second * a2
    lane = lax.broadcasted_iota(jnp.int32, merged.shape, merged.ndim - 1)
    return jnp.where(lane == HD, m, merged)


def exchange(part, distance, count):
    pairs = [(i, i ^ distance) for i in range(count)]
    row_major = Layout(major_to_minor=(0, 1))
    part = with_layout_constraint(part, row_major)
    return with_layout_constraint(lax.ppermute(part, "seq", pairs), row_major)


def combine_over_seq(kept, sent, count):
    half_heads, rows, lanes = kept.shape
    me = lax.axis_index("seq")
    core = me % 2
    kept = kept.reshape(half_heads * rows, lanes)
    sent = sent.reshape(half_heads * rows, lanes)
    got = exchange(sent, 1, count)
    low_first = core == 0
    state = merge(jnp.where(low_first, kept, got), jnp.where(low_first, got, kept))
    distance = 2
    while distance < count:
        got = exchange(state, distance, count)
        low_first = (me // distance) % 2 == 0
        state = merge(jnp.where(low_first, state, got), jnp.where(low_first, got, state))
        distance *= 2
    other = exchange(state, 1, count)
    return state.reshape(half_heads, rows, lanes), other.reshape(half_heads, rows, lanes)


def folded_rows(rows, peak, total, qmask_float, fold, lane):
    own = rows * qmask_float
    high = own.astype(jnp.bfloat16)
    rest = own - high.astype(jnp.float32)
    middle = rest.astype(jnp.bfloat16)
    low = (rest - middle.astype(jnp.float32)).astype(jnp.bfloat16)
    folded = (
        jnp.dot(high, fold, preferred_element_type=jnp.float32)
        + jnp.dot(middle, fold, preferred_element_type=jnp.float32)
    ) + jnp.dot(low, fold, preferred_element_type=jnp.float32)
    return jnp.where(lane == HD, peak, jnp.where(lane == HD + 1, total, folded))


def folded_store(target, r, rows, peak, total, qmask_float, fold, lane):
    heads = target.shape[0]
    count = rows.shape[0] // heads
    folded = folded_rows(rows, peak, total, qmask_float, fold, lane)
    for h in range(heads):
        target[h, pl.ds(r * count, count), :] = folded[h * count:(h + 1) * count, :]


def normed_rows(patch_ref, gain_ref):
    groups = patch_ref.shape[0]
    rows = jnp.concatenate([patch_ref[r].astype(jnp.float32) for r in range(groups)], axis=0)
    return rms_norm(rows, gain_ref[...]).astype(jnp.bfloat16)


def cache_partial_kernel(
    length_ref, patch_ref, gain_ref, wq_ref, key_ref, value_ref, qmask_ref, fold_ref, kept_ref, sent_ref, query_ref
):
    groups, slots, _ = key_ref.shape
    half_heads = kept_ref.shape[0]
    heads = 2 * half_heads
    count = kept_ref.shape[1] // groups
    step = pl.program_id(0)
    me = lax.axis_index("seq")
    core = me % 2

    @pl.when(step == 0)
    def _():
        query_float = jnp.dot(normed_rows(patch_ref, gain_ref), wq_ref[...], preferred_element_type=jnp.float32)
        for r in range(query_ref.shape[0]):
            query_ref[r] = query_float[r * count:(r + 1) * count, :].astype(query_ref.dtype)

    scale_factor = HD ** (-0.5)
    qmask = qmask_ref[core]
    qmask_float = qmask.astype(jnp.float32)
    fold = fold_ref[...]
    position = me * slots + lax.broadcasted_iota(jnp.int32, (1, slots), 1)
    lane = lax.broadcasted_iota(jnp.int32, (heads * count, LANES), 1)
    for r in range(groups):
        queries = query_ref[step * groups + r]
        query_rows = jnp.concatenate([queries] * heads, axis=0) * qmask
        scores = lax.dot_general(
            query_rows, key_ref[r], (((1,), (1,)), ((), ())), preferred_element_type=jnp.float32
        ) * scale_factor
        live = position < length_ref[step * groups + r]
        masked = jnp.where(live, scores, negative_fill)
        peak = jnp.max(masked, axis=1, keepdims=True)
        weights = jnp.where(live, jnp.exp(masked - peak), 0.0)
        total = jnp.sum(weights, axis=1, keepdims=True)
        value_rows = jnp.dot(
            weights.astype(jnp.bfloat16), value_ref[r], preferred_element_type=jnp.float32
        )
        folded = folded_rows(value_rows, peak, total, qmask_float, fold, lane)
        for h in range(heads):
            target = kept_ref if h < half_heads else sent_ref
            target[h % half_heads, pl.ds(r * count, count), :] = folded[h * count:(h + 1) * count, :]


def kv_projection_kernel(patch_ref, gain_ref, w_ref, out_ref):
    normed = normed_rows(patch_ref, gain_ref)
    out_ref[...] = jnp.dot(normed, w_ref[...], preferred_element_type=jnp.float32).astype(out_ref.dtype)


def new_partial_kernel(query_ref, kv_ref, qmask_ref, fold_ref, out_ref):
    groups, count, width = query_ref.shape
    heads = out_ref.shape[0]
    keys_all = kv_ref[:, pl.ds(0, width)]
    values_all = kv_ref[:, pl.ds(width, width)]
    scale_factor = HD ** (-0.5)
    qmask = qmask_ref[...]
    qmask_float = qmask.astype(jnp.float32)
    fold = fold_ref[...]
    lane = lax.broadcasted_iota(jnp.int32, (heads * count, LANES), 1)
    patch = lax.broadcasted_iota(jnp.int32, (heads * count, 1), 0) & (count - 1)
    for r in range(groups):
        queries = query_ref[r]
        query_float = (jnp.concatenate([queries] * heads, axis=0) * qmask).astype(jnp.float32)
        keys_new = keys_all.astype(jnp.float32)[r * count:(r + 1) * count, :]
        values_new = values_all.astype(jnp.float32)[r * count:(r + 1) * count, :]
        new_scores = []
        for u in range(count):
            score = jnp.sum(query_float * keys_new[u:u + 1, :], axis=1, keepdims=True) * scale_factor
            new_scores.append(jnp.where(patch >= u, score, negative_fill))
        new_peak = new_scores[0]
        for score in new_scores[1:]:
            new_peak = jnp.maximum(new_peak, score)
        new_total = jnp.zeros_like(new_peak)
        new_rows = jnp.zeros((heads * count, width), jnp.float32)
        for u in range(count):
            weight = jnp.where(patch >= u, jnp.exp(new_scores[u] - new_peak), 0.0)
            new_total = new_total + weight
            weight = weight.astype(jnp.bfloat16).astype(jnp.float32)
            new_rows = new_rows + weight * values_new[u:u + 1, :]
        folded_store(out_ref, r, new_rows, new_peak, new_total, qmask_float, fold, lane)


def head_constants(count, width):
    row_head = np.arange(HEADS * count)[:, None] // count
    col_head = np.arange(width)[None, :] // HD
    qmask = jnp.asarray((row_head == col_head).astype(np.float32), dtype=jnp.bfloat16)
    fold = jnp.asarray(
        (np.arange(width)[:, None] % HD == np.arange(LANES)[None, :]).astype(np.float32), dtype=jnp.bfloat16
    )
    return qmask, fold


def ordered_masks(count, width):
    masks = []
    for core in range(2):
        row_head = (np.arange(HEADS * count)[:, None] // count + core * (HEADS // 2)) % HEADS
        col_head = np.arange(width)[None, :] // HD
        masks.append((row_head == col_head).astype(np.float32))
    return jnp.asarray(np.stack(masks), dtype=jnp.bfloat16)


def cache_partials(cache_len, patches, attn_gain, w_qkv, key_cache, value_cache):
    groups, slots, width = key_cache.shape
    count = patches.shape[1]
    rows = groups * count
    _, fold = head_constants(count, width)
    qmask = ordered_masks(count, width)
    smem = pl.BlockSpec(memory_space=pltpu.SMEM)
    vmem = pl.BlockSpec(memory_space=pltpu.VMEM)
    query_block = pl.BlockSpec((width, width), lambda i: (0, 0))
    steps = 2
    cache_block = pl.BlockSpec((groups // steps, slots, width), lambda i: (i, 0, 0))
    half_block = pl.BlockSpec((HEADS // 2, rows // steps, LANES), lambda i: (0, i, 0))
    half = jax.ShapeDtypeStruct((HEADS // 2, rows, LANES), jnp.float32)
    return pl.pallas_call(
        cache_partial_kernel,
        grid=(steps,),
        out_shape=(half, half, jax.ShapeDtypeStruct(patches.shape, jnp.bfloat16)),
        in_specs=[smem, vmem, vmem, query_block, cache_block, cache_block, vmem, vmem],
        out_specs=(half_block, half_block, vmem),
    )(cache_len, patches, attn_gain, w_qkv, key_cache, value_cache, qmask, fold)


def kv_projection(patches, attn_gain, w_qkv):
    groups, count, width = patches.shape
    vmem = pl.BlockSpec(memory_space=pltpu.VMEM)
    pieces = 4
    piece = 2 * width // pieces
    weight_block = pl.BlockSpec((width, piece), lambda i: (0, pieces // 2 + i))
    out_block = pl.BlockSpec((groups * count, piece), lambda i: (0, i))
    both = pl.pallas_call(
        kv_projection_kernel,
        grid=(pieces,),
        out_shape=jax.ShapeDtypeStruct((groups * count, 2 * width), jnp.bfloat16),
        in_specs=[vmem, vmem, weight_block],
        out_specs=out_block,
    )(patches, attn_gain, w_qkv)
    return both


def new_partials(query_rows, kv_rows):
    groups, count, width = query_rows.shape
    rows = groups * count
    qmask, fold = head_constants(count, width)
    vmem = pl.BlockSpec(memory_space=pltpu.VMEM)
    return pl.pallas_call(
        new_partial_kernel,
        out_shape=jax.ShapeDtypeStruct((HEADS, rows, LANES), jnp.float32),
        in_specs=[vmem] * 4,
        out_specs=vmem,
    )(query_rows, kv_rows, qmask, fold)


def tail_kernel(
    state_ref, other_ref, new_ref, patch_ref, w_out_ref, gain_ref, w_up_hbm, w_down_hbm, out_ref,
    w_up_ref, w_down_ref, copy_sems,
):
    copy_up = pltpu.make_async_copy(w_up_hbm, w_up_ref, copy_sems.at[0])
    copy_down = pltpu.make_async_copy(w_down_hbm, w_down_ref, copy_sems.at[1])
    copy_up.start()
    copy_down.start()
    half_heads, rows, _ = state_ref.shape
    width = w_out_ref.shape[0]
    low_first = lax.axis_index("seq") % 2 == 0
    out_sum = jnp.zeros((rows, width), jnp.float32)
    for h in range(2 * half_heads):
        mine, theirs = state_ref[h % half_heads], other_ref[h % half_heads]
        first = jnp.where(low_first == (h < half_heads), mine, theirs)
        second = new_ref[h]
        m1 = first[:, HD:HD + 1]
        m2 = second[:, HD:HD + 1]
        m = jnp.maximum(m1, m2)
        merged = first * jnp.exp(m1 - m) + second * jnp.exp(m2 - m)
        attended = (merged / merged[:, HD + 1:HD + 2]).astype(jnp.bfloat16)
        out_sum = out_sum + jnp.dot(
            attended[:, :HD], w_out_ref[pl.ds(h * HD, HD), :], preferred_element_type=jnp.float32
        )
    out_rows = out_sum.astype(jnp.bfloat16).astype(jnp.float32)
    groups, count, _ = patch_ref.shape
    patch_rows = jnp.concatenate([patch_ref[r].astype(jnp.float32) for r in range(groups)], axis=0)
    mixed_rows = patch_rows + out_rows
    normed_mixed = rms_norm(mixed_rows, gain_ref[...]).astype(jnp.bfloat16)
    copy_up.wait()
    up_rows = jnp.dot(normed_mixed, w_up_ref[...], preferred_element_type=jnp.float32).astype(jnp.bfloat16)
    up_float = up_rows.astype(jnp.float32)
    hidden = (up_float / (1.0 + jnp.exp(-up_float))).astype(jnp.bfloat16)
    copy_down.wait()
    down_rows = jnp.dot(hidden, w_down_ref[...], preferred_element_type=jnp.float32).astype(jnp.bfloat16)
    decoded = mixed_rows + down_rows.astype(jnp.float32)
    for r in range(groups):
        out_ref[r] = decoded[r * count:(r + 1) * count, :].astype(out_ref.dtype)


def tail(state, other, new_packed, patches, w_out, ffn_gain, w_up, w_down):
    vmem = pl.BlockSpec(memory_space=pltpu.VMEM)
    hbm = pl.BlockSpec(memory_space=pl.ANY)
    return pl.pallas_call(
        tail_kernel,
        out_shape=jax.ShapeDtypeStruct(patches.shape, jnp.bfloat16),
        in_specs=[vmem] * 6 + [hbm, hbm],
        out_specs=vmem,
        scratch_shapes=[
            pltpu.VMEM(w_up.shape, w_up.dtype),
            pltpu.VMEM(w_down.shape, w_down.dtype),
            pltpu.SemaphoreType.DMA((2,)),
        ],
    )(state, other, new_packed, patches, w_out, ffn_gain, w_up, w_down)


def layer(
    patches, key_cache, value_cache, cache_len, attn_gain, w_qkv, w_out, ffn_gain, w_up, w_down
):
    seq_count = lax.axis_size("seq")
    kept, sent, query_rows = cache_partials(cache_len, patches, attn_gain, w_qkv, key_cache, value_cache)
    kv_rows = kv_projection(patches, attn_gain, w_qkv)
    new_packed = new_partials(query_rows, kv_rows)
    state, other = combine_over_seq(kept, sent, seq_count)
    return tail(state, other, new_packed, patches, w_out, ffn_gain, w_up, w_down)


def solution(mesh):
    placed = (
        P("req", None, None),
        P("req", "seq", None),
        P("req", "seq", None),
        P("req"),
        P(),
        P(),
        P(),
        P(),
        P(),
        P(),
    )
    return jax.shard_map(layer, mesh=mesh, in_specs=placed, out_specs=P("req", None, None), check_vma=False)
```
